512 devices in a mesh: seq: 32 (over x, y), head: 8 (over z), doc: 2 (over core).
Axes of the slice: x: 4, y: 8, z: 8, core: 2. Of those that a mesh axis runs over, the one named last changes fastest.
Arguments:
- byte_states: bfloat16 [32768, 1024], P(('doc', 'seq')), parts along dimension 0, may hold values from -36 to 36
- conv_kernel: float32 [4, 1024], replicated, may hold values from -3 to 3
- mix_weight: bfloat16 [1024, 1024], replicated, may hold values from -0.1875 to 0.1875
- norm_gain: float32 [1024], replicated, may hold values from 0.1 to 1.9
- query_weight: bfloat16 [1024, 1024], P(None, 'head'), may hold values from -3 to 3
- key_weight: bfloat16 [1024, 1024], P(None, 'head'), may hold values from -3 to 3
- value_weight: bfloat16 [1024, 1024], P(None, 'head'), may hold values from -0.1875 to 0.1875
- boundaries: int32 [4096], P(('doc', 'seq')), parts along dimension 0, may hold values from 0 to 511, as said below
- span_counts: int32 [64], P(('doc', 'seq')), parts along dimension 0, may hold values from 16 to 64, as said below
- grad_attended: bfloat16 [4096, 1024], P(('doc', 'seq'), 'head'), parts along dimension 0, may hold values from -6 to 6
Outputs:
- attended: bfloat16 [4096, 1024], P(('doc', 'seq'), 'head'), parts along dimension 0
- grad_bytes: bfloat16 [32768, 1024], P(('doc', 'seq')), parts along dimension 0
The draws below stay inside these ranges and needn't reach their ends.
There are 2 independent parts, one for each index of `doc`. The reference program is written for one: setup_inputs(seed, part) draws one part's arguments, and reference() takes and returns one part's arrays. A program takes and returns all parts, laid end to end along the dimension named above; an argument that names none is the same for every part. Nothing has to cross between parts.
Inputs may be any that keep to these rules, and one draw needn't show every extreme that they name: `span_counts`: number of spans starting in each shard; in every draw some shard has exactly 64. `boundaries`: in each shard's 64 slots the first span_counts entries are strictly increasing byte positions inside the shard, the first of them 0; the remaining slots hold 0.
All inputs are finite; a program needn't handle non-finite values.
Results may differ from the reference program's by a relative error of at most 0.017.
Values may be sent and summed in bfloat16 or wider, within the bound.
No kernel may reach another device: no remote copies, remote signals or barrier semaphores. Data moves between devices by JAX's collectives and lax.ppermute only.
A program may use at most 64 MiB of HBM per device.

```python
import math
import jax
import jax.numpy as jnp
from jax import lax

D = 1024
HEADS = 8
HD = 128
KCONV = 4
BYTES_DEV = 512
CMAX = 64
WIDTH_E = 1024
SEQ_LEN = 16384
SPANS = 2048
N_SEQ = 32


def draw_byte_states(key, part):
    base_key, row_key, column_key = jax.random.split(key, 3)
    base_draw = jnp.clip(jax.random.normal(base_key, (SEQ_LEN, D), jnp.float32), -4.0, 4.0)
    row_scale = jnp.exp(jax.random.uniform(row_key, (SEQ_LEN, 1), jnp.float32, math.log(0.3), math.log(3.0)))
    column_scale = jnp.exp(jax.random.uniform(column_key, (1, D), jnp.float32, math.log(0.3), math.log(3.0)))
    return (base_draw * row_scale * column_scale).astype(jnp.bfloat16)


def projection_pair(key):
    query_key, other_key = jax.random.split(jax.random.fold_in(key, 11), 2)
    fan_scale = 1.0 / math.sqrt(D)
    query_part = jnp.clip(jax.random.normal(query_key, (D, WIDTH_E), jnp.float32), -4.0, 4.0) * fan_scale
    other_part = jnp.clip(jax.random.normal(other_key, (D, WIDTH_E), jnp.float32), -4.0, 4.0) * fan_scale
    return (query_part, other_part)


def draw_query_weight(key, part):
    return projection_pair(key)[0].astype(jnp.bfloat16)


def draw_key_weight(key, part):
    return projection_pair(key)[1].astype(jnp.bfloat16)


def span_layout(key):
    count_key, full_key, place_key = jax.random.split(jax.random.fold_in(key, 23), 3)
    counts = jax.random.randint(count_key, (N_SEQ,), CMAX // 4, CMAX + 1)
    full_shard = jax.random.randint(full_key, (), 0, N_SEQ)
    counts = jnp.where(jnp.arange(N_SEQ) == full_shard, CMAX, counts)
    shard_keys = jax.random.split(place_key, N_SEQ)
    shuffled = jax.vmap(lambda shard_key: jax.random.permutation(shard_key, BYTES_DEV - 1))(shard_keys) + 1
    picked = shuffled[:, :CMAX - 1]
    keep_slot = jnp.arange(CMAX - 1)[None, :] < counts[:, None] - 1
    picked = jnp.where(keep_slot, picked, BYTES_DEV)
    ordered = jnp.sort(picked, axis=1)
    ordered = jnp.where(ordered >= BYTES_DEV, 0, ordered)
    bounds = jnp.concatenate([jnp.zeros((N_SEQ, 1), jnp.int32), ordered.astype(jnp.int32)], axis=1)
    return (bounds.reshape(SPANS).astype(jnp.int32), counts.astype(jnp.int32))


def draw_boundaries(key, part):
    return span_layout(key)[0]


def draw_span_counts(key, part):
    return span_layout(key)[1]


def block_scale(stream_key, extent, shards, low, largest):
    def one(position, parts):
        heights = jax.random.uniform(jax.random.fold_in(jax.random.fold_in(stream_key, 6), position), (parts,), jnp.float32, low / len(shards), largest / len(shards))
        return jnp.repeat(jnp.exp(heights), extent[position] // parts).reshape((-1,) + (1,) * (len(extent) - position - 1))

    loudness = one(*shards[0])
    for cut in shards[1:]:
        loudness = loudness * one(*cut)
    return loudness


def noise(key, extent, width, reach, pieces=(), kind=jnp.bfloat16):
    loudness = block_scale(key, extent, pieces, -0.22, 0.18) if pieces else 1.0
    result = jax.random.normal(key, extent, jnp.float32) * width * loudness
    return jnp.minimum(jnp.maximum(result, -reach), reach).astype(kind)


def setup_inputs(seed: int = 0, part: int = 0) -> dict:
    splits = jax.random.split(jax.random.key(seed), 11)
    part_splits = jax.random.split(jax.random.fold_in(splits[10], part), 11)
    return {
        "byte_states": draw_byte_states(jax.random.fold_in(jax.random.fold_in(splits[10], part), 71), part),
        "conv_kernel": noise(splits[1], (KCONV, D), 0.5, 3.0, (), jnp.float32),
        "mix_weight": noise(splits[2], (D, D), D ** -0.5, 0.1875),
        "norm_gain": jnp.clip(1.0 + 0.18 * jax.random.normal(splits[3], (D,), jnp.float32), 0.1, 1.9),
        "query_weight": draw_query_weight(jax.random.fold_in(splits[10], 71), part),
        "key_weight": draw_key_weight(jax.random.fold_in(splits[10], 71), part),
        "value_weight": noise(splits[6], (D, WIDTH_E), D ** -0.5, 0.1875, ((1, 8),)),
        "boundaries": draw_boundaries(jax.random.fold_in(jax.random.fold_in(splits[10], part), 71), part),
        "span_counts": draw_span_counts(jax.random.fold_in(jax.random.fold_in(splits[10], part), 71), part),
        "grad_attended": noise(part_splits[9], (SPANS, WIDTH_E), 1.0, 6.0, ((0, 32), (1, 8))),
    }


masked_score = -1e+30

def split_heads(matrix):
    return jnp.transpose(matrix.reshape(SPANS, HEADS, HD), (1, 0, 2))

def join_heads(stacked):
    return jnp.transpose(stacked, (1, 0, 2)).reshape(SPANS, HEADS * HD)

def reference(byte_states, conv_kernel, mix_weight, norm_gain, query_weight, key_weight, value_weight, boundaries, span_counts, grad_attended):
    score_scale = 1.0 / math.sqrt(HD)
    bytes_float = byte_states.astype(jnp.float32)
    padded = jnp.concatenate([jnp.zeros((KCONV - 1, D), jnp.float32), bytes_float], axis=0)
    depthwise = conv_kernel[0] * bytes_float
    for offset in range(1, KCONV):
        depthwise = depthwise + conv_kernel[offset] * padded[KCONV - 1 - offset:KCONV - 1 - offset + SEQ_LEN]
    depthwise = depthwise.astype(jnp.bfloat16)
    slot_ids = jnp.arange(SPANS, dtype=jnp.int32)
    shard_ids = (slot_ids // CMAX).astype(jnp.int32)
    live_mask = slot_ids % CMAX < span_counts[shard_ids]
    row_ids = (shard_ids * BYTES_DEV + boundaries).astype(jnp.int32)
    span_state = bytes_float[row_ids] + jnp.dot(depthwise[row_ids], mix_weight, preferred_element_type=jnp.float32)
    inverse_rms = lax.rsqrt(lax.optimization_barrier(jnp.mean(span_state * span_state, axis=1)) + 1e-05)
    normed = (span_state * inverse_rms[:, None] * norm_gain).astype(jnp.bfloat16)
    queries = jnp.dot(normed, query_weight, preferred_element_type=jnp.float32).astype(jnp.bfloat16)
    key_rows = jnp.dot(normed, key_weight, preferred_element_type=jnp.float32).astype(jnp.bfloat16)
    value_rows = jnp.dot(normed, value_weight, preferred_element_type=jnp.float32).astype(jnp.bfloat16)
    grad_rows = jnp.where(live_mask[:, None], grad_attended, jnp.zeros_like(grad_attended))
    allowed = (slot_ids[None, :] <= slot_ids[:, None]) & live_mask[None, :]

    def one_head(operands):
        query_head, key_head, value_head, grad_head = operands
        scores = jnp.dot(query_head, key_head.T, preferred_element_type=jnp.float32) * score_scale
        scores = jnp.where(allowed, scores, masked_score)
        row_max = lax.optimization_barrier(jnp.max(scores, axis=1))
        softmax_part = jnp.exp(scores - row_max[:, None])
        row_sum = lax.optimization_barrier(jnp.sum(softmax_part, axis=1))
        attention = jnp.dot(softmax_part.astype(jnp.bfloat16), value_head, preferred_element_type=jnp.float32) / row_sum[:, None]
        attention = jnp.where(live_mask[:, None], attention, jnp.float32(0.0)).astype(jnp.bfloat16)
        log_total = row_max + jnp.log(row_sum)
        delta_rows = lax.optimization_barrier(jnp.sum(grad_head.astype(jnp.float32) * attention.astype(jnp.float32), axis=1))
        probs_full = jnp.exp(scores - log_total[:, None])
        grad_value = jnp.dot(probs_full.astype(jnp.bfloat16).T, grad_head, preferred_element_type=jnp.float32)
        grad_probs = jnp.dot(grad_head, value_head.T, preferred_element_type=jnp.float32)
        grad_scores = (probs_full * (grad_probs - delta_rows[:, None])).astype(jnp.bfloat16)
        grad_query = jnp.dot(grad_scores, key_head, preferred_element_type=jnp.float32) * score_scale
        grad_key = jnp.dot(grad_scores.T, query_head, preferred_element_type=jnp.float32) * score_scale
        return (attention, grad_query.astype(jnp.bfloat16), grad_key.astype(jnp.bfloat16), grad_value.astype(jnp.bfloat16))
    outputs = lax.map(one_head, (split_heads(queries), split_heads(key_rows), split_heads(value_rows), split_heads(grad_rows)))
    attended = join_heads(outputs[0])
    contract = (((1,), (1,)), ((), ()))
    grad_normed = lax.dot_general(join_heads(outputs[1]), query_weight, contract, preferred_element_type=jnp.float32)
    grad_normed = grad_normed + lax.dot_general(join_heads(outputs[2]), key_weight, contract, preferred_element_type=jnp.float32)
    grad_normed = grad_normed + lax.dot_general(join_heads(outputs[3]), value_weight, contract, preferred_element_type=jnp.float32)
    scaled_grad = norm_gain * grad_normed
    cubed = inverse_rms * inverse_rms * inverse_rms
    grad_state = inverse_rms[:, None] * scaled_grad - span_state * cubed[:, None] * lax.optimization_barrier(jnp.mean(scaled_grad * span_state, axis=1))[:, None]
    grad_state = jnp.where(live_mask[:, None], grad_state, jnp.float32(0.0))
    mixed_grad = lax.dot_general(grad_state.astype(jnp.bfloat16), mix_weight, contract, preferred_element_type=jnp.float32)
    spread_mix = jnp.zeros((SEQ_LEN, D), jnp.float32).at[row_ids].add(mixed_grad)
    residual_grad = jnp.zeros((SEQ_LEN, D), jnp.float32).at[row_ids].add(grad_state)
    padded_grad = jnp.concatenate([spread_mix, jnp.zeros((KCONV - 1, D), jnp.float32)], axis=0)
    conv_grad = conv_kernel[0] * spread_mix
    for offset in range(1, KCONV):
        conv_grad = conv_grad + conv_kernel[offset] * padded_grad[offset:offset + SEQ_LEN]
    grad_bytes = (residual_grad + conv_grad).astype(jnp.bfloat16)
    return (attended, grad_bytes)
```

```python
import math

import jax
import jax.numpy as jnp
from jax import lax
from jax.sharding import PartitionSpec as P

D = 1024
HD = 128
KCONV = 4
CHUNK = 256


masked_score = -1e30


def passed_along(array, axis, by):
    devices = lax.axis_size(axis)
    pairs = [(i, i + by) for i in range(devices) if 0 <= i + by < devices]
    return lax.ppermute(array, axis, pairs)


def neighbour(rim_rows, offset_by):
    return passed_along(rim_rows, "seq", offset_by)


def gather_blocks(block, axis):
    devices = lax.axis_size(axis)
    me = lax.axis_index(axis)
    held = block[None]
    step = 1
    while step < devices:
        other = lax.ppermute(held, axis, [(i, i ^ step) for i in range(devices)])
        held = jnp.concatenate([held, other], axis=0)
        step *= 2
    order = jnp.arange(devices, dtype=jnp.int32) ^ me
    return jnp.take(held, order, axis=0)


def summed_over(partial, axis):
    devices = lax.axis_size(axis)
    sent = partial.astype(jnp.bfloat16)
    total = sent.astype(jnp.float32)
    for shift in range(1, devices):
        total = total + lax.ppermute(
            sent, axis, [(i, (i + shift) % devices) for i in range(devices)]
        ).astype(jnp.float32)
    return total


def per_device(
    byte_states,
    conv_kernel,
    mix_weight,
    norm_gain,
    query_weight,
    key_weight,
    value_weight,
    boundaries,
    span_counts,
    grad_attended,
):
    row_count = byte_states.shape[0]
    slot_count = boundaries.shape[0]
    head_width = query_weight.shape[1]
    score_scale = 1.0 / math.sqrt(HD)
    shard_index = lax.axis_index("seq")
    shards = lax.axis_size("seq")
    first_slot = shard_index * slot_count
    own_ids = first_slot + jnp.arange(slot_count, dtype=jnp.int32)
    before_rim = neighbour(byte_states[row_count - (KCONV - 1) :].astype(jnp.float32), 1)
    extended = jnp.concatenate([before_rim.astype(jnp.bfloat16), byte_states], axis=0)
    span_depth = conv_kernel[0] * jnp.take(extended, boundaries + (KCONV - 1), axis=0).astype(
        jnp.float32
    )
    for offset in range(1, KCONV):
        tapped = jnp.take(extended, boundaries + (KCONV - 1 - offset), axis=0).astype(jnp.float32)
        span_depth = span_depth + conv_kernel[offset] * tapped
    span_depth = span_depth.astype(jnp.bfloat16)
    span_bytes = jnp.take(byte_states, boundaries, axis=0).astype(jnp.float32)
    live_mask = jnp.arange(slot_count, dtype=jnp.int32) < span_counts[0]
    span_state = span_bytes + jnp.dot(span_depth, mix_weight, preferred_element_type=jnp.float32)
    inverse_rms = lax.rsqrt(jnp.mean(span_state * span_state, axis=1) + 1e-05)
    normed = (span_state * inverse_rms[:, None] * norm_gain).astype(jnp.bfloat16)
    queries = jnp.dot(normed, query_weight, preferred_element_type=jnp.float32).astype(jnp.bfloat16)
    key_rows = jnp.dot(normed, key_weight, preferred_element_type=jnp.float32).astype(jnp.bfloat16)
    value_rows = jnp.dot(normed, value_weight, preferred_element_type=jnp.float32).astype(
        jnp.bfloat16
    )
    grad_rows = jnp.where(live_mask[:, None], grad_attended, jnp.zeros_like(grad_attended))

    count_rows = jnp.broadcast_to(span_counts[0].astype(jnp.bfloat16), (16, head_width))
    packed = jnp.concatenate([queries, key_rows, value_rows, grad_rows, count_rows], axis=0)
    gathered = gather_blocks(packed, "seq")
    total_slots = shards * slot_count

    def piece(k):
        return gathered[:, k * slot_count : (k + 1) * slot_count].reshape(total_slots, head_width)

    all_queries, all_keys, all_values, all_grads = piece(0), piece(1), piece(2), piece(3)
    all_counts = gathered[:, 4 * slot_count, 0].astype(jnp.int32)
    all_live = (
        jnp.arange(slot_count, dtype=jnp.int32)[None, :] < all_counts[:, None]
    ).reshape(total_slots)
    slot_ids = jnp.arange(total_slots, dtype=jnp.int32)

    log_parts = []
    delta_parts = []
    attended_parts = []
    for chunk in range(total_slots // CHUNK):
        q0, q1 = chunk * CHUNK, (chunk + 1) * CHUNK
        q_ids = slot_ids[q0:q1]
        k_ids = slot_ids[:q1]
        allowed = (k_ids[None, :] <= q_ids[:, None]) & all_live[None, :q1]
        scores = (
            jnp.dot(all_queries[q0:q1], all_keys[:q1].T, preferred_element_type=jnp.float32)
            * score_scale
        )
        scores = jnp.where(allowed, scores, masked_score)
        row_max = jnp.max(scores, axis=1)
        softmax_part = jnp.exp(scores - row_max[:, None])
        row_sum = jnp.sum(softmax_part, axis=1)
        product = jnp.dot(
            softmax_part.astype(jnp.bfloat16), all_values[:q1], preferred_element_type=jnp.float32
        )
        attention = jnp.where(
            all_live[q0:q1, None], product / row_sum[:, None], jnp.float32(0.0)
        ).astype(jnp.bfloat16)
        log_parts.append(row_max + jnp.log(row_sum))
        delta_parts.append(
            jnp.sum(all_grads[q0:q1].astype(jnp.float32) * attention.astype(jnp.float32), axis=1)
        )
        attended_parts.append(attention)
    all_logs = jnp.concatenate(log_parts)
    all_deltas = jnp.concatenate(delta_parts)
    all_attended = jnp.concatenate(attended_parts, axis=0)
    attended = lax.dynamic_slice_in_dim(all_attended, first_slot, slot_count, axis=0)
    own_logs = lax.dynamic_slice_in_dim(all_logs, first_slot, slot_count)
    own_deltas = lax.dynamic_slice_in_dim(all_deltas, first_slot, slot_count)

    allowed = (slot_ids[None, :] <= own_ids[:, None]) & all_live[None, :]
    scores = jnp.dot(queries, all_keys.T, preferred_element_type=jnp.float32) * score_scale
    scores = jnp.where(allowed, scores, masked_score)
    probs_full = jnp.exp(scores - own_logs[:, None])
    grad_probs = jnp.dot(grad_rows, all_values.T, preferred_element_type=jnp.float32)
    grad_scores = (probs_full * (grad_probs - own_deltas[:, None])).astype(jnp.bfloat16)
    query_grad_rows = (
        jnp.dot(grad_scores, all_keys, preferred_element_type=jnp.float32) * score_scale
    ).astype(jnp.bfloat16)

    allowed = (own_ids[None, :] <= slot_ids[:, None]) & live_mask[None, :]
    scores = jnp.dot(all_queries, key_rows.T, preferred_element_type=jnp.float32) * score_scale
    scores = jnp.where(allowed, scores, masked_score)
    probs_full = jnp.exp(scores - all_logs[:, None])
    contract_rows = (((0,), (0,)), ((), ()))
    value_grad_rows = lax.dot_general(
        probs_full.astype(jnp.bfloat16), all_grads, contract_rows, preferred_element_type=jnp.float32
    ).astype(jnp.bfloat16)
    grad_probs = jnp.dot(all_grads, value_rows.T, preferred_element_type=jnp.float32)
    grad_scores = (probs_full * (grad_probs - all_deltas[:, None])).astype(jnp.bfloat16)
    key_grad_rows = (
        lax.dot_general(grad_scores, all_queries, contract_rows, preferred_element_type=jnp.float32)
        * score_scale
    ).astype(jnp.bfloat16)

    contract = (((1,), (1,)), ((), ()))
    partial_normed = lax.dot_general(
        query_grad_rows, query_weight, contract, preferred_element_type=jnp.float32
    )
    partial_normed = partial_normed + lax.dot_general(
        key_grad_rows, key_weight, contract, preferred_element_type=jnp.float32
    )
    partial_normed = partial_normed + lax.dot_general(
        value_grad_rows, value_weight, contract, preferred_element_type=jnp.float32
    )
    grad_normed = summed_over(partial_normed, "head")
    scaled_grad = norm_gain * grad_normed
    cubed = inverse_rms * inverse_rms * inverse_rms
    grad_state = (
        inverse_rms[:, None] * scaled_grad
        - span_state * cubed[:, None] * jnp.mean(scaled_grad * span_state, axis=1)[:, None]
    )
    grad_state = jnp.where(live_mask[:, None], grad_state, jnp.float32(0.0))
    mixed_grad = lax.dot_general(
        grad_state.astype(jnp.bfloat16), mix_weight, contract, preferred_element_type=jnp.float32
    )
    spread_mix = jnp.zeros((row_count, D), jnp.float32).at[boundaries].add(mixed_grad)
    residual_grad = jnp.zeros((row_count, D), jnp.float32).at[boundaries].add(grad_state)
    after_rim = neighbour(spread_mix[: KCONV - 1], -1)
    padded_grad = jnp.concatenate([spread_mix, after_rim], axis=0)
    conv_grad = conv_kernel[0] * spread_mix
    for offset in range(1, KCONV):
        conv_grad = conv_grad + conv_kernel[offset] * padded_grad[offset : offset + row_count]
    grad_bytes = (residual_grad + conv_grad).astype(jnp.bfloat16)
    return (attended, grad_bytes)


def solution(mesh):
    return jax.shard_map(
        per_device,
        mesh=mesh,
        in_specs=(
            P(("doc", "seq"), None),
            P(),
            P(),
            P(),
            P(None, "head"),
            P(None, "head"),
            P(None, "head"),
            P(("doc", "seq")),
            P(("doc", "seq")),
            P(("doc", "seq"), "head"),
        ),
        out_specs=(P(("doc", "seq"), "head"), P(("doc", "seq"), None)),
        check_vma=False,
    )
```

```python
import math

import jax
import jax.numpy as jnp
from jax import lax
from jax.sharding import PartitionSpec as P

D = 1024
HD = 128
KCONV = 4
CHUNK = 256


masked_score = -1e30


def passed_along(array, axis, by):
    devices = lax.axis_size(axis)
    pairs = [(i, i + by) for i in range(devices) if 0 <= i + by < devices]
    return lax.ppermute(array, axis, pairs)


def neighbour(rim_rows, offset_by):
    return passed_along(rim_rows, "seq", offset_by)


def gather_blocks(block, axis):
    devices = lax.axis_size(axis)
    me = lax.axis_index(axis)
    steps = [4, 16, 2, 1, 8] if devices == 32 else [1 << b for b in range(devices.bit_length() - 1)]
    held = block[None]
    for step in steps:
        other = lax.ppermute(held, axis, [(i, i ^ step) for i in range(devices)])
        held = jnp.concatenate([held, other], axis=0)
    offset = [0]
    for step in steps:
        offset = offset + [o ^ step for o in offset]
    position = [0] * devices
    for j, o in enumerate(offset):
        position[o] = j
    order = jnp.asarray(position, dtype=jnp.int32)[jnp.arange(devices, dtype=jnp.int32) ^ me]
    return jnp.take(held, order, axis=0)


def summed_over(partial, axis):
    devices = lax.axis_size(axis)
    sent = partial.astype(jnp.bfloat16)
    total = sent.astype(jnp.float32)
    for shift in range(1, devices):
        total = total + lax.ppermute(
            sent, axis, [(i, (i + shift) % devices) for i in range(devices)]
        ).astype(jnp.float32)
    return total


def per_device(
    byte_states,
    conv_kernel,
    mix_weight,
    norm_gain,
    query_weight,
    key_weight,
    value_weight,
    boundaries,
    span_counts,
    grad_attended,
):
    row_count = byte_states.shape[0]
    slot_count = boundaries.shape[0]
    head_width = query_weight.shape[1]
    score_scale = 1.0 / math.sqrt(HD)
    shard_index = lax.axis_index("seq")
    shards = lax.axis_size("seq")
    first_slot = shard_index * slot_count
    own_ids = first_slot + jnp.arange(slot_count, dtype=jnp.int32)
    before_rim = neighbour(byte_states[row_count - (KCONV - 1) :].astype(jnp.float32), 1)
    extended = jnp.concatenate([before_rim.astype(jnp.bfloat16), byte_states], axis=0)
    span_depth = conv_kernel[0] * jnp.take(extended, boundaries + (KCONV - 1), axis=0).astype(
        jnp.float32
    )
    for offset in range(1, KCONV):
        tapped = jnp.take(extended, boundaries + (KCONV - 1 - offset), axis=0).astype(jnp.float32)
        span_depth = span_depth + conv_kernel[offset] * tapped
    span_depth = span_depth.astype(jnp.bfloat16)
    span_bytes = jnp.take(byte_states, boundaries, axis=0).astype(jnp.float32)
    live_mask = jnp.arange(slot_count, dtype=jnp.int32) < span_counts[0]
    span_state = span_bytes + jnp.dot(span_depth, mix_weight, preferred_element_type=jnp.float32)
    inverse_rms = lax.rsqrt(jnp.mean(span_state * span_state, axis=1) + 1e-05)
    normed = (span_state * inverse_rms[:, None] * norm_gain).astype(jnp.bfloat16)
    queries = jnp.dot(normed, query_weight, preferred_element_type=jnp.float32).astype(jnp.bfloat16)
    key_rows = jnp.dot(normed, key_weight, preferred_element_type=jnp.float32).astype(jnp.bfloat16)
    value_rows = jnp.dot(normed, value_weight, preferred_element_type=jnp.float32).astype(
        jnp.bfloat16
    )
    grad_rows = jnp.where(live_mask[:, None], grad_attended, jnp.zeros_like(grad_attended))

    count_rows = jnp.broadcast_to(span_counts[0].astype(jnp.bfloat16), (16, head_width))
    packed = jnp.concatenate([queries, key_rows, value_rows, grad_rows, count_rows], axis=0)
    gathered = gather_blocks(packed, "seq")
    total_slots = shards * slot_count

    def piece(k):
        return gathered[:, k * slot_count : (k + 1) * slot_count].reshape(total_slots, head_width)

    all_queries, all_keys, all_values, all_grads = piece(0), piece(1), piece(2), piece(3)
    all_counts = gathered[:, 4 * slot_count, 0].astype(jnp.int32)
    all_live = (
        jnp.arange(slot_count, dtype=jnp.int32)[None, :] < all_counts[:, None]
    ).reshape(total_slots)
    slot_ids = jnp.arange(total_slots, dtype=jnp.int32)

    log_parts = []
    delta_parts = []
    attended_parts = []
    for chunk in range(total_slots // CHUNK):
        q0, q1 = chunk * CHUNK, (chunk + 1) * CHUNK
        q_ids = slot_ids[q0:q1]
        k_ids = slot_ids[:q1]
        allowed = (k_ids[None, :] <= q_ids[:, None]) & all_live[None, :q1]
        scores = (
            jnp.dot(all_queries[q0:q1], all_keys[:q1].T, preferred_element_type=jnp.float32)
            * score_scale
        )
        scores = jnp.where(allowed, scores, masked_score)
        row_max = jnp.max(scores, axis=1)
        softmax_part = jnp.exp(scores - row_max[:, None])
        row_sum = jnp.sum(softmax_part, axis=1)
        product = jnp.dot(
            softmax_part.astype(jnp.bfloat16), all_values[:q1], preferred_element_type=jnp.float32
        )
        attention = jnp.where(
            all_live[q0:q1, None], product / row_sum[:, None], jnp.float32(0.0)
        ).astype(jnp.bfloat16)
        log_parts.append(row_max + jnp.log(row_sum))
        delta_parts.append(
            jnp.sum(all_grads[q0:q1].astype(jnp.float32) * attention.astype(jnp.float32), axis=1)
        )
        attended_parts.append(attention)
    all_logs = jnp.concatenate(log_parts)
    all_deltas = jnp.concatenate(delta_parts)
    all_attended = jnp.concatenate(attended_parts, axis=0)
    attended = lax.dynamic_slice_in_dim(all_attended, first_slot, slot_count, axis=0)
    own_logs = lax.dynamic_slice_in_dim(all_logs, first_slot, slot_count)
    own_deltas = lax.dynamic_slice_in_dim(all_deltas, first_slot, slot_count)

    allowed = (slot_ids[None, :] <= own_ids[:, None]) & all_live[None, :]
    scores = jnp.dot(queries, all_keys.T, preferred_element_type=jnp.float32) * score_scale
    scores = jnp.where(allowed, scores, masked_score)
    probs_full = jnp.exp(scores - own_logs[:, None])
    grad_probs = jnp.dot(grad_rows, all_values.T, preferred_element_type=jnp.float32)
    grad_scores = (probs_full * (grad_probs - own_deltas[:, None])).astype(jnp.bfloat16)
    query_grad_rows = (
        jnp.dot(grad_scores, all_keys, preferred_element_type=jnp.float32) * score_scale
    ).astype(jnp.bfloat16)

    allowed = (own_ids[None, :] <= slot_ids[:, None]) & live_mask[None, :]
    scores = jnp.dot(all_queries, key_rows.T, preferred_element_type=jnp.float32) * score_scale
    scores = jnp.where(allowed, scores, masked_score)
    probs_full = jnp.exp(scores - all_logs[:, None])
    contract_rows = (((0,), (0,)), ((), ()))
    value_grad_rows = lax.dot_general(
        probs_full.astype(jnp.bfloat16), all_grads, contract_rows, preferred_element_type=jnp.float32
    ).astype(jnp.bfloat16)
    grad_probs = jnp.dot(all_grads, value_rows.T, preferred_element_type=jnp.float32)
    grad_scores = (probs_full * (grad_probs - all_deltas[:, None])).astype(jnp.bfloat16)
    key_grad_rows = (
        lax.dot_general(grad_scores, all_queries, contract_rows, preferred_element_type=jnp.float32)
        * score_scale
    ).astype(jnp.bfloat16)

    contract = (((1,), (1,)), ((), ()))
    partial_normed = lax.dot_general(
        query_grad_rows, query_weight, contract, preferred_element_type=jnp.float32
    )
    partial_normed = partial_normed + lax.dot_general(
        key_grad_rows, key_weight, contract, preferred_element_type=jnp.float32
    )
    partial_normed = partial_normed + lax.dot_general(
        value_grad_rows, value_weight, contract, preferred_element_type=jnp.float32
    )
    grad_normed = summed_over(partial_normed, "head")
    scaled_grad = norm_gain * grad_normed
    cubed = inverse_rms * inverse_rms * inverse_rms
    grad_state = (
        inverse_rms[:, None] * scaled_grad
        - span_state * cubed[:, None] * jnp.mean(scaled_grad * span_state, axis=1)[:, None]
    )
    grad_state = jnp.where(live_mask[:, None], grad_state, jnp.float32(0.0))
    mixed_grad = lax.dot_general(
        grad_state.astype(jnp.bfloat16), mix_weight, contract, preferred_element_type=jnp.float32
    )
    spread_mix = jnp.zeros((row_count, D), jnp.float32).at[boundaries].add(mixed_grad)
    residual_grad = jnp.zeros((row_count, D), jnp.float32).at[boundaries].add(grad_state)
    after_rim = neighbour(spread_mix[: KCONV - 1], -1)
    padded_grad = jnp.concatenate([spread_mix, after_rim], axis=0)
    conv_grad = conv_kernel[0] * spread_mix
    for offset in range(1, KCONV):
        conv_grad = conv_grad + conv_kernel[offset] * padded_grad[offset : offset + row_count]
    grad_bytes = (residual_grad + conv_grad).astype(jnp.bfloat16)
    return (attended, grad_bytes)


def solution(mesh):
    return jax.shard_map(
        per_device,
        mesh=mesh,
        in_specs=(
            P(("doc", "seq"), None),
            P(),
            P(),
            P(),
            P(None, "head"),
            P(None, "head"),
            P(None, "head"),
            P(("doc", "seq")),
            P(("doc", "seq")),
            P(("doc", "seq"), "head"),
        ),
        out_specs=(P(("doc", "seq"), "head"), P(("doc", "seq"), None)),
        check_vma=False,
    )
```

```python
import math

import jax
import jax.numpy as jnp
from jax import lax
from jax.experimental import pallas as pl
from jax.sharding import PartitionSpec as P

D = 1024
HD = 128
KCONV = 4
QBLOCK = 256


masked_score = -1e30


def passed_along(array, axis, by):
    devices = lax.axis_size(axis)
    pairs = [(i, i + by) for i in range(devices) if 0 <= i + by < devices]
    return lax.ppermute(array, axis, pairs)


def neighbour(rim_rows, offset_by):
    return passed_along(rim_rows, "seq", offset_by)


def gather_blocks(block, axis):
    devices = lax.axis_size(axis)
    me = lax.axis_index(axis)
    held = block[None]
    step = 1
    while step < devices:
        other = lax.ppermute(held, axis, [(i, i ^ step) for i in range(devices)])
        held = jnp.concatenate([held, other], axis=0)
        step *= 2
    order = jnp.arange(devices, dtype=jnp.int32) ^ me
    return jnp.take(held, order, axis=0)


def summed_over(partial, axis):
    devices = lax.axis_size(axis)
    sent = partial.astype(jnp.bfloat16)
    total = sent.astype(jnp.float32)
    for shift in range(1, devices):
        total = total + lax.ppermute(
            sent, axis, [(i, (i + shift) % devices) for i in range(devices)]
        ).astype(jnp.float32)
    return total


def forward_kernel(q_ref, k_ref, v_ref, g_ref, live_row_ref, live_col_ref, att_ref, log_ref, delta_ref):
    block = pl.program_id(0)
    rows = q_ref.shape[0]
    keys = k_ref.shape[0]
    scale = 1.0 / math.sqrt(HD)
    scores = lax.dot_general(
        q_ref[...], k_ref[...], (((1,), (1,)), ((), ())), preferred_element_type=jnp.float32
    ) * scale
    q_ids = block * rows + lax.broadcasted_iota(jnp.int32, (rows, keys), 0)
    k_ids = lax.broadcasted_iota(jnp.int32, (rows, keys), 1)
    allowed = (k_ids <= q_ids) & (live_row_ref[...] > 0.5)
    scores = jnp.where(allowed, scores, masked_score)
    row_max = jnp.max(scores, axis=1, keepdims=True)
    softmax_part = jnp.exp(scores - row_max)
    row_sum = jnp.sum(softmax_part, axis=1, keepdims=True)
    product = jnp.dot(
        softmax_part.astype(jnp.bfloat16), v_ref[...], preferred_element_type=jnp.float32
    )
    attention = jnp.where(live_col_ref[...] > 0.5, product / row_sum, 0.0).astype(jnp.bfloat16)
    att_ref[...] = attention
    log_ref[...] = row_max + jnp.log(row_sum)
    delta_ref[...] = jnp.sum(
        g_ref[...].astype(jnp.float32) * attention.astype(jnp.float32), axis=1, keepdims=True
    )


def forward_all(queries, keys, values, grads, live):
    slots, width = queries.shape
    live_f = live.astype(jnp.float32)
    row_spec = pl.BlockSpec((QBLOCK, width), lambda i: (i, 0))
    full_spec = pl.BlockSpec((slots, width), lambda i: (0, 0))
    col_spec = pl.BlockSpec((QBLOCK, 1), lambda i: (i, 0))
    return pl.pallas_call(
        forward_kernel,
        grid=(slots // QBLOCK,),
        in_specs=[row_spec, full_spec, full_spec, row_spec,
                  pl.BlockSpec((1, slots), lambda i: (0, 0)), col_spec],
        out_specs=[row_spec, col_spec, col_spec],
        out_shape=[
            jax.ShapeDtypeStruct((slots, width), jnp.bfloat16),
            jax.ShapeDtypeStruct((slots, 1), jnp.float32),
            jax.ShapeDtypeStruct((slots, 1), jnp.float32),
        ],
    )(queries, keys, values, grads, live_f.reshape(1, slots), live_f.reshape(slots, 1))


def per_device(
    byte_states,
    conv_kernel,
    mix_weight,
    norm_gain,
    query_weight,
    key_weight,
    value_weight,
    boundaries,
    span_counts,
    grad_attended,
):
    row_count = byte_states.shape[0]
    slot_count = boundaries.shape[0]
    head_width = query_weight.shape[1]
    score_scale = 1.0 / math.sqrt(HD)
    shard_index = lax.axis_index("seq")
    shards = lax.axis_size("seq")
    first_slot = shard_index * slot_count
    own_ids = first_slot + jnp.arange(slot_count, dtype=jnp.int32)
    before_rim = neighbour(byte_states[row_count - (KCONV - 1) :].astype(jnp.float32), 1)
    extended = jnp.concatenate([before_rim.astype(jnp.bfloat16), byte_states], axis=0)
    span_depth = conv_kernel[0] * jnp.take(extended, boundaries + (KCONV - 1), axis=0).astype(
        jnp.float32
    )
    for offset in range(1, KCONV):
        tapped = jnp.take(extended, boundaries + (KCONV - 1 - offset), axis=0).astype(jnp.float32)
        span_depth = span_depth + conv_kernel[offset] * tapped
    span_depth = span_depth.astype(jnp.bfloat16)
    span_bytes = jnp.take(byte_states, boundaries, axis=0).astype(jnp.float32)
    live_mask = jnp.arange(slot_count, dtype=jnp.int32) < span_counts[0]
    span_state = span_bytes + jnp.dot(span_depth, mix_weight, preferred_element_type=jnp.float32)
    inverse_rms = lax.rsqrt(jnp.mean(span_state * span_state, axis=1) + 1e-05)
    normed = (span_state * inverse_rms[:, None] * norm_gain).astype(jnp.bfloat16)
    queries = jnp.dot(normed, query_weight, preferred_element_type=jnp.float32).astype(jnp.bfloat16)
    key_rows = jnp.dot(normed, key_weight, preferred_element_type=jnp.float32).astype(jnp.bfloat16)
    value_rows = jnp.dot(normed, value_weight, preferred_element_type=jnp.float32).astype(
        jnp.bfloat16
    )
    grad_rows = jnp.where(live_mask[:, None], grad_attended, jnp.zeros_like(grad_attended))

    count_rows = jnp.broadcast_to(span_counts[0].astype(jnp.bfloat16), (16, head_width))
    packed = jnp.concatenate([queries, key_rows, value_rows, grad_rows, count_rows], axis=0)
    gathered = gather_blocks(packed, "seq")
    total_slots = shards * slot_count

    def piece(k):
        return gathered[:, k * slot_count : (k + 1) * slot_count].reshape(total_slots, head_width)

    all_queries, all_keys, all_values, all_grads = piece(0), piece(1), piece(2), piece(3)
    all_counts = gathered[:, 4 * slot_count, 0].astype(jnp.int32)
    all_live = (
        jnp.arange(slot_count, dtype=jnp.int32)[None, :] < all_counts[:, None]
    ).reshape(total_slots)
    slot_ids = jnp.arange(total_slots, dtype=jnp.int32)

    all_attended, all_logs, all_deltas = forward_all(
        all_queries, all_keys, all_values, all_grads, all_live
    )
    all_logs = all_logs.reshape(total_slots)
    all_deltas = all_deltas.reshape(total_slots)
    attended = lax.dynamic_slice_in_dim(all_attended, first_slot, slot_count, axis=0)
    own_logs = lax.dynamic_slice_in_dim(all_logs, first_slot, slot_count)
    own_deltas = lax.dynamic_slice_in_dim(all_deltas, first_slot, slot_count)

    allowed = (slot_ids[None, :] <= own_ids[:, None]) & all_live[None, :]
    scores = jnp.dot(queries, all_keys.T, preferred_element_type=jnp.float32) * score_scale
    scores = jnp.where(allowed, scores, masked_score)
    probs_full = jnp.exp(scores - own_logs[:, None])
    grad_probs = jnp.dot(grad_rows, all_values.T, preferred_element_type=jnp.float32)
    grad_scores = (probs_full * (grad_probs - own_deltas[:, None])).astype(jnp.bfloat16)
    query_grad_rows = (
        jnp.dot(grad_scores, all_keys, preferred_element_type=jnp.float32) * score_scale
    ).astype(jnp.bfloat16)

    allowed = (own_ids[None, :] <= slot_ids[:, None]) & live_mask[None, :]
    scores = jnp.dot(all_queries, key_rows.T, preferred_element_type=jnp.float32) * score_scale
    scores = jnp.where(allowed, scores, masked_score)
    probs_full = jnp.exp(scores - all_logs[:, None])
    contract_rows = (((0,), (0,)), ((), ()))
    value_grad_rows = lax.dot_general(
        probs_full.astype(jnp.bfloat16), all_grads, contract_rows, preferred_element_type=jnp.float32
    ).astype(jnp.bfloat16)
    grad_probs = jnp.dot(all_grads, value_rows.T, preferred_element_type=jnp.float32)
    grad_scores = (probs_full * (grad_probs - all_deltas[:, None])).astype(jnp.bfloat16)
    key_grad_rows = (
        lax.dot_general(grad_scores, all_queries, contract_rows, preferred_element_type=jnp.float32)
        * score_scale
    ).astype(jnp.bfloat16)

    contract = (((1,), (1,)), ((), ()))
    partial_normed = lax.dot_general(
        query_grad_rows, query_weight, contract, preferred_element_type=jnp.float32
    )
    partial_normed = partial_normed + lax.dot_general(
        key_grad_rows, key_weight, contract, preferred_element_type=jnp.float32
    )
    partial_normed = partial_normed + lax.dot_general(
        value_grad_rows, value_weight, contract, preferred_element_type=jnp.float32
    )
    grad_normed = summed_over(partial_normed, "head")
    scaled_grad = norm_gain * grad_normed
    cubed = inverse_rms * inverse_rms * inverse_rms
    grad_state = (
        inverse_rms[:, None] * scaled_grad
        - span_state * cubed[:, None] * jnp.mean(scaled_grad * span_state, axis=1)[:, None]
    )
    grad_state = jnp.where(live_mask[:, None], grad_state, jnp.float32(0.0))
    mixed_grad = lax.dot_general(
        grad_state.astype(jnp.bfloat16), mix_weight, contract, preferred_element_type=jnp.float32
    )
    spread_mix = jnp.zeros((row_count, D), jnp.float32).at[boundaries].add(mixed_grad)
    residual_grad = jnp.zeros((row_count, D), jnp.float32).at[boundaries].add(grad_state)
    after_rim = neighbour(spread_mix[: KCONV - 1], -1)
    padded_grad = jnp.concatenate([spread_mix, after_rim], axis=0)
    conv_grad = conv_kernel[0] * spread_mix
    for offset in range(1, KCONV):
        conv_grad = conv_grad + conv_kernel[offset] * padded_grad[offset : offset + row_count]
    grad_bytes = (residual_grad + conv_grad).astype(jnp.bfloat16)
    return (attended, grad_bytes)


def solution(mesh):
    return jax.shard_map(
        per_device,
        mesh=mesh,
        in_specs=(
            P(("doc", "seq"), None),
            P(),
            P(),
            P(),
            P(None, "head"),
            P(None, "head"),
            P(None, "head"),
            P(("doc", "seq")),
            P(("doc", "seq")),
            P(("doc", "seq"), "head"),
        ),
        out_specs=(P(("doc", "seq"), "head"), P(("doc", "seq"), None)),
        check_vma=False,
    )
```

```python
import math

import jax
import jax.numpy as jnp
from jax import lax
from jax.experimental import pallas as pl
from jax.sharding import PartitionSpec as P

D = 1024
HD = 128
KCONV = 4
QBLOCK = 256


masked_score = -1e30


def passed_along(array, axis, by):
    devices = lax.axis_size(axis)
    pairs = [(i, i + by) for i in range(devices) if 0 <= i + by < devices]
    return lax.ppermute(array, axis, pairs)


def neighbour(rim_rows, offset_by):
    return passed_along(rim_rows, "seq", offset_by)


def gather_blocks(block, axis):
    devices = lax.axis_size(axis)
    me = lax.axis_index(axis)
    held = block[None]
    step = 1
    while step < devices:
        other = lax.ppermute(held, axis, [(i, i ^ step) for i in range(devices)])
        held = jnp.concatenate([held, other], axis=0)
        step *= 2
    order = jnp.arange(devices, dtype=jnp.int32) ^ me
    return jnp.take(held, order, axis=0)


def summed_over(partial, axis):
    devices = lax.axis_size(axis)
    total = partial
    step = 1
    while step < devices:
        sent = total.astype(jnp.bfloat16)
        got = lax.ppermute(sent, axis, [(i, i ^ step) for i in range(devices)])
        total = sent.astype(jnp.float32) + got.astype(jnp.float32)
        step *= 2
    return total


def forward_kernel(q_ref, k_ref, v_ref, g_ref, live_row_ref, live_col_ref, att_ref, log_ref, delta_ref):
    block = pl.program_id(0)
    rows = q_ref.shape[0]
    keys = k_ref.shape[0]
    scale = 1.0 / math.sqrt(HD)
    scores = lax.dot_general(
        q_ref[...], k_ref[...], (((1,), (1,)), ((), ())), preferred_element_type=jnp.float32
    ) * scale
    q_ids = block * rows + lax.broadcasted_iota(jnp.int32, (rows, keys), 0)
    k_ids = lax.broadcasted_iota(jnp.int32, (rows, keys), 1)
    allowed = (k_ids <= q_ids) & (live_row_ref[...] > 0.5)
    scores = jnp.where(allowed, scores, masked_score)
    row_max = jnp.max(scores, axis=1, keepdims=True)
    softmax_part = jnp.exp(scores - row_max)
    row_sum = jnp.sum(softmax_part, axis=1, keepdims=True)
    product = jnp.dot(
        softmax_part.astype(jnp.bfloat16), v_ref[...], preferred_element_type=jnp.float32
    )
    attention = jnp.where(live_col_ref[...] > 0.5, product / row_sum, 0.0).astype(jnp.bfloat16)
    att_ref[...] = attention
    log_ref[...] = row_max + jnp.log(row_sum)
    delta_ref[...] = jnp.sum(
        g_ref[...].astype(jnp.float32) * attention.astype(jnp.float32), axis=1, keepdims=True
    )


def forward_all(queries, keys, values, grads, live):
    slots, width = queries.shape
    live_f = live.astype(jnp.float32)
    row_spec = pl.BlockSpec((QBLOCK, width), lambda i: (i, 0))
    full_spec = pl.BlockSpec((slots, width), lambda i: (0, 0))
    col_spec = pl.BlockSpec((QBLOCK, 1), lambda i: (i, 0))
    return pl.pallas_call(
        forward_kernel,
        grid=(slots // QBLOCK,),
        in_specs=[row_spec, full_spec, full_spec, row_spec,
                  pl.BlockSpec((1, slots), lambda i: (0, 0)), col_spec],
        out_specs=[row_spec, col_spec, col_spec],
        out_shape=[
            jax.ShapeDtypeStruct((slots, width), jnp.bfloat16),
            jax.ShapeDtypeStruct((slots, 1), jnp.float32),
            jax.ShapeDtypeStruct((slots, 1), jnp.float32),
        ],
    )(queries, keys, values, grads, live_f.reshape(1, slots), live_f.reshape(slots, 1))


def per_device(
    byte_states,
    conv_kernel,
    mix_weight,
    norm_gain,
    query_weight,
    key_weight,
    value_weight,
    boundaries,
    span_counts,
    grad_attended,
):
    row_count = byte_states.shape[0]
    slot_count = boundaries.shape[0]
    head_width = query_weight.shape[1]
    score_scale = 1.0 / math.sqrt(HD)
    shard_index = lax.axis_index("seq")
    shards = lax.axis_size("seq")
    first_slot = shard_index * slot_count
    own_ids = first_slot + jnp.arange(slot_count, dtype=jnp.int32)
    before_rim = neighbour(byte_states[row_count - (KCONV - 1) :].astype(jnp.float32), 1)
    extended = jnp.concatenate([before_rim.astype(jnp.bfloat16), byte_states], axis=0)
    span_depth = conv_kernel[0] * jnp.take(extended, boundaries + (KCONV - 1), axis=0).astype(
        jnp.float32
    )
    for offset in range(1, KCONV):
        tapped = jnp.take(extended, boundaries + (KCONV - 1 - offset), axis=0).astype(jnp.float32)
        span_depth = span_depth + conv_kernel[offset] * tapped
    span_depth = span_depth.astype(jnp.bfloat16)
    span_bytes = jnp.take(byte_states, boundaries, axis=0).astype(jnp.float32)
    live_mask = jnp.arange(slot_count, dtype=jnp.int32) < span_counts[0]
    span_state = span_bytes + jnp.dot(span_depth, mix_weight, preferred_element_type=jnp.float32)
    inverse_rms = lax.rsqrt(jnp.mean(span_state * span_state, axis=1) + 1e-05)
    normed = (span_state * inverse_rms[:, None] * norm_gain).astype(jnp.bfloat16)
    queries = jnp.dot(normed, query_weight, preferred_element_type=jnp.float32).astype(jnp.bfloat16)
    key_rows = jnp.dot(normed, key_weight, preferred_element_type=jnp.float32).astype(jnp.bfloat16)
    value_rows = jnp.dot(normed, value_weight, preferred_element_type=jnp.float32).astype(
        jnp.bfloat16
    )
    grad_rows = jnp.where(live_mask[:, None], grad_attended, jnp.zeros_like(grad_attended))

    count_rows = jnp.broadcast_to(span_counts[0].astype(jnp.bfloat16), (16, head_width))
    packed = jnp.concatenate([queries, key_rows, value_rows, grad_rows, count_rows], axis=0)
    gathered = gather_blocks(packed, "seq")
    total_slots = shards * slot_count

    def piece(k):
        return gathered[:, k * slot_count : (k + 1) * slot_count].reshape(total_slots, head_width)

    all_queries, all_keys, all_values, all_grads = piece(0), piece(1), piece(2), piece(3)
    all_counts = gathered[:, 4 * slot_count, 0].astype(jnp.int32)
    all_live = (
        jnp.arange(slot_count, dtype=jnp.int32)[None, :] < all_counts[:, None]
    ).reshape(total_slots)
    slot_ids = jnp.arange(total_slots, dtype=jnp.int32)

    all_attended, all_logs, all_deltas = forward_all(
        all_queries, all_keys, all_values, all_grads, all_live
    )
    all_logs = all_logs.reshape(total_slots)
    all_deltas = all_deltas.reshape(total_slots)
    attended = lax.dynamic_slice_in_dim(all_attended, first_slot, slot_count, axis=0)
    own_logs = lax.dynamic_slice_in_dim(all_logs, first_slot, slot_count)
    own_deltas = lax.dynamic_slice_in_dim(all_deltas, first_slot, slot_count)

    allowed = (slot_ids[None, :] <= own_ids[:, None]) & all_live[None, :]
    scores = jnp.dot(queries, all_keys.T, preferred_element_type=jnp.float32) * score_scale
    scores = jnp.where(allowed, scores, masked_score)
    probs_full = jnp.exp(scores - own_logs[:, None])
    grad_probs = jnp.dot(grad_rows, all_values.T, preferred_element_type=jnp.float32)
    grad_scores = (probs_full * (grad_probs - own_deltas[:, None])).astype(jnp.bfloat16)
    query_grad_rows = (
        jnp.dot(grad_scores, all_keys, preferred_element_type=jnp.float32) * score_scale
    ).astype(jnp.bfloat16)

    allowed = (own_ids[None, :] <= slot_ids[:, None]) & live_mask[None, :]
    scores = jnp.dot(all_queries, key_rows.T, preferred_element_type=jnp.float32) * score_scale
    scores = jnp.where(allowed, scores, masked_score)
    probs_full = jnp.exp(scores - all_logs[:, None])
    contract_rows = (((0,), (0,)), ((), ()))
    value_grad_rows = lax.dot_general(
        probs_full.astype(jnp.bfloat16), all_grads, contract_rows, preferred_element_type=jnp.float32
    ).astype(jnp.bfloat16)
    grad_probs = jnp.dot(all_grads, value_rows.T, preferred_element_type=jnp.float32)
    grad_scores = (probs_full * (grad_probs - all_deltas[:, None])).astype(jnp.bfloat16)
    key_grad_rows = (
        lax.dot_general(grad_scores, all_queries, contract_rows, preferred_element_type=jnp.float32)
        * score_scale
    ).astype(jnp.bfloat16)

    contract = (((1,), (1,)), ((), ()))
    partial_normed = lax.dot_general(
        query_grad_rows, query_weight, contract, preferred_element_type=jnp.float32
    )
    partial_normed = partial_normed + lax.dot_general(
        key_grad_rows, key_weight, contract, preferred_element_type=jnp.float32
    )
    partial_normed = partial_normed + lax.dot_general(
        value_grad_rows, value_weight, contract, preferred_element_type=jnp.float32
    )
    grad_normed = summed_over(partial_normed, "head")
    scaled_grad = norm_gain * grad_normed
    cubed = inverse_rms * inverse_rms * inverse_rms
    grad_state = (
        inverse_rms[:, None] * scaled_grad
        - span_state * cubed[:, None] * jnp.mean(scaled_grad * span_state, axis=1)[:, None]
    )
    grad_state = jnp.where(live_mask[:, None], grad_state, jnp.float32(0.0))
    mixed_grad = lax.dot_general(
        grad_state.astype(jnp.bfloat16), mix_weight, contract, preferred_element_type=jnp.float32
    )
    spread_mix = jnp.zeros((row_count, D), jnp.float32).at[boundaries].add(mixed_grad)
    residual_grad = jnp.zeros((row_count, D), jnp.float32).at[boundaries].add(grad_state)
    after_rim = neighbour(spread_mix[: KCONV - 1], -1)
    padded_grad = jnp.concatenate([spread_mix, after_rim], axis=0)
    conv_grad = conv_kernel[0] * spread_mix
    for offset in range(1, KCONV):
        conv_grad = conv_grad + conv_kernel[offset] * padded_grad[offset : offset + row_count]
    grad_bytes = (residual_grad + conv_grad).astype(jnp.bfloat16)
    return (attended, grad_bytes)


def solution(mesh):
    return jax.shard_map(
        per_device,
        mesh=mesh,
        in_specs=(
            P(("doc", "seq"), None),
            P(),
            P(),
            P(),
            P(None, "head"),
            P(None, "head"),
            P(None, "head"),
            P(("doc", "seq")),
            P(("doc", "seq")),
            P(("doc", "seq"), "head"),
        ),
        out_specs=(P(("doc", "seq"), "head"), P(("doc", "seq"), None)),
        check_vma=False,
    )
```

```python
import math

import jax
import jax.numpy as jnp
from jax import lax
from jax.experimental import pallas as pl
from jax.sharding import PartitionSpec as P

D = 1024
HD = 128
KCONV = 4
QBLOCK = 256


masked_score = -1e30


def passed_along(array, axis, by):
    devices = lax.axis_size(axis)
    pairs = [(i, i + by) for i in range(devices) if 0 <= i + by < devices]
    return lax.ppermute(array, axis, pairs)


def neighbour(rim_rows, offset_by):
    return passed_along(rim_rows, "seq", offset_by)


def gather_blocks(block, axis):
    devices = lax.axis_size(axis)
    held = block[None]
    step = 1
    while step < devices:
        other = lax.ppermute(held, axis, [(i, i ^ step) for i in range(devices)])
        held = jnp.concatenate([held, other], axis=0)
        step *= 2
    return held


def summed_over(partial, axis):
    devices = lax.axis_size(axis)
    total = partial
    step = 1
    while step < devices:
        sent = total.astype(jnp.bfloat16)
        got = lax.ppermute(sent, axis, [(i, i ^ step) for i in range(devices)])
        total = sent.astype(jnp.float32) + got.astype(jnp.float32)
        step *= 2
    return total


def forward_kernel(
    q_ref, k_ref, v_ref, g_ref, live_row_ref, live_col_ref, id_row_ref, id_col_ref, att_ref, log_ref, delta_ref
):
    scale = 1.0 / math.sqrt(HD)
    scores = lax.dot_general(
        q_ref[...], k_ref[...], (((1,), (1,)), ((), ())), preferred_element_type=jnp.float32
    ) * scale
    allowed = (id_row_ref[...] <= id_col_ref[...]) & (live_row_ref[...] > 0.5)
    scores = jnp.where(allowed, scores, masked_score)
    row_max = jnp.max(scores, axis=1, keepdims=True)
    softmax_part = jnp.exp(scores - row_max)
    row_sum = jnp.sum(softmax_part, axis=1, keepdims=True)
    product = jnp.dot(
        softmax_part.astype(jnp.bfloat16), v_ref[...], preferred_element_type=jnp.float32
    )
    attention = jnp.where(live_col_ref[...] > 0.5, product / row_sum, 0.0).astype(jnp.bfloat16)
    att_ref[...] = attention
    log_ref[...] = row_max + jnp.log(row_sum)
    delta_ref[...] = jnp.sum(
        g_ref[...].astype(jnp.float32) * attention.astype(jnp.float32), axis=1, keepdims=True
    )


def forward_all(queries, keys, values, grads, live, ids):
    slots, width = queries.shape
    live_f = live.astype(jnp.float32)
    row_spec = pl.BlockSpec((QBLOCK, width), lambda i: (i, 0))
    full_spec = pl.BlockSpec((slots, width), lambda i: (0, 0))
    col_spec = pl.BlockSpec((QBLOCK, 1), lambda i: (i, 0))
    return pl.pallas_call(
        forward_kernel,
        grid=(slots // QBLOCK,),
        in_specs=[row_spec, full_spec, full_spec, row_spec,
                  pl.BlockSpec((1, slots), lambda i: (0, 0)), col_spec,
                  pl.BlockSpec((1, slots), lambda i: (0, 0)), col_spec],
        out_specs=[row_spec, col_spec, col_spec],
        out_shape=[
            jax.ShapeDtypeStruct((slots, width), jnp.bfloat16),
            jax.ShapeDtypeStruct((slots, 1), jnp.float32),
            jax.ShapeDtypeStruct((slots, 1), jnp.float32),
        ],
    )(
        queries, keys, values, grads, live_f.reshape(1, slots), live_f.reshape(slots, 1),
        ids.reshape(1, slots), ids.reshape(slots, 1),
    )


def per_device(
    byte_states,
    conv_kernel,
    mix_weight,
    norm_gain,
    query_weight,
    key_weight,
    value_weight,
    boundaries,
    span_counts,
    grad_attended,
):
    row_count = byte_states.shape[0]
    slot_count = boundaries.shape[0]
    head_width = query_weight.shape[1]
    score_scale = 1.0 / math.sqrt(HD)
    shard_index = lax.axis_index("seq")
    shards = lax.axis_size("seq")
    first_slot = shard_index * slot_count
    own_ids = first_slot + jnp.arange(slot_count, dtype=jnp.int32)
    before_rim = neighbour(byte_states[row_count - (KCONV - 1) :].astype(jnp.float32), 1)
    extended = jnp.concatenate([before_rim.astype(jnp.bfloat16), byte_states], axis=0)
    span_depth = conv_kernel[0] * jnp.take(extended, boundaries + (KCONV - 1), axis=0).astype(
        jnp.float32
    )
    for offset in range(1, KCONV):
        tapped = jnp.take(extended, boundaries + (KCONV - 1 - offset), axis=0).astype(jnp.float32)
        span_depth = span_depth + conv_kernel[offset] * tapped
    span_depth = span_depth.astype(jnp.bfloat16)
    span_bytes = jnp.take(byte_states, boundaries, axis=0).astype(jnp.float32)
    live_mask = jnp.arange(slot_count, dtype=jnp.int32) < span_counts[0]
    span_state = span_bytes + jnp.dot(span_depth, mix_weight, preferred_element_type=jnp.float32)
    inverse_rms = lax.rsqrt(jnp.mean(span_state * span_state, axis=1) + 1e-05)
    normed = (span_state * inverse_rms[:, None] * norm_gain).astype(jnp.bfloat16)
    queries = jnp.dot(normed, query_weight, preferred_element_type=jnp.float32).astype(jnp.bfloat16)
    key_rows = jnp.dot(normed, key_weight, preferred_element_type=jnp.float32).astype(jnp.bfloat16)
    value_rows = jnp.dot(normed, value_weight, preferred_element_type=jnp.float32).astype(
        jnp.bfloat16
    )
    grad_rows = jnp.where(live_mask[:, None], grad_attended, jnp.zeros_like(grad_attended))

    count_rows = jnp.broadcast_to(span_counts[0].astype(jnp.bfloat16), (16, head_width))
    packed = jnp.concatenate([queries, key_rows, value_rows, grad_rows, count_rows], axis=0)
    gathered = gather_blocks(packed, "seq")
    total_slots = shards * slot_count

    def piece(k):
        return gathered[:, k * slot_count : (k + 1) * slot_count].reshape(total_slots, head_width)

    all_queries, all_keys, all_values, all_grads = piece(0), piece(1), piece(2), piece(3)
    all_counts = gathered[:, 4 * slot_count, 0].astype(jnp.int32)
    all_live = (
        jnp.arange(slot_count, dtype=jnp.int32)[None, :] < all_counts[:, None]
    ).reshape(total_slots)
    held_shards = jnp.arange(shards, dtype=jnp.int32) ^ shard_index
    slot_ids = (
        held_shards[:, None] * slot_count + jnp.arange(slot_count, dtype=jnp.int32)[None, :]
    ).reshape(total_slots)

    all_attended, all_logs, all_deltas = forward_all(
        all_queries, all_keys, all_values, all_grads, all_live, slot_ids
    )
    all_logs = all_logs.reshape(total_slots)
    all_deltas = all_deltas.reshape(total_slots)
    attended = all_attended[:slot_count]
    own_logs = all_logs[:slot_count]
    own_deltas = all_deltas[:slot_count]

    allowed = (slot_ids[None, :] <= own_ids[:, None]) & all_live[None, :]
    scores = jnp.dot(queries, all_keys.T, preferred_element_type=jnp.float32) * score_scale
    scores = jnp.where(allowed, scores, masked_score)
    probs_full = jnp.exp(scores - own_logs[:, None])
    grad_probs = jnp.dot(grad_rows, all_values.T, preferred_element_type=jnp.float32)
    grad_scores = (probs_full * (grad_probs - own_deltas[:, None])).astype(jnp.bfloat16)
    query_grad_rows = (
        jnp.dot(grad_scores, all_keys, preferred_element_type=jnp.float32) * score_scale
    ).astype(jnp.bfloat16)

    allowed = (own_ids[None, :] <= slot_ids[:, None]) & live_mask[None, :]
    scores = jnp.dot(all_queries, key_rows.T, preferred_element_type=jnp.float32) * score_scale
    scores = jnp.where(allowed, scores, masked_score)
    probs_full = jnp.exp(scores - all_logs[:, None])
    contract_rows = (((0,), (0,)), ((), ()))
    value_grad_rows = lax.dot_general(
        probs_full.astype(jnp.bfloat16), all_grads, contract_rows, preferred_element_type=jnp.float32
    ).astype(jnp.bfloat16)
    grad_probs = jnp.dot(all_grads, value_rows.T, preferred_element_type=jnp.float32)
    grad_scores = (probs_full * (grad_probs - all_deltas[:, None])).astype(jnp.bfloat16)
    key_grad_rows = (
        lax.dot_general(grad_scores, all_queries, contract_rows, preferred_element_type=jnp.float32)
        * score_scale
    ).astype(jnp.bfloat16)

    contract = (((1,), (1,)), ((), ()))
    partial_normed = lax.dot_general(
        query_grad_rows, query_weight, contract, preferred_element_type=jnp.float32
    )
    partial_normed = partial_normed + lax.dot_general(
        key_grad_rows, key_weight, contract, preferred_element_type=jnp.float32
    )
    partial_normed = partial_normed + lax.dot_general(
        value_grad_rows, value_weight, contract, preferred_element_type=jnp.float32
    )
    grad_normed = summed_over(partial_normed, "head")
    scaled_grad = norm_gain * grad_normed
    cubed = inverse_rms * inverse_rms * inverse_rms
    grad_state = (
        inverse_rms[:, None] * scaled_grad
        - span_state * cubed[:, None] * jnp.mean(scaled_grad * span_state, axis=1)[:, None]
    )
    grad_state = jnp.where(live_mask[:, None], grad_state, jnp.float32(0.0))
    mixed_grad = lax.dot_general(
        grad_state.astype(jnp.bfloat16), mix_weight, contract, preferred_element_type=jnp.float32
    )
    spread_mix = jnp.zeros((row_count, D), jnp.float32).at[boundaries].add(mixed_grad)
    residual_grad = jnp.zeros((row_count, D), jnp.float32).at[boundaries].add(grad_state)
    after_rim = neighbour(spread_mix[: KCONV - 1], -1)
    padded_grad = jnp.concatenate([spread_mix, after_rim], axis=0)
    conv_grad = conv_kernel[0] * spread_mix
    for offset in range(1, KCONV):
        conv_grad = conv_grad + conv_kernel[offset] * padded_grad[offset : offset + row_count]
    grad_bytes = (residual_grad + conv_grad).astype(jnp.bfloat16)
    return (attended, grad_bytes)


def solution(mesh):
    return jax.shard_map(
        per_device,
        mesh=mesh,
        in_specs=(
            P(("doc", "seq"), None),
            P(),
            P(),
            P(),
            P(None, "head"),
            P(None, "head"),
            P(None, "head"),
            P(("doc", "seq")),
            P(("doc", "seq")),
            P(("doc", "seq"), "head"),
        ),
        out_specs=(P(("doc", "seq"), "head"), P(("doc", "seq"), None)),
        check_vma=False,
    )
```

```python
import math

import jax
import jax.numpy as jnp
from jax import lax
from jax.experimental import pallas as pl
from jax.sharding import PartitionSpec as P

D = 1024
HD = 128
KCONV = 4
QBLOCK = 256


masked_score = -1e30


def passed_along(array, axis, by):
    devices = lax.axis_size(axis)
    pairs = [(i, i + by) for i in range(devices) if 0 <= i + by < devices]
    return lax.ppermute(array, axis, pairs)


def neighbour(rim_rows, offset_by):
    return passed_along(rim_rows, "seq", offset_by)


def gather_blocks(block, axis, inner):
    devices = lax.axis_size(axis)
    me = lax.axis_index(axis)
    held = block[None]
    step = 1
    while step < inner:
        other = lax.ppermute(held, axis, [(i, i ^ step) for i in range(devices)])
        held = jnp.concatenate([held, other], axis=0)
        step *= 2
    sources = jnp.arange(inner, dtype=jnp.int32) ^ me
    outer = devices // inner
    if outer == 1:
        return held, sources

    def shifted(array, by):
        return lax.ppermute(array, axis, [(i, (i + by) % devices) for i in range(devices)])

    parts = [held]
    origins = [sources]
    from_below = shifted(held, inner)
    from_above = shifted(held, -inner) if outer > 2 else None
    parts.append(from_below)
    origins.append((sources - inner) % devices)
    if outer > 2:
        parts.append(from_above)
        origins.append((sources + inner) % devices)
    if outer == 4:
        half = inner // 2
        parts.append(shifted(from_below[:half], inner))
        origins.append((sources[:half] - 2 * inner) % devices)
        parts.append(shifted(from_above[half:], -inner))
        origins.append((sources[half:] + 2 * inner) % devices)
    else:
        assert outer <= 3
    return jnp.concatenate(parts, axis=0), jnp.concatenate(origins)


def summed_over(partial, axis):
    devices = lax.axis_size(axis)
    total = partial
    step = 1
    while step < devices:
        sent = total.astype(jnp.bfloat16)
        got = lax.ppermute(sent, axis, [(i, i ^ step) for i in range(devices)])
        total = sent.astype(jnp.float32) + got.astype(jnp.float32)
        step *= 2
    return total


def forward_kernel(
    q_ref, k_ref, v_ref, g_ref, live_row_ref, live_col_ref, id_row_ref, id_col_ref, att_ref, log_ref, delta_ref
):
    scale = 1.0 / math.sqrt(HD)
    scores = lax.dot_general(
        q_ref[...], k_ref[...], (((1,), (1,)), ((), ())), preferred_element_type=jnp.float32
    ) * scale
    allowed = (id_row_ref[...] <= id_col_ref[...]) & (live_row_ref[...] > 0.5)
    scores = jnp.where(allowed, scores, masked_score)
    row_max = jnp.max(scores, axis=1, keepdims=True)
    softmax_part = jnp.exp(scores - row_max)
    row_sum = jnp.sum(softmax_part, axis=1, keepdims=True)
    product = jnp.dot(
        softmax_part.astype(jnp.bfloat16), v_ref[...], preferred_element_type=jnp.float32
    )
    attention = jnp.where(live_col_ref[...] > 0.5, product / row_sum, 0.0).astype(jnp.bfloat16)
    att_ref[...] = attention
    log_ref[...] = row_max + jnp.log(row_sum)
    delta_ref[...] = jnp.sum(
        g_ref[...].astype(jnp.float32) * attention.astype(jnp.float32), axis=1, keepdims=True
    )


def forward_all(queries, keys, values, grads, live, ids):
    slots, width = queries.shape
    live_f = live.astype(jnp.float32)
    row_spec = pl.BlockSpec((QBLOCK, width), lambda i: (i, 0))
    full_spec = pl.BlockSpec((slots, width), lambda i: (0, 0))
    col_spec = pl.BlockSpec((QBLOCK, 1), lambda i: (i, 0))
    return pl.pallas_call(
        forward_kernel,
        grid=(slots // QBLOCK,),
        in_specs=[row_spec, full_spec, full_spec, row_spec,
                  pl.BlockSpec((1, slots), lambda i: (0, 0)), col_spec,
                  pl.BlockSpec((1, slots), lambda i: (0, 0)), col_spec],
        out_specs=[row_spec, col_spec, col_spec],
        out_shape=[
            jax.ShapeDtypeStruct((slots, width), jnp.bfloat16),
            jax.ShapeDtypeStruct((slots, 1), jnp.float32),
            jax.ShapeDtypeStruct((slots, 1), jnp.float32),
        ],
    )(
        queries, keys, values, grads, live_f.reshape(1, slots), live_f.reshape(slots, 1),
        ids.reshape(1, slots), ids.reshape(slots, 1),
    )


def per_device(
    byte_states,
    conv_kernel,
    mix_weight,
    norm_gain,
    query_weight,
    key_weight,
    value_weight,
    boundaries,
    span_counts,
    grad_attended,
):
    row_count = byte_states.shape[0]
    slot_count = boundaries.shape[0]
    head_width = query_weight.shape[1]
    score_scale = 1.0 / math.sqrt(HD)
    shard_index = lax.axis_index("seq")
    shards = lax.axis_size("seq")
    first_slot = shard_index * slot_count
    own_ids = first_slot + jnp.arange(slot_count, dtype=jnp.int32)
    before_rim = neighbour(byte_states[row_count - (KCONV - 1) :].astype(jnp.float32), 1)
    extended = jnp.concatenate([before_rim.astype(jnp.bfloat16), byte_states], axis=0)
    span_depth = conv_kernel[0] * jnp.take(extended, boundaries + (KCONV - 1), axis=0).astype(
        jnp.float32
    )
    for offset in range(1, KCONV):
        tapped = jnp.take(extended, boundaries + (KCONV - 1 - offset), axis=0).astype(jnp.float32)
        span_depth = span_depth + conv_kernel[offset] * tapped
    span_depth = span_depth.astype(jnp.bfloat16)
    span_bytes = jnp.take(byte_states, boundaries, axis=0).astype(jnp.float32)
    live_mask = jnp.arange(slot_count, dtype=jnp.int32) < span_counts[0]
    span_state = span_bytes + jnp.dot(span_depth, mix_weight, preferred_element_type=jnp.float32)
    inverse_rms = lax.rsqrt(jnp.mean(span_state * span_state, axis=1) + 1e-05)
    normed = (span_state * inverse_rms[:, None] * norm_gain).astype(jnp.bfloat16)
    queries = jnp.dot(normed, query_weight, preferred_element_type=jnp.float32).astype(jnp.bfloat16)
    key_rows = jnp.dot(normed, key_weight, preferred_element_type=jnp.float32).astype(jnp.bfloat16)
    value_rows = jnp.dot(normed, value_weight, preferred_element_type=jnp.float32).astype(
        jnp.bfloat16
    )
    grad_rows = jnp.where(live_mask[:, None], grad_attended, jnp.zeros_like(grad_attended))

    count_rows = jnp.broadcast_to(span_counts[0].astype(jnp.bfloat16), (16, head_width))
    packed = jnp.concatenate([queries, key_rows, value_rows, grad_rows, count_rows], axis=0)
    gathered, held_shards = gather_blocks(packed, "seq", 8 if shards == 32 else shards)
    total_slots = shards * slot_count

    def piece(k):
        return gathered[:, k * slot_count : (k + 1) * slot_count].reshape(total_slots, head_width)

    all_queries, all_keys, all_values, all_grads = piece(0), piece(1), piece(2), piece(3)
    all_counts = gathered[:, 4 * slot_count, 0].astype(jnp.int32)
    all_live = (
        jnp.arange(slot_count, dtype=jnp.int32)[None, :] < all_counts[:, None]
    ).reshape(total_slots)
    slot_ids = (
        held_shards[:, None] * slot_count + jnp.arange(slot_count, dtype=jnp.int32)[None, :]
    ).reshape(total_slots)

    all_attended, all_logs, all_deltas = forward_all(
        all_queries, all_keys, all_values, all_grads, all_live, slot_ids
    )
    all_logs = all_logs.reshape(total_slots)
    all_deltas = all_deltas.reshape(total_slots)
    attended = all_attended[:slot_count]
    own_logs = all_logs[:slot_count]
    own_deltas = all_deltas[:slot_count]

    allowed = (slot_ids[None, :] <= own_ids[:, None]) & all_live[None, :]
    scores = jnp.dot(queries, all_keys.T, preferred_element_type=jnp.float32) * score_scale
    scores = jnp.where(allowed, scores, masked_score)
    probs_full = jnp.exp(scores - own_logs[:, None])
    grad_probs = jnp.dot(grad_rows, all_values.T, preferred_element_type=jnp.float32)
    grad_scores = (probs_full * (grad_probs - own_deltas[:, None])).astype(jnp.bfloat16)
    query_grad_rows = (
        jnp.dot(grad_scores, all_keys, preferred_element_type=jnp.float32) * score_scale
    ).astype(jnp.bfloat16)

    allowed = (own_ids[None, :] <= slot_ids[:, None]) & live_mask[None, :]
    scores = jnp.dot(all_queries, key_rows.T, preferred_element_type=jnp.float32) * score_scale
    scores = jnp.where(allowed, scores, masked_score)
    probs_full = jnp.exp(scores - all_logs[:, None])
    contract_rows = (((0,), (0,)), ((), ()))
    value_grad_rows = lax.dot_general(
        probs_full.astype(jnp.bfloat16), all_grads, contract_rows, preferred_element_type=jnp.float32
    ).astype(jnp.bfloat16)
    grad_probs = jnp.dot(all_grads, value_rows.T, preferred_element_type=jnp.float32)
    grad_scores = (probs_full * (grad_probs - all_deltas[:, None])).astype(jnp.bfloat16)
    key_grad_rows = (
        lax.dot_general(grad_scores, all_queries, contract_rows, preferred_element_type=jnp.float32)
        * score_scale
    ).astype(jnp.bfloat16)

    contract = (((1,), (1,)), ((), ()))
    partial_normed = lax.dot_general(
        query_grad_rows, query_weight, contract, preferred_element_type=jnp.float32
    )
    partial_normed = partial_normed + lax.dot_general(
        key_grad_rows, key_weight, contract, preferred_element_type=jnp.float32
    )
    partial_normed = partial_normed + lax.dot_general(
        value_grad_rows, value_weight, contract, preferred_element_type=jnp.float32
    )
    grad_normed = summed_over(partial_normed, "head")
    scaled_grad = norm_gain * grad_normed
    cubed = inverse_rms * inverse_rms * inverse_rms
    grad_state = (
        inverse_rms[:, None] * scaled_grad
        - span_state * cubed[:, None] * jnp.mean(scaled_grad * span_state, axis=1)[:, None]
    )
    grad_state = jnp.where(live_mask[:, None], grad_state, jnp.float32(0.0))
    mixed_grad = lax.dot_general(
        grad_state.astype(jnp.bfloat16), mix_weight, contract, preferred_element_type=jnp.float32
    )
    spread_mix = jnp.zeros((row_count, D), jnp.float32).at[boundaries].add(mixed_grad)
    residual_grad = jnp.zeros((row_count, D), jnp.float32).at[boundaries].add(grad_state)
    after_rim = neighbour(spread_mix[: KCONV - 1], -1)
    padded_grad = jnp.concatenate([spread_mix, after_rim], axis=0)
    conv_grad = conv_kernel[0] * spread_mix
    for offset in range(1, KCONV):
        conv_grad = conv_grad + conv_kernel[offset] * padded_grad[offset : offset + row_count]
    grad_bytes = (residual_grad + conv_grad).astype(jnp.bfloat16)
    return (attended, grad_bytes)


def solution(mesh):
    return jax.shard_map(
        per_device,
        mesh=mesh,
        in_specs=(
            P(("doc", "seq"), None),
            P(),
            P(),
            P(),
            P(None, "head"),
            P(None, "head"),
            P(None, "head"),
            P(("doc", "seq")),
            P(("doc", "seq")),
            P(("doc", "seq"), "head"),
        ),
        out_specs=(P(("doc", "seq"), "head"), P(("doc", "seq"), None)),
        check_vma=False,
    )
```

```python
import math

import jax
import jax.numpy as jnp
from jax import lax
from jax.experimental import pallas as pl
from jax.experimental.pallas import tpu as pltpu
from jax.sharding import PartitionSpec as P

D = 1024
HD = 128
KCONV = 4
QBLOCK = 256
BLOCKS_PER_STEP = 4


masked_score = -1e30


def passed_along(array, axis, by):
    devices = lax.axis_size(axis)
    pairs = [(i, i + by) for i in range(devices) if 0 <= i + by < devices]
    return lax.ppermute(array, axis, pairs)


def neighbour(rim_rows, offset_by):
    return passed_along(rim_rows, "seq", offset_by)


def gather_blocks(block, axis, inner):
    devices = lax.axis_size(axis)
    me = lax.axis_index(axis)
    held = block[None]
    step = 1
    while step < inner:
        other = lax.ppermute(held, axis, [(i, i ^ step) for i in range(devices)])
        held = jnp.concatenate([held, other], axis=0)
        step *= 2
    sources = jnp.arange(inner, dtype=jnp.int32) ^ me
    outer = devices // inner
    if outer == 1:
        return held, sources

    def shifted(array, by):
        return lax.ppermute(array, axis, [(i, (i + by) % devices) for i in range(devices)])

    parts = [held]
    origins = [sources]
    from_below = shifted(held, inner)
    from_above = shifted(held, -inner) if outer > 2 else None
    parts.append(from_below)
    origins.append((sources - inner) % devices)
    if outer > 2:
        parts.append(from_above)
        origins.append((sources + inner) % devices)
    if outer == 4:
        half = inner // 2
        parts.append(shifted(from_below[:half], inner))
        origins.append((sources[:half] - 2 * inner) % devices)
        parts.append(shifted(from_above[half:], -inner))
        origins.append((sources[half:] + 2 * inner) % devices)
    else:
        assert outer <= 3
    return jnp.concatenate(parts, axis=0), jnp.concatenate(origins)


def summed_over(partial, axis):
    devices = lax.axis_size(axis)
    total = partial
    step = 1
    while step < devices:
        sent = total.astype(jnp.bfloat16)
        got = lax.ppermute(sent, axis, [(i, i ^ step) for i in range(devices)])
        total = sent.astype(jnp.float32) + got.astype(jnp.float32)
        step *= 2
    return total


def forward_kernel(shards_ref, q_ref, k_ref, v_ref, g_ref, key_code_ref, att_ref, log_ref, delta_ref):
    rows = q_ref.shape[0]
    block_rows = rows // BLOCKS_PER_STEP
    first = pl.program_id(0) * BLOCKS_PER_STEP
    row = lax.broadcasted_iota(jnp.int32, (rows, 1), 0)
    q_ids = row % block_rows
    for t in range(BLOCKS_PER_STEP):
        q_ids = q_ids + jnp.where(row // block_rows == t, shards_ref[first + t] * block_rows, 0)
    scale = 1.0 / math.sqrt(HD)
    scores = lax.dot_general(
        q_ref[...], k_ref[...], (((1,), (1,)), ((), ())), preferred_element_type=jnp.float32
    ) * scale
    scores = jnp.where(key_code_ref[...] <= q_ids, scores, masked_score)
    row_max = jnp.max(scores, axis=1, keepdims=True)
    softmax_part = jnp.exp(scores - row_max)
    row_sum = jnp.sum(softmax_part, axis=1, keepdims=True)
    product = jnp.dot(
        softmax_part.astype(jnp.bfloat16), v_ref[...], preferred_element_type=jnp.float32
    )
    attention = (product / row_sum).astype(jnp.bfloat16)
    att_ref[...] = attention
    log_ref[...] = row_max + jnp.log(row_sum)
    delta_ref[...] = jnp.sum(
        g_ref[...].astype(jnp.float32) * attention.astype(jnp.float32), axis=1, keepdims=True
    )


def forward_all(queries, keys, values, grads, key_code, held_shards):
    slots, width = queries.shape
    row_spec = pl.BlockSpec((QBLOCK, width), lambda i, shards: (i, 0))
    full_spec = pl.BlockSpec((slots, width), lambda i, shards: (0, 0))
    col_spec = pl.BlockSpec((QBLOCK, 1), lambda i, shards: (i, 0))
    grid_spec = pltpu.PrefetchScalarGridSpec(
        num_scalar_prefetch=1,
        grid=(slots // QBLOCK,),
        in_specs=[row_spec, full_spec, full_spec, row_spec,
                  pl.BlockSpec((1, slots), lambda i, shards: (0, 0))],
        out_specs=[row_spec, col_spec, col_spec],
    )
    return pl.pallas_call(
        forward_kernel,
        grid_spec=grid_spec,
        out_shape=[
            jax.ShapeDtypeStruct((slots, width), jnp.bfloat16),
            jax.ShapeDtypeStruct((slots, 1), jnp.float32),
            jax.ShapeDtypeStruct((slots, 1), jnp.float32),
        ],
    )(held_shards, queries, keys, values, grads, key_code.reshape(1, slots))


def per_device(
    byte_states,
    conv_kernel,
    mix_weight,
    norm_gain,
    query_weight,
    key_weight,
    value_weight,
    boundaries,
    span_counts,
    grad_attended,
):
    row_count = byte_states.shape[0]
    slot_count = boundaries.shape[0]
    head_width = query_weight.shape[1]
    score_scale = 1.0 / math.sqrt(HD)
    shard_index = lax.axis_index("seq")
    shards = lax.axis_size("seq")
    first_slot = shard_index * slot_count
    own_ids = first_slot + jnp.arange(slot_count, dtype=jnp.int32)
    before_rim = neighbour(byte_states[row_count - (KCONV - 1) :].astype(jnp.float32), 1)
    extended = jnp.concatenate([before_rim.astype(jnp.bfloat16), byte_states], axis=0)
    tap_rows = (boundaries[None, :] + jnp.arange(KCONV - 1, -1, -1, dtype=jnp.int32)[:, None])
    tapped = jnp.take(extended, tap_rows.reshape(-1), axis=0).astype(jnp.float32)
    tapped = tapped.reshape(KCONV, slot_count, D)
    span_depth = conv_kernel[0] * tapped[0]
    for offset in range(1, KCONV):
        span_depth = span_depth + conv_kernel[offset] * tapped[offset]
    span_depth = span_depth.astype(jnp.bfloat16)
    span_bytes = tapped[0]
    live_mask = jnp.arange(slot_count, dtype=jnp.int32) < span_counts[0]
    span_state = span_bytes + jnp.dot(span_depth, mix_weight, preferred_element_type=jnp.float32)
    inverse_rms = lax.rsqrt(jnp.mean(span_state * span_state, axis=1) + 1e-05)
    normed = (span_state * inverse_rms[:, None] * norm_gain).astype(jnp.bfloat16)
    queries = jnp.dot(normed, query_weight, preferred_element_type=jnp.float32).astype(jnp.bfloat16)
    key_rows = jnp.dot(normed, key_weight, preferred_element_type=jnp.float32).astype(jnp.bfloat16)
    value_rows = jnp.dot(normed, value_weight, preferred_element_type=jnp.float32).astype(
        jnp.bfloat16
    )
    grad_rows = jnp.where(live_mask[:, None], grad_attended, jnp.zeros_like(grad_attended))

    count_rows = jnp.broadcast_to(span_counts[0].astype(jnp.bfloat16), (16, head_width))
    packed = jnp.concatenate([queries, key_rows, value_rows, grad_rows, count_rows], axis=0)
    gathered, held_shards = gather_blocks(packed, "seq", 8 if shards == 32 else shards)
    total_slots = shards * slot_count

    def piece(k):
        return gathered[:, k * slot_count : (k + 1) * slot_count].reshape(total_slots, head_width)

    all_queries, all_keys, all_values, all_grads = piece(0), piece(1), piece(2), piece(3)
    all_counts = gathered[:, 4 * slot_count, 0].astype(jnp.int32)
    all_live = (
        jnp.arange(slot_count, dtype=jnp.int32)[None, :] < all_counts[:, None]
    ).reshape(total_slots)
    slot_ids = (
        held_shards[:, None] * slot_count + jnp.arange(slot_count, dtype=jnp.int32)[None, :]
    ).reshape(total_slots)

    all_attended, all_logs, all_deltas = forward_all(
        all_queries, all_keys, all_values, all_grads,
        jnp.where(all_live, slot_ids, total_slots), held_shards,
    )
    all_logs = all_logs.reshape(total_slots)
    all_deltas = all_deltas.reshape(total_slots)
    attended = jnp.where(live_mask[:, None], all_attended[:slot_count], jnp.bfloat16(0.0))
    own_logs = all_logs[:slot_count]
    own_deltas = all_deltas[:slot_count]

    allowed = (slot_ids[None, :] <= own_ids[:, None]) & all_live[None, :]
    scores = jnp.dot(queries, all_keys.T, preferred_element_type=jnp.float32) * score_scale
    scores = jnp.where(allowed, scores, masked_score)
    probs_full = jnp.exp(scores - own_logs[:, None])
    grad_probs = jnp.dot(grad_rows, all_values.T, preferred_element_type=jnp.float32)
    grad_scores = (probs_full * (grad_probs - own_deltas[:, None])).astype(jnp.bfloat16)
    query_grad_rows = (
        jnp.dot(grad_scores, all_keys, preferred_element_type=jnp.float32) * score_scale
    ).astype(jnp.bfloat16)

    allowed = (own_ids[None, :] <= slot_ids[:, None]) & live_mask[None, :]
    scores = jnp.dot(all_queries, key_rows.T, preferred_element_type=jnp.float32) * score_scale
    scores = jnp.where(allowed, scores, masked_score)
    probs_full = jnp.exp(scores - all_logs[:, None])
    contract_rows = (((0,), (0,)), ((), ()))
    value_grad_rows = lax.dot_general(
        probs_full.astype(jnp.bfloat16), all_grads, contract_rows, preferred_element_type=jnp.float32
    ).astype(jnp.bfloat16)
    grad_probs = jnp.dot(all_grads, value_rows.T, preferred_element_type=jnp.float32)
    grad_scores = (probs_full * (grad_probs - all_deltas[:, None])).astype(jnp.bfloat16)
    key_grad_rows = (
        lax.dot_general(grad_scores, all_queries, contract_rows, preferred_element_type=jnp.float32)
        * score_scale
    ).astype(jnp.bfloat16)

    contract = (((1,), (1,)), ((), ()))
    partial_normed = lax.dot_general(
        query_grad_rows, query_weight, contract, preferred_element_type=jnp.float32
    )
    partial_normed = partial_normed + lax.dot_general(
        key_grad_rows, key_weight, contract, preferred_element_type=jnp.float32
    )
    partial_normed = partial_normed + lax.dot_general(
        value_grad_rows, value_weight, contract, preferred_element_type=jnp.float32
    )
    grad_normed = summed_over(partial_normed, "head")
    scaled_grad = norm_gain * grad_normed
    cubed = inverse_rms * inverse_rms * inverse_rms
    grad_state = (
        inverse_rms[:, None] * scaled_grad
        - span_state * cubed[:, None] * jnp.mean(scaled_grad * span_state, axis=1)[:, None]
    )
    grad_state = jnp.where(live_mask[:, None], grad_state, jnp.float32(0.0))
    mixed_grad = lax.dot_general(
        grad_state.astype(jnp.bfloat16), mix_weight, contract, preferred_element_type=jnp.float32
    )
    spread_mix = jnp.zeros((row_count, D), jnp.float32).at[boundaries].add(mixed_grad)
    residual_grad = jnp.zeros((row_count, D), jnp.float32).at[boundaries].add(grad_state)
    after_rim = neighbour(spread_mix[: KCONV - 1], -1)
    padded_grad = jnp.concatenate([spread_mix, after_rim], axis=0)
    conv_grad = conv_kernel[0] * spread_mix
    for offset in range(1, KCONV):
        conv_grad = conv_grad + conv_kernel[offset] * padded_grad[offset : offset + row_count]
    grad_bytes = (residual_grad + conv_grad).astype(jnp.bfloat16)
    return (attended, grad_bytes)


def solution(mesh):
    return jax.shard_map(
        per_device,
        mesh=mesh,
        in_specs=(
            P(("doc", "seq"), None),
            P(),
            P(),
            P(),
            P(None, "head"),
            P(None, "head"),
            P(None, "head"),
            P(("doc", "seq")),
            P(("doc", "seq")),
            P(("doc", "seq"), "head"),
        ),
        out_specs=(P(("doc", "seq"), "head"), P(("doc", "seq"), None)),
        check_vma=False,
    )
```

```python
import math

import jax
import jax.numpy as jnp
from jax import lax
from jax.experimental import pallas as pl
from jax.experimental.pallas import tpu as pltpu
from jax.sharding import PartitionSpec as P

D = 1024
HD = 128
KCONV = 4
QBLOCK = 256
BLOCKS_PER_STEP = 4


masked_score = -1e30


def passed_along(array, axis, by):
    devices = lax.axis_size(axis)
    pairs = [(i, i + by) for i in range(devices) if 0 <= i + by < devices]
    return lax.ppermute(array, axis, pairs)


def neighbour(rim_rows, offset_by):
    return passed_along(rim_rows, "seq", offset_by)


def gather_blocks(block, axis, inner):
    devices = lax.axis_size(axis)
    me = lax.axis_index(axis)
    held = block[None]
    step = 1
    while step < inner:
        other = lax.ppermute(held, axis, [(i, i ^ step) for i in range(devices)])
        held = jnp.concatenate([held, other], axis=0)
        step *= 2
    sources = jnp.arange(inner, dtype=jnp.int32) ^ me
    outer = devices // inner
    if outer == 1:
        return held, sources

    def shifted(array, by):
        return lax.ppermute(array, axis, [(i, (i + by) % devices) for i in range(devices)])

    parts = [held]
    origins = [sources]
    from_below = shifted(held, inner)
    from_above = shifted(held, -inner) if outer > 2 else None
    parts.append(from_below)
    origins.append((sources - inner) % devices)
    if outer > 2:
        parts.append(from_above)
        origins.append((sources + inner) % devices)
    if outer == 4:
        half = inner // 2
        parts.append(shifted(from_below[:half], inner))
        origins.append((sources[:half] - 2 * inner) % devices)
        parts.append(shifted(from_above[half:], -inner))
        origins.append((sources[half:] + 2 * inner) % devices)
    else:
        assert outer <= 3
    return jnp.concatenate(parts, axis=0), jnp.concatenate(origins)


def summed_over(partial, axis):
    devices = lax.axis_size(axis)
    total = partial
    step = 1
    while step < devices:
        sent = total.astype(jnp.bfloat16)
        got = lax.ppermute(sent, axis, [(i, i ^ step) for i in range(devices)])
        total = sent.astype(jnp.float32) + got.astype(jnp.float32)
        step *= 2
    return total


def forward_kernel(shards_ref, q_ref, k_ref, v_ref, g_ref, key_code_ref, att_ref, log_ref, delta_ref):
    rows = q_ref.shape[0]
    block_rows = rows // BLOCKS_PER_STEP
    first = pl.program_id(0) * BLOCKS_PER_STEP
    row = lax.broadcasted_iota(jnp.int32, (rows, 1), 0)
    q_ids = row % block_rows
    for t in range(BLOCKS_PER_STEP):
        q_ids = q_ids + jnp.where(row // block_rows == t, shards_ref[first + t] * block_rows, 0)
    scale = 1.0 / math.sqrt(HD)
    scores = lax.dot_general(
        q_ref[...], k_ref[...], (((1,), (1,)), ((), ())), preferred_element_type=jnp.float32
    ) * scale
    scores = jnp.where(key_code_ref[...] <= q_ids, scores, masked_score)
    row_max = jnp.max(scores, axis=1, keepdims=True)
    softmax_part = jnp.exp(scores - row_max)
    row_sum = jnp.sum(softmax_part, axis=1, keepdims=True)
    product = jnp.dot(
        softmax_part.astype(jnp.bfloat16), v_ref[...], preferred_element_type=jnp.float32
    )
    attention = (product / row_sum).astype(jnp.bfloat16)
    att_ref[...] = attention
    log_ref[...] = row_max + jnp.log(row_sum)
    delta_ref[...] = jnp.sum(
        g_ref[...].astype(jnp.float32) * attention.astype(jnp.float32), axis=1, keepdims=True
    )


def forward_all(queries, keys, values, grads, key_code, held_shards):
    slots, width = queries.shape
    row_spec = pl.BlockSpec((QBLOCK, width), lambda i, shards: (i, 0))
    full_spec = pl.BlockSpec((slots, width), lambda i, shards: (0, 0))
    col_spec = pl.BlockSpec((QBLOCK, 1), lambda i, shards: (i, 0))
    grid_spec = pltpu.PrefetchScalarGridSpec(
        num_scalar_prefetch=1,
        grid=(slots // QBLOCK,),
        in_specs=[row_spec, full_spec, full_spec, row_spec,
                  pl.BlockSpec((1, slots), lambda i, shards: (0, 0))],
        out_specs=[row_spec, col_spec, col_spec],
    )
    return pl.pallas_call(
        forward_kernel,
        grid_spec=grid_spec,
        out_shape=[
            jax.ShapeDtypeStruct((slots, width), jnp.bfloat16),
            jax.ShapeDtypeStruct((slots, 1), jnp.float32),
            jax.ShapeDtypeStruct((slots, 1), jnp.float32),
        ],
    )(held_shards, queries, keys, values, grads, key_code.reshape(1, slots))


def per_device(
    byte_states,
    conv_kernel,
    mix_weight,
    norm_gain,
    query_weight,
    key_weight,
    value_weight,
    boundaries,
    span_counts,
    grad_attended,
):
    row_count = byte_states.shape[0]
    slot_count = boundaries.shape[0]
    head_width = query_weight.shape[1]
    score_scale = 1.0 / math.sqrt(HD)
    shard_index = lax.axis_index("seq")
    shards = lax.axis_size("seq")
    first_slot = shard_index * slot_count
    own_ids = first_slot + jnp.arange(slot_count, dtype=jnp.int32)
    before_rim = neighbour(byte_states[row_count - (KCONV - 1) :].astype(jnp.float32), 1)
    extended = jnp.concatenate([before_rim.astype(jnp.bfloat16), byte_states], axis=0)
    tap_rows = (boundaries[None, :] + jnp.arange(KCONV - 1, -1, -1, dtype=jnp.int32)[:, None])
    tapped = jnp.take(extended, tap_rows.reshape(-1), axis=0).astype(jnp.float32)
    tapped = tapped.reshape(KCONV, slot_count, D)
    span_depth = conv_kernel[0] * tapped[0]
    for offset in range(1, KCONV):
        span_depth = span_depth + conv_kernel[offset] * tapped[offset]
    span_depth = span_depth.astype(jnp.bfloat16)
    span_bytes = tapped[0]
    live_mask = jnp.arange(slot_count, dtype=jnp.int32) < span_counts[0]
    span_state = span_bytes + jnp.dot(span_depth, mix_weight, preferred_element_type=jnp.float32)
    inverse_rms = lax.rsqrt(jnp.mean(span_state * span_state, axis=1) + 1e-05)
    normed = (span_state * inverse_rms[:, None] * norm_gain).astype(jnp.bfloat16)
    queries = jnp.dot(normed, query_weight, preferred_element_type=jnp.float32).astype(jnp.bfloat16)
    key_rows = jnp.dot(normed, key_weight, preferred_element_type=jnp.float32).astype(jnp.bfloat16)
    value_rows = jnp.dot(normed, value_weight, preferred_element_type=jnp.float32).astype(
        jnp.bfloat16
    )
    grad_rows = jnp.where(live_mask[:, None], grad_attended, jnp.zeros_like(grad_attended))

    count_rows = jnp.broadcast_to(span_counts[0].astype(jnp.bfloat16), (16, head_width))
    packed = jnp.concatenate([queries, key_rows, value_rows, grad_rows, count_rows], axis=0)
    gathered, held_shards = gather_blocks(packed, "seq", 8 if shards == 32 else shards)
    total_slots = shards * slot_count

    def piece(k):
        return gathered[:, k * slot_count : (k + 1) * slot_count].reshape(total_slots, head_width)

    all_queries, all_keys, all_values, all_grads = piece(0), piece(1), piece(2), piece(3)
    all_counts = gathered[:, 4 * slot_count, 0].astype(jnp.int32)
    all_live = (
        jnp.arange(slot_count, dtype=jnp.int32)[None, :] < all_counts[:, None]
    ).reshape(total_slots)
    slot_ids = (
        held_shards[:, None] * slot_count + jnp.arange(slot_count, dtype=jnp.int32)[None, :]
    ).reshape(total_slots)

    all_attended, all_logs, all_deltas = forward_all(
        all_queries, all_keys, all_values, all_grads,
        jnp.where(all_live, slot_ids, total_slots), held_shards,
    )
    all_logs = all_logs.reshape(total_slots)
    all_deltas = all_deltas.reshape(total_slots)
    attended = jnp.where(live_mask[:, None], all_attended[:slot_count], jnp.bfloat16(0.0))
    own_logs = all_logs[:slot_count]
    own_deltas = all_deltas[:slot_count]

    allowed = (slot_ids[None, :] <= own_ids[:, None]) & all_live[None, :]
    scores = jnp.dot(queries, all_keys.T, preferred_element_type=jnp.float32) * score_scale
    scores = jnp.where(allowed, scores, masked_score)
    probs_full = jnp.exp(scores - own_logs[:, None])
    grad_probs = jnp.dot(grad_rows, all_values.T, preferred_element_type=jnp.float32)
    grad_scores = (probs_full * (grad_probs - own_deltas[:, None])).astype(jnp.bfloat16)
    query_grad_rows = (
        jnp.dot(grad_scores, all_keys, preferred_element_type=jnp.float32) * score_scale
    ).astype(jnp.bfloat16)

    allowed = (own_ids[None, :] <= slot_ids[:, None]) & live_mask[None, :]
    scores = jnp.dot(all_queries, key_rows.T, preferred_element_type=jnp.float32) * score_scale
    scores = jnp.where(allowed, scores, masked_score)
    probs_full = jnp.exp(scores - all_logs[:, None])
    contract_rows = (((0,), (0,)), ((), ()))
    value_grad_rows = lax.dot_general(
        probs_full.astype(jnp.bfloat16), all_grads, contract_rows, preferred_element_type=jnp.float32
    ).astype(jnp.bfloat16)
    grad_probs = jnp.dot(all_grads, value_rows.T, preferred_element_type=jnp.float32)
    grad_scores = (probs_full * (grad_probs - all_deltas[:, None])).astype(jnp.bfloat16)
    key_grad_rows = (
        lax.dot_general(grad_scores, all_queries, contract_rows, preferred_element_type=jnp.float32)
        * score_scale
    ).astype(jnp.bfloat16)

    contract = (((1,), (1,)), ((), ()))
    partial_normed = lax.dot_general(
        query_grad_rows, query_weight, contract, preferred_element_type=jnp.float32
    )
    partial_normed = partial_normed + lax.dot_general(
        key_grad_rows, key_weight, contract, preferred_element_type=jnp.float32
    )
    partial_normed = partial_normed + lax.dot_general(
        value_grad_rows, value_weight, contract, preferred_element_type=jnp.float32
    )
    grad_normed = summed_over(partial_normed, "head")
    scaled_grad = norm_gain * grad_normed
    cubed = inverse_rms * inverse_rms * inverse_rms
    grad_state = (
        inverse_rms[:, None] * scaled_grad
        - span_state * cubed[:, None] * jnp.mean(scaled_grad * span_state, axis=1)[:, None]
    )
    grad_state = jnp.where(live_mask[:, None], grad_state, jnp.float32(0.0))
    mixed_grad = lax.dot_general(
        grad_state.astype(jnp.bfloat16), mix_weight, contract, preferred_element_type=jnp.float32
    )
    mixed_grad = mixed_grad.astype(jnp.float32)
    contributions = jnp.concatenate(
        [grad_state + conv_kernel[0] * mixed_grad]
        + [conv_kernel[offset] * mixed_grad for offset in range(1, KCONV)],
        axis=0,
    )
    target_rows = (
        boundaries[None, :] - jnp.arange(KCONV, dtype=jnp.int32)[:, None]
    ).reshape(KCONV * slot_count)
    exact = lax.Precision.HIGHEST
    rim_rows = jnp.arange(-(KCONV - 1), 0, dtype=jnp.int32)
    rim_pick = (rim_rows[:, None] == target_rows[None, :]).astype(jnp.float32)
    before_rows = jnp.dot(rim_pick, contributions, precision=exact)
    after_rim = neighbour(before_rows, -1)
    row_pick = (
        jnp.arange(row_count, dtype=jnp.int32)[:, None] == target_rows[None, :]
    ).astype(jnp.float32)
    local_grad = jnp.dot(row_pick, contributions, precision=exact)
    tail = jnp.concatenate(
        [jnp.zeros((row_count - (KCONV - 1), D), jnp.float32), after_rim], axis=0
    )
    grad_bytes = (local_grad + tail).astype(jnp.bfloat16)
    return (attended, grad_bytes)


def solution(mesh):
    return jax.shard_map(
        per_device,
        mesh=mesh,
        in_specs=(
            P(("doc", "seq"), None),
            P(),
            P(),
            P(),
            P(None, "head"),
            P(None, "head"),
            P(None, "head"),
            P(("doc", "seq")),
            P(("doc", "seq")),
            P(("doc", "seq"), "head"),
        ),
        out_specs=(P(("doc", "seq"), "head"), P(("doc", "seq"), None)),
        check_vma=False,
    )
```

```python
import math

import jax
import jax.numpy as jnp
from jax import lax
from jax.experimental import pallas as pl
from jax.experimental.pallas import tpu as pltpu
from jax.sharding import PartitionSpec as P

D = 1024
HD = 128
KCONV = 4
QBLOCK = 256
BLOCKS_PER_STEP = 4


masked_score = -1e30


def passed_along(array, axis, by):
    devices = lax.axis_size(axis)
    pairs = [(i, i + by) for i in range(devices) if 0 <= i + by < devices]
    return lax.ppermute(array, axis, pairs)


def neighbour(rim_rows, offset_by):
    return passed_along(rim_rows, "seq", offset_by)


def gather_blocks(block, axis, inner):
    devices = lax.axis_size(axis)
    me = lax.axis_index(axis)
    held = block[None]
    step = 1
    while step < inner:
        other = lax.ppermute(held, axis, [(i, i ^ step) for i in range(devices)])
        held = jnp.concatenate([held, other], axis=0)
        step *= 2
    sources = jnp.arange(inner, dtype=jnp.int32) ^ me
    outer = devices // inner
    if outer == 1:
        return held, sources

    def shifted(array, by):
        return lax.ppermute(array, axis, [(i, (i + by) % devices) for i in range(devices)])

    parts = [held]
    origins = [sources]
    from_below = shifted(held, inner)
    from_above = shifted(held, -inner) if outer > 2 else None
    parts.append(from_below)
    origins.append((sources - inner) % devices)
    if outer > 2:
        parts.append(from_above)
        origins.append((sources + inner) % devices)
    if outer == 4:
        half = inner // 2
        parts.append(shifted(from_below[:half], inner))
        origins.append((sources[:half] - 2 * inner) % devices)
        parts.append(shifted(from_above[half:], -inner))
        origins.append((sources[half:] + 2 * inner) % devices)
    else:
        assert outer <= 3
    return jnp.concatenate(parts, axis=0), jnp.concatenate(origins)


def summed_over(partial, axis):
    devices = lax.axis_size(axis)
    total = partial
    step = 1
    while step < devices:
        sent = total.astype(jnp.bfloat16)
        got = lax.ppermute(sent, axis, [(i, i ^ step) for i in range(devices)])
        total = sent.astype(jnp.float32) + got.astype(jnp.float32)
        step *= 2
    return total


def forward_kernel(
    shards_ref, q_ref, k_ref, v_ref, g_ref, key_code_ref, own_code_ref,
    att_ref, log_ref, delta_ref, gq_ref, gk_ref, gv_ref,
):
    rows = q_ref.shape[0]
    block_rows = rows // BLOCKS_PER_STEP
    step = pl.program_id(0)
    first = step * BLOCKS_PER_STEP
    row = lax.broadcasted_iota(jnp.int32, (rows, 1), 0)
    q_ids = row % block_rows
    for t in range(BLOCKS_PER_STEP):
        q_ids = q_ids + jnp.where(row // block_rows == t, shards_ref[first + t] * block_rows, 0)
    scale = 1.0 / math.sqrt(HD)
    by_rows = (((1,), (1,)), ((), ()))
    by_cols = (((0,), (0,)), ((), ()))
    queries = q_ref[...]
    grads = g_ref[...]
    scores = lax.dot_general(queries, k_ref[...], by_rows, preferred_element_type=jnp.float32) * scale
    scores = jnp.where(key_code_ref[...] <= q_ids, scores, masked_score)
    row_max = jnp.max(scores, axis=1, keepdims=True)
    softmax_part = jnp.exp(scores - row_max)
    row_sum = jnp.sum(softmax_part, axis=1, keepdims=True)
    product = jnp.dot(
        softmax_part.astype(jnp.bfloat16), v_ref[...], preferred_element_type=jnp.float32
    )
    attention = (product / row_sum).astype(jnp.bfloat16)
    log_total = row_max + jnp.log(row_sum)
    delta = jnp.sum(grads.astype(jnp.float32) * attention.astype(jnp.float32), axis=1, keepdims=True)
    att_ref[...] = attention
    log_ref[...] = log_total
    delta_ref[...] = delta

    own = block_rows

    @pl.when(step == 0)
    def _():
        probs = jnp.exp(scores[:own] - log_total[:own])
        grad_probs = lax.dot_general(
            grads[:own], v_ref[...], by_rows, preferred_element_type=jnp.float32
        )
        grad_scores = (probs * (grad_probs - delta[:own])).astype(jnp.bfloat16)
        gq_ref[...] = jnp.dot(grad_scores, k_ref[...], preferred_element_type=jnp.float32)
        gk_ref[...] = jnp.zeros_like(gk_ref)
        gv_ref[...] = jnp.zeros_like(gv_ref)

    own_scores = lax.dot_general(
        queries, k_ref[:own], by_rows, preferred_element_type=jnp.float32
    ) * scale
    own_scores = jnp.where(own_code_ref[...] <= q_ids, own_scores, masked_score)
    probs = jnp.exp(own_scores - log_total)
    gv_ref[...] += lax.dot_general(
        probs.astype(jnp.bfloat16), grads, by_cols, preferred_element_type=jnp.float32
    )
    grad_probs = lax.dot_general(grads, v_ref[:own], by_rows, preferred_element_type=jnp.float32)
    grad_scores = (probs * (grad_probs - delta)).astype(jnp.bfloat16)
    gk_ref[...] += lax.dot_general(grad_scores, queries, by_cols, preferred_element_type=jnp.float32)


def attention_all(queries, keys, values, grads, key_code, held_shards, own_rows):
    slots, width = queries.shape
    row_spec = pl.BlockSpec((QBLOCK, width), lambda i, shards: (i, 0))
    full_spec = pl.BlockSpec((slots, width), lambda i, shards: (0, 0))
    col_spec = pl.BlockSpec((QBLOCK, 1), lambda i, shards: (i, 0))
    own_spec = pl.BlockSpec((own_rows, width), lambda i, shards: (0, 0))
    grid_spec = pltpu.PrefetchScalarGridSpec(
        num_scalar_prefetch=1,
        grid=(slots // QBLOCK,),
        in_specs=[row_spec, full_spec, full_spec, row_spec,
                  pl.BlockSpec((1, slots), lambda i, shards: (0, 0)),
                  pl.BlockSpec((1, own_rows), lambda i, shards: (0, 0))],
        out_specs=[row_spec, col_spec, col_spec, own_spec, own_spec, own_spec],
    )
    own_grad = jax.ShapeDtypeStruct((own_rows, width), jnp.float32)
    return pl.pallas_call(
        forward_kernel,
        grid_spec=grid_spec,
        out_shape=[
            jax.ShapeDtypeStruct((slots, width), jnp.bfloat16),
            jax.ShapeDtypeStruct((slots, 1), jnp.float32),
            jax.ShapeDtypeStruct((slots, 1), jnp.float32),
            own_grad, own_grad, own_grad,
        ],
    )(held_shards, queries, keys, values, grads, key_code.reshape(1, slots),
      key_code[:own_rows].reshape(1, own_rows))


def per_device(
    byte_states,
    conv_kernel,
    mix_weight,
    norm_gain,
    query_weight,
    key_weight,
    value_weight,
    boundaries,
    span_counts,
    grad_attended,
):
    row_count = byte_states.shape[0]
    slot_count = boundaries.shape[0]
    head_width = query_weight.shape[1]
    score_scale = 1.0 / math.sqrt(HD)
    shard_index = lax.axis_index("seq")
    shards = lax.axis_size("seq")
    first_slot = shard_index * slot_count
    own_ids = first_slot + jnp.arange(slot_count, dtype=jnp.int32)
    before_rim = neighbour(byte_states[row_count - (KCONV - 1) :].astype(jnp.float32), 1)
    extended = jnp.concatenate([before_rim.astype(jnp.bfloat16), byte_states], axis=0)
    tap_rows = (boundaries[None, :] + jnp.arange(KCONV - 1, -1, -1, dtype=jnp.int32)[:, None])
    tapped = jnp.take(extended, tap_rows.reshape(-1), axis=0).astype(jnp.float32)
    tapped = tapped.reshape(KCONV, slot_count, D)
    span_depth = conv_kernel[0] * tapped[0]
    for offset in range(1, KCONV):
        span_depth = span_depth + conv_kernel[offset] * tapped[offset]
    span_depth = span_depth.astype(jnp.bfloat16)
    span_bytes = tapped[0]
    live_mask = jnp.arange(slot_count, dtype=jnp.int32) < span_counts[0]
    span_state = span_bytes + jnp.dot(span_depth, mix_weight, preferred_element_type=jnp.float32)
    inverse_rms = lax.rsqrt(jnp.mean(span_state * span_state, axis=1) + 1e-05)
    normed = (span_state * inverse_rms[:, None] * norm_gain).astype(jnp.bfloat16)
    queries = jnp.dot(normed, query_weight, preferred_element_type=jnp.float32).astype(jnp.bfloat16)
    key_rows = jnp.dot(normed, key_weight, preferred_element_type=jnp.float32).astype(jnp.bfloat16)
    value_rows = jnp.dot(normed, value_weight, preferred_element_type=jnp.float32).astype(
        jnp.bfloat16
    )
    grad_rows = jnp.where(live_mask[:, None], grad_attended, jnp.zeros_like(grad_attended))

    count_rows = jnp.broadcast_to(span_counts[0].astype(jnp.bfloat16), (16, head_width))
    packed = jnp.concatenate([queries, key_rows, value_rows, grad_rows, count_rows], axis=0)
    gathered, held_shards = gather_blocks(packed, "seq", 8 if shards == 32 else shards)
    total_slots = shards * slot_count

    def piece(k):
        return gathered[:, k * slot_count : (k + 1) * slot_count].reshape(total_slots, head_width)

    all_queries, all_keys, all_values, all_grads = piece(0), piece(1), piece(2), piece(3)
    all_counts = gathered[:, 4 * slot_count, 0].astype(jnp.int32)
    all_live = (
        jnp.arange(slot_count, dtype=jnp.int32)[None, :] < all_counts[:, None]
    ).reshape(total_slots)
    slot_ids = (
        held_shards[:, None] * slot_count + jnp.arange(slot_count, dtype=jnp.int32)[None, :]
    ).reshape(total_slots)

    all_attended, _, _, query_grad, key_grad, value_grad = attention_all(
        all_queries, all_keys, all_values, all_grads,
        jnp.where(all_live, slot_ids, total_slots), held_shards, slot_count,
    )
    attended = jnp.where(live_mask[:, None], all_attended[:slot_count], jnp.bfloat16(0.0))
    query_grad_rows = (query_grad * score_scale).astype(jnp.bfloat16)
    key_grad_rows = (key_grad * score_scale).astype(jnp.bfloat16)
    value_grad_rows = value_grad.astype(jnp.bfloat16)

    contract = (((1,), (1,)), ((), ()))
    partial_normed = lax.dot_general(
        query_grad_rows, query_weight, contract, preferred_element_type=jnp.float32
    )
    partial_normed = partial_normed + lax.dot_general(
        key_grad_rows, key_weight, contract, preferred_element_type=jnp.float32
    )
    partial_normed = partial_normed + lax.dot_general(
        value_grad_rows, value_weight, contract, preferred_element_type=jnp.float32
    )
    grad_normed = summed_over(partial_normed, "head")
    scaled_grad = norm_gain * grad_normed
    cubed = inverse_rms * inverse_rms * inverse_rms
    grad_state = (
        inverse_rms[:, None] * scaled_grad
        - span_state * cubed[:, None] * jnp.mean(scaled_grad * span_state, axis=1)[:, None]
    )
    grad_state = jnp.where(live_mask[:, None], grad_state, jnp.float32(0.0))
    mixed_grad = lax.dot_general(
        grad_state.astype(jnp.bfloat16), mix_weight, contract, preferred_element_type=jnp.float32
    )
    mixed_grad = mixed_grad.astype(jnp.float32)
    contributions = jnp.concatenate(
        [grad_state + conv_kernel[0] * mixed_grad]
        + [conv_kernel[offset] * mixed_grad for offset in range(1, KCONV)],
        axis=0,
    )
    target_rows = (
        boundaries[None, :] - jnp.arange(KCONV, dtype=jnp.int32)[:, None]
    ).reshape(KCONV * slot_count)
    exact = lax.Precision.HIGHEST
    rim_rows = jnp.arange(-(KCONV - 1), 0, dtype=jnp.int32)
    rim_pick = (rim_rows[:, None] == target_rows[None, :]).astype(jnp.float32)
    before_rows = jnp.dot(rim_pick, contributions, precision=exact)
    after_rim = neighbour(before_rows, -1)
    row_pick = (
        jnp.arange(row_count, dtype=jnp.int32)[:, None] == target_rows[None, :]
    ).astype(jnp.float32)
    local_grad = jnp.dot(row_pick, contributions, precision=exact)
    tail = jnp.concatenate(
        [jnp.zeros((row_count - (KCONV - 1), D), jnp.float32), after_rim], axis=0
    )
    grad_bytes = (local_grad + tail).astype(jnp.bfloat16)
    return (attended, grad_bytes)


def solution(mesh):
    return jax.shard_map(
        per_device,
        mesh=mesh,
        in_specs=(
            P(("doc", "seq"), None),
            P(),
            P(),
            P(),
            P(None, "head"),
            P(None, "head"),
            P(None, "head"),
            P(("doc", "seq")),
            P(("doc", "seq")),
            P(("doc", "seq"), "head"),
        ),
        out_specs=(P(("doc", "seq"), "head"), P(("doc", "seq"), None)),
        check_vma=False,
    )
```

```python
import math

import jax
import jax.numpy as jnp
from jax import lax
from jax.experimental import pallas as pl
from jax.experimental.pallas import tpu as pltpu
from jax.sharding import PartitionSpec as P

D = 1024
HD = 128
KCONV = 4
QBLOCK = 512
BLOCKS_PER_STEP = 8


masked_score = -1e30


def passed_along(array, axis, by):
    devices = lax.axis_size(axis)
    pairs = [(i, i + by) for i in range(devices) if 0 <= i + by < devices]
    return lax.ppermute(array, axis, pairs)


def neighbour(rim_rows, offset_by):
    return passed_along(rim_rows, "seq", offset_by)


def gather_blocks(block, axis, inner):
    devices = lax.axis_size(axis)
    me = lax.axis_index(axis)
    held = block[None]
    step = 1
    while step < inner:
        other = lax.ppermute(held, axis, [(i, i ^ step) for i in range(devices)])
        held = jnp.concatenate([held, other], axis=0)
        step *= 2
    sources = jnp.arange(inner, dtype=jnp.int32) ^ me
    outer = devices // inner
    if outer == 1:
        return held, sources

    def shifted(array, by):
        return lax.ppermute(array, axis, [(i, (i + by) % devices) for i in range(devices)])

    parts = [held]
    origins = [sources]
    from_below = shifted(held, inner)
    from_above = shifted(held, -inner) if outer > 2 else None
    parts.append(from_below)
    origins.append((sources - inner) % devices)
    if outer > 2:
        parts.append(from_above)
        origins.append((sources + inner) % devices)
    if outer == 4:
        half = inner // 2
        parts.append(shifted(from_below[:half], inner))
        origins.append((sources[:half] - 2 * inner) % devices)
        parts.append(shifted(from_above[half:], -inner))
        origins.append((sources[half:] + 2 * inner) % devices)
    else:
        assert outer <= 3
    return jnp.concatenate(parts, axis=0), jnp.concatenate(origins)


def summed_over(partial, axis):
    devices = lax.axis_size(axis)
    total = partial
    step = 1
    while step < devices:
        sent = total.astype(jnp.bfloat16)
        got = lax.ppermute(sent, axis, [(i, i ^ step) for i in range(devices)])
        total = sent.astype(jnp.float32) + got.astype(jnp.float32)
        step *= 2
    return total


def forward_kernel(
    shards_ref, q_ref, k_ref, v_ref, g_ref, key_code_ref, own_code_ref,
    att_ref, log_ref, delta_ref, gq_ref, gk_ref, gv_ref,
):
    rows = q_ref.shape[0]
    block_rows = rows // BLOCKS_PER_STEP
    step = pl.program_id(0)
    first = step * BLOCKS_PER_STEP
    row = lax.broadcasted_iota(jnp.int32, (rows, 1), 0)
    q_ids = row % block_rows
    for t in range(BLOCKS_PER_STEP):
        q_ids = q_ids + jnp.where(row // block_rows == t, shards_ref[first + t] * block_rows, 0)
    scale = 1.0 / math.sqrt(HD)
    by_rows = (((1,), (1,)), ((), ()))
    by_cols = (((0,), (0,)), ((), ()))
    queries = q_ref[...]
    grads = g_ref[...]
    scores = lax.dot_general(queries, k_ref[...], by_rows, preferred_element_type=jnp.float32) * scale
    scores = jnp.where(key_code_ref[...] <= q_ids, scores, masked_score)
    row_max = jnp.max(scores, axis=1, keepdims=True)
    softmax_part = jnp.exp(scores - row_max)
    row_sum = jnp.sum(softmax_part, axis=1, keepdims=True)
    product = jnp.dot(
        softmax_part.astype(jnp.bfloat16), v_ref[...], preferred_element_type=jnp.float32
    )
    attention = (product / row_sum).astype(jnp.bfloat16)
    log_total = row_max + jnp.log(row_sum)
    delta = jnp.sum(grads.astype(jnp.float32) * attention.astype(jnp.float32), axis=1, keepdims=True)
    att_ref[...] = attention
    log_ref[...] = log_total
    delta_ref[...] = delta

    own = block_rows

    @pl.when(step == 0)
    def _():
        probs = jnp.exp(scores[:own] - log_total[:own])
        grad_probs = lax.dot_general(
            grads[:own], v_ref[...], by_rows, preferred_element_type=jnp.float32
        )
        grad_scores = (probs * (grad_probs - delta[:own])).astype(jnp.bfloat16)
        gq_ref[...] = jnp.dot(grad_scores, k_ref[...], preferred_element_type=jnp.float32)
        gk_ref[...] = jnp.zeros_like(gk_ref)
        gv_ref[...] = jnp.zeros_like(gv_ref)

    own_scores = lax.dot_general(
        queries, k_ref[:own], by_rows, preferred_element_type=jnp.float32
    ) * scale
    own_scores = jnp.where(own_code_ref[...] <= q_ids, own_scores, masked_score)
    probs = jnp.exp(own_scores - log_total)
    gv_ref[...] += lax.dot_general(
        probs.astype(jnp.bfloat16), grads, by_cols, preferred_element_type=jnp.float32
    )
    grad_probs = lax.dot_general(grads, v_ref[:own], by_rows, preferred_element_type=jnp.float32)
    grad_scores = (probs * (grad_probs - delta)).astype(jnp.bfloat16)
    gk_ref[...] += lax.dot_general(grad_scores, queries, by_cols, preferred_element_type=jnp.float32)


def attention_all(queries, keys, values, grads, key_code, held_shards, own_rows):
    slots, width = queries.shape
    row_spec = pl.BlockSpec((QBLOCK, width), lambda i, shards: (i, 0))
    full_spec = pl.BlockSpec((slots, width), lambda i, shards: (0, 0))
    col_spec = pl.BlockSpec((QBLOCK, 1), lambda i, shards: (i, 0))
    own_spec = pl.BlockSpec((own_rows, width), lambda i, shards: (0, 0))
    grid_spec = pltpu.PrefetchScalarGridSpec(
        num_scalar_prefetch=1,
        grid=(slots // QBLOCK,),
        in_specs=[row_spec, full_spec, full_spec, row_spec,
                  pl.BlockSpec((1, slots), lambda i, shards: (0, 0)),
                  pl.BlockSpec((1, own_rows), lambda i, shards: (0, 0))],
        out_specs=[row_spec, col_spec, col_spec, own_spec, own_spec, own_spec],
    )
    own_grad = jax.ShapeDtypeStruct((own_rows, width), jnp.float32)
    return pl.pallas_call(
        forward_kernel,
        grid_spec=grid_spec,
        out_shape=[
            jax.ShapeDtypeStruct((slots, width), jnp.bfloat16),
            jax.ShapeDtypeStruct((slots, 1), jnp.float32),
            jax.ShapeDtypeStruct((slots, 1), jnp.float32),
            own_grad, own_grad, own_grad,
        ],
    )(held_shards, queries, keys, values, grads, key_code.reshape(1, slots),
      key_code[:own_rows].reshape(1, own_rows))


def per_device(
    byte_states,
    conv_kernel,
    mix_weight,
    norm_gain,
    query_weight,
    key_weight,
    value_weight,
    boundaries,
    span_counts,
    grad_attended,
):
    row_count = byte_states.shape[0]
    slot_count = boundaries.shape[0]
    head_width = query_weight.shape[1]
    score_scale = 1.0 / math.sqrt(HD)
    shard_index = lax.axis_index("seq")
    shards = lax.axis_size("seq")
    first_slot = shard_index * slot_count
    own_ids = first_slot + jnp.arange(slot_count, dtype=jnp.int32)
    before_rim = neighbour(byte_states[row_count - (KCONV - 1) :].astype(jnp.float32), 1)
    extended = jnp.concatenate([before_rim.astype(jnp.bfloat16), byte_states], axis=0)
    tap_rows = (boundaries[None, :] + jnp.arange(KCONV - 1, -1, -1, dtype=jnp.int32)[:, None])
    tapped = jnp.take(extended, tap_rows.reshape(-1), axis=0).astype(jnp.float32)
    tapped = tapped.reshape(KCONV, slot_count, D)
    span_depth = conv_kernel[0] * tapped[0]
    for offset in range(1, KCONV):
        span_depth = span_depth + conv_kernel[offset] * tapped[offset]
    span_depth = span_depth.astype(jnp.bfloat16)
    span_bytes = tapped[0]
    live_mask = jnp.arange(slot_count, dtype=jnp.int32) < span_counts[0]
    span_state = span_bytes + jnp.dot(span_depth, mix_weight, preferred_element_type=jnp.float32)
    inverse_rms = lax.rsqrt(jnp.mean(span_state * span_state, axis=1) + 1e-05)
    normed = (span_state * inverse_rms[:, None] * norm_gain).astype(jnp.bfloat16)
    queries = jnp.dot(normed, query_weight, preferred_element_type=jnp.float32).astype(jnp.bfloat16)
    key_rows = jnp.dot(normed, key_weight, preferred_element_type=jnp.float32).astype(jnp.bfloat16)
    value_rows = jnp.dot(normed, value_weight, preferred_element_type=jnp.float32).astype(
        jnp.bfloat16
    )
    grad_rows = jnp.where(live_mask[:, None], grad_attended, jnp.zeros_like(grad_attended))

    count_rows = jnp.broadcast_to(span_counts[0].astype(jnp.bfloat16), (16, head_width))
    packed = jnp.concatenate([queries, key_rows, value_rows, grad_rows, count_rows], axis=0)
    gathered, held_shards = gather_blocks(packed, "seq", 8 if shards == 32 else shards)
    total_slots = shards * slot_count

    def piece(k):
        return gathered[:, k * slot_count : (k + 1) * slot_count].reshape(total_slots, head_width)

    all_queries, all_keys, all_values, all_grads = piece(0), piece(1), piece(2), piece(3)
    all_counts = gathered[:, 4 * slot_count, 0].astype(jnp.int32)
    all_live = (
        jnp.arange(slot_count, dtype=jnp.int32)[None, :] < all_counts[:, None]
    ).reshape(total_slots)
    slot_ids = (
        held_shards[:, None] * slot_count + jnp.arange(slot_count, dtype=jnp.int32)[None, :]
    ).reshape(total_slots)

    all_attended, _, _, query_grad, key_grad, value_grad = attention_all(
        all_queries, all_keys, all_values, all_grads,
        jnp.where(all_live, slot_ids, total_slots), held_shards, slot_count,
    )
    attended = jnp.where(live_mask[:, None], all_attended[:slot_count], jnp.bfloat16(0.0))
    query_grad_rows = (query_grad * score_scale).astype(jnp.bfloat16)
    key_grad_rows = (key_grad * score_scale).astype(jnp.bfloat16)
    value_grad_rows = value_grad.astype(jnp.bfloat16)

    contract = (((1,), (1,)), ((), ()))
    partial_normed = lax.dot_general(
        query_grad_rows, query_weight, contract, preferred_element_type=jnp.float32
    )
    partial_normed = partial_normed + lax.dot_general(
        key_grad_rows, key_weight, contract, preferred_element_type=jnp.float32
    )
    partial_normed = partial_normed + lax.dot_general(
        value_grad_rows, value_weight, contract, preferred_element_type=jnp.float32
    )
    grad_normed = summed_over(partial_normed, "head")
    scaled_grad = norm_gain * grad_normed
    cubed = inverse_rms * inverse_rms * inverse_rms
    grad_state = (
        inverse_rms[:, None] * scaled_grad
        - span_state * cubed[:, None] * jnp.mean(scaled_grad * span_state, axis=1)[:, None]
    )
    grad_state = jnp.where(live_mask[:, None], grad_state, jnp.float32(0.0))
    mixed_grad = lax.dot_general(
        grad_state.astype(jnp.bfloat16), mix_weight, contract, preferred_element_type=jnp.float32
    )
    mixed_grad = mixed_grad.astype(jnp.float32)
    contributions = jnp.concatenate(
        [grad_state + conv_kernel[0] * mixed_grad]
        + [conv_kernel[offset] * mixed_grad for offset in range(1, KCONV)],
        axis=0,
    )
    target_rows = (
        boundaries[None, :] - jnp.arange(KCONV, dtype=jnp.int32)[:, None]
    ).reshape(KCONV * slot_count)
    exact = lax.Precision.HIGHEST
    rim_rows = jnp.arange(-(KCONV - 1), 0, dtype=jnp.int32)
    rim_pick = (rim_rows[:, None] == target_rows[None, :]).astype(jnp.float32)
    before_rows = jnp.dot(rim_pick, contributions, precision=exact)
    after_rim = neighbour(before_rows, -1)
    row_pick = (
        jnp.arange(row_count, dtype=jnp.int32)[:, None] == target_rows[None, :]
    ).astype(jnp.float32)
    local_grad = jnp.dot(row_pick, contributions, precision=exact)
    tail = jnp.concatenate(
        [jnp.zeros((row_count - (KCONV - 1), D), jnp.float32), after_rim], axis=0
    )
    grad_bytes = (local_grad + tail).astype(jnp.bfloat16)
    return (attended, grad_bytes)


def solution(mesh):
    return jax.shard_map(
        per_device,
        mesh=mesh,
        in_specs=(
            P(("doc", "seq"), None),
            P(),
            P(),
            P(),
            P(None, "head"),
            P(None, "head"),
            P(None, "head"),
            P(("doc", "seq")),
            P(("doc", "seq")),
            P(("doc", "seq"), "head"),
        ),
        out_specs=(P(("doc", "seq"), "head"), P(("doc", "seq"), None)),
        check_vma=False,
    )
```

```python
import math

import jax
import jax.numpy as jnp
from jax import lax
from jax.experimental import pallas as pl
from jax.experimental.pallas import tpu as pltpu
from jax.sharding import PartitionSpec as P

D = 1024
HD = 128
KCONV = 4
QBLOCK = 256
BLOCKS_PER_STEP = 4


masked_score = -1e30


def passed_along(array, axis, by):
    devices = lax.axis_size(axis)
    pairs = [(i, i + by) for i in range(devices) if 0 <= i + by < devices]
    return lax.ppermute(array, axis, pairs)


def neighbour(rim_rows, offset_by):
    return passed_along(rim_rows, "seq", offset_by)


def gather_blocks(block, axis, inner):
    devices = lax.axis_size(axis)
    me = lax.axis_index(axis)
    held = block[None]
    step = 1
    while step < inner:
        other = lax.ppermute(held, axis, [(i, i ^ step) for i in range(devices)])
        held = jnp.concatenate([held, other], axis=0)
        step *= 2
    sources = jnp.arange(inner, dtype=jnp.int32) ^ me
    outer = devices // inner
    if outer == 1:
        return held, sources

    def shifted(array, by):
        return lax.ppermute(array, axis, [(i, (i + by) % devices) for i in range(devices)])

    parts = [held]
    origins = [sources]
    from_below = shifted(held, inner)
    from_above = shifted(held, -inner) if outer > 2 else None
    parts.append(from_below)
    origins.append((sources - inner) % devices)
    if outer > 2:
        parts.append(from_above)
        origins.append((sources + inner) % devices)
    if outer == 4:
        half = inner // 2
        parts.append(shifted(from_below[:half], inner))
        origins.append((sources[:half] - 2 * inner) % devices)
        parts.append(shifted(from_above[half:], -inner))
        origins.append((sources[half:] + 2 * inner) % devices)
    else:
        assert outer <= 3
    return jnp.concatenate(parts, axis=0), jnp.concatenate(origins)


def summed_over(partial, axis):
    devices = lax.axis_size(axis)
    total = partial
    step = 1
    while step < devices:
        sent = total.astype(jnp.bfloat16)
        got = lax.ppermute(sent, axis, [(i, i ^ step) for i in range(devices)])
        total = sent.astype(jnp.float32) + got.astype(jnp.float32)
        step *= 2
    return total


def forward_kernel(
    shards_ref, q_ref, k_ref, v_ref, g_ref, key_code_ref, own_code_ref,
    att_ref, log_ref, delta_ref, gq_ref, gk_ref, gv_ref,
):
    rows = q_ref.shape[0]
    block_rows = rows // BLOCKS_PER_STEP
    step = pl.program_id(0)
    first = step * BLOCKS_PER_STEP
    row = lax.broadcasted_iota(jnp.int32, (rows, 1), 0)
    q_ids = row % block_rows
    for t in range(BLOCKS_PER_STEP):
        q_ids = q_ids + jnp.where(row // block_rows == t, shards_ref[first + t] * block_rows, 0)
    scale = 1.0 / math.sqrt(HD)
    by_rows = (((1,), (1,)), ((), ()))
    by_cols = (((0,), (0,)), ((), ()))
    queries = q_ref[...]
    grads = g_ref[...]
    scores = lax.dot_general(queries, k_ref[...], by_rows, preferred_element_type=jnp.float32) * scale
    scores = jnp.where(key_code_ref[...] <= q_ids, scores, masked_score)
    row_max = jnp.max(scores, axis=1, keepdims=True)
    softmax_part = jnp.exp(scores - row_max)
    row_sum = jnp.sum(softmax_part, axis=1, keepdims=True)
    product = jnp.dot(
        softmax_part.astype(jnp.bfloat16), v_ref[...], preferred_element_type=jnp.float32
    )
    attention = (product / row_sum).astype(jnp.bfloat16)
    log_total = row_max + jnp.log(row_sum)
    delta = jnp.sum(grads.astype(jnp.float32) * attention.astype(jnp.float32), axis=1, keepdims=True)
    att_ref[...] = attention
    log_ref[...] = log_total
    delta_ref[...] = delta

    own = block_rows

    @pl.when(step == 0)
    def _():
        probs = jnp.exp(scores[:own] - log_total[:own])
        grad_probs = lax.dot_general(
            grads[:own], v_ref[...], by_rows, preferred_element_type=jnp.float32
        )
        grad_scores = (probs * (grad_probs - delta[:own])).astype(jnp.bfloat16)
        gq_ref[...] = jnp.dot(grad_scores, k_ref[...], preferred_element_type=jnp.float32)
        gk_ref[...] = jnp.zeros_like(gk_ref)
        gv_ref[...] = jnp.zeros_like(gv_ref)

    own_scores = lax.dot_general(
        queries, k_ref[:own], by_rows, preferred_element_type=jnp.float32
    ) * scale
    own_scores = jnp.where(own_code_ref[...] <= q_ids, own_scores, masked_score)
    probs = jnp.exp(own_scores - log_total)
    gv_ref[...] += lax.dot_general(
        probs.astype(jnp.bfloat16), grads, by_cols, preferred_element_type=jnp.float32
    )
    grad_probs = lax.dot_general(grads, v_ref[:own], by_rows, preferred_element_type=jnp.float32)
    grad_scores = (probs * (grad_probs - delta)).astype(jnp.bfloat16)
    gk_ref[...] += lax.dot_general(grad_scores, queries, by_cols, preferred_element_type=jnp.float32)


def attention_all(queries, keys, values, grads, key_code, held_shards, own_rows):
    slots, width = queries.shape
    row_spec = pl.BlockSpec((QBLOCK, width), lambda i, shards: (i, 0))
    full_spec = pl.BlockSpec((slots, width), lambda i, shards: (0, 0))
    col_spec = pl.BlockSpec((QBLOCK, 1), lambda i, shards: (i, 0))
    own_spec = pl.BlockSpec((own_rows, width), lambda i, shards: (0, 0))
    grid_spec = pltpu.PrefetchScalarGridSpec(
        num_scalar_prefetch=1,
        grid=(slots // QBLOCK,),
        in_specs=[row_spec, full_spec, full_spec, row_spec,
                  pl.BlockSpec((1, slots), lambda i, shards: (0, 0)),
                  pl.BlockSpec((1, own_rows), lambda i, shards: (0, 0))],
        out_specs=[row_spec, col_spec, col_spec, own_spec, own_spec, own_spec],
    )
    own_grad = jax.ShapeDtypeStruct((own_rows, width), jnp.float32)
    return pl.pallas_call(
        forward_kernel,
        grid_spec=grid_spec,
        out_shape=[
            jax.ShapeDtypeStruct((slots, width), jnp.bfloat16),
            jax.ShapeDtypeStruct((slots, 1), jnp.float32),
            jax.ShapeDtypeStruct((slots, 1), jnp.float32),
            own_grad, own_grad, own_grad,
        ],
    )(held_shards, queries, keys, values, grads, key_code.reshape(1, slots),
      key_code[:own_rows].reshape(1, own_rows))


def per_device(
    byte_states,
    conv_kernel,
    mix_weight,
    norm_gain,
    query_weight,
    key_weight,
    value_weight,
    boundaries,
    span_counts,
    grad_attended,
):
    row_count = byte_states.shape[0]
    slot_count = boundaries.shape[0]
    head_width = query_weight.shape[1]
    score_scale = 1.0 / math.sqrt(HD)
    shard_index = lax.axis_index("seq")
    shards = lax.axis_size("seq")
    first_slot = shard_index * slot_count
    own_ids = first_slot + jnp.arange(slot_count, dtype=jnp.int32)
    before_rim = neighbour(byte_states[row_count - (KCONV - 1) :].astype(jnp.float32), 1)
    extended = jnp.concatenate([before_rim.astype(jnp.bfloat16), byte_states], axis=0)
    tap_rows = (boundaries[None, :] + jnp.arange(KCONV - 1, -1, -1, dtype=jnp.int32)[:, None])
    tapped = jnp.take(extended, tap_rows.reshape(-1), axis=0).astype(jnp.float32)
    tapped = tapped.reshape(KCONV, slot_count, D)
    span_depth = conv_kernel[0] * tapped[0]
    for offset in range(1, KCONV):
        span_depth = span_depth + conv_kernel[offset] * tapped[offset]
    span_depth = span_depth.astype(jnp.bfloat16)
    span_bytes = tapped[0]
    live_mask = jnp.arange(slot_count, dtype=jnp.int32) < span_counts[0]
    span_state = span_bytes + jnp.dot(span_depth, mix_weight, preferred_element_type=jnp.float32)
    inverse_rms = lax.rsqrt(jnp.mean(span_state * span_state, axis=1) + 1e-05)
    normed = (span_state * inverse_rms[:, None] * norm_gain).astype(jnp.bfloat16)
    queries = jnp.dot(normed, query_weight, preferred_element_type=jnp.float32).astype(jnp.bfloat16)
    key_rows = jnp.dot(normed, key_weight, preferred_element_type=jnp.float32).astype(jnp.bfloat16)
    value_rows = jnp.dot(normed, value_weight, preferred_element_type=jnp.float32).astype(
        jnp.bfloat16
    )
    grad_rows = jnp.where(live_mask[:, None], grad_attended, jnp.zeros_like(grad_attended))

    count_rows = jnp.broadcast_to(span_counts[0].astype(jnp.bfloat16), (16, head_width))
    packed = jnp.concatenate([queries, key_rows, value_rows, grad_rows, count_rows], axis=0)
    gathered, held_shards = gather_blocks(packed, "seq", 8 if shards == 32 else shards)
    total_slots = shards * slot_count

    def piece(k):
        return gathered[:, k * slot_count : (k + 1) * slot_count].reshape(total_slots, head_width)

    all_queries, all_keys, all_values, all_grads = piece(0), piece(1), piece(2), piece(3)
    all_counts = gathered[:, 4 * slot_count, 0].astype(jnp.int32)
    all_live = (
        jnp.arange(slot_count, dtype=jnp.int32)[None, :] < all_counts[:, None]
    ).reshape(total_slots)
    slot_ids = (
        held_shards[:, None] * slot_count + jnp.arange(slot_count, dtype=jnp.int32)[None, :]
    ).reshape(total_slots)

    all_attended, _, _, query_grad, key_grad, value_grad = attention_all(
        all_queries, all_keys, all_values, all_grads,
        jnp.where(all_live, slot_ids, total_slots), held_shards, slot_count,
    )
    attended = jnp.where(live_mask[:, None], all_attended[:slot_count], jnp.bfloat16(0.0))
    query_grad_rows = (query_grad * score_scale).astype(jnp.bfloat16)
    key_grad_rows = (key_grad * score_scale).astype(jnp.bfloat16)
    value_grad_rows = value_grad.astype(jnp.bfloat16)

    contract = (((1,), (1,)), ((), ()))
    partial_normed = lax.dot_general(
        jnp.concatenate([query_grad_rows, key_grad_rows, value_grad_rows], axis=1),
        jnp.concatenate([query_weight, key_weight, value_weight], axis=1),
        contract,
        preferred_element_type=jnp.float32,
    )
    grad_normed = summed_over(partial_normed, "head")
    scaled_grad = norm_gain * grad_normed
    cubed = inverse_rms * inverse_rms * inverse_rms
    grad_state = (
        inverse_rms[:, None] * scaled_grad
        - span_state * cubed[:, None] * jnp.mean(scaled_grad * span_state, axis=1)[:, None]
    )
    grad_state = jnp.where(live_mask[:, None], grad_state, jnp.float32(0.0))
    mixed_grad = lax.dot_general(
        grad_state.astype(jnp.bfloat16), mix_weight, contract, preferred_element_type=jnp.float32
    )
    mixed_grad = mixed_grad.astype(jnp.float32)
    contributions = jnp.concatenate(
        [grad_state + conv_kernel[0] * mixed_grad]
        + [conv_kernel[offset] * mixed_grad for offset in range(1, KCONV)],
        axis=0,
    )
    target_rows = (
        boundaries[None, :] - jnp.arange(KCONV, dtype=jnp.int32)[:, None]
    ).reshape(KCONV * slot_count)
    exact = lax.Precision.HIGHEST
    rim_rows = jnp.arange(-(KCONV - 1), 0, dtype=jnp.int32)
    rim_pick = (rim_rows[:, None] == target_rows[None, :]).astype(jnp.float32)
    before_rows = jnp.dot(rim_pick, contributions, precision=exact)
    after_rim = neighbour(before_rows, -1)
    row_pick = (
        jnp.arange(row_count, dtype=jnp.int32)[:, None] == target_rows[None, :]
    ).astype(jnp.float32)
    local_grad = lax.optimization_barrier(jnp.dot(row_pick, contributions, precision=exact))
    tail = jnp.concatenate(
        [jnp.zeros((row_count - (KCONV - 1), D), jnp.float32), after_rim], axis=0
    )
    grad_bytes = (local_grad + tail).astype(jnp.bfloat16)
    return (attended, grad_bytes)


def solution(mesh):
    return jax.shard_map(
        per_device,
        mesh=mesh,
        in_specs=(
            P(("doc", "seq"), None),
            P(),
            P(),
            P(),
            P(None, "head"),
            P(None, "head"),
            P(None, "head"),
            P(("doc", "seq")),
            P(("doc", "seq")),
            P(("doc", "seq"), "head"),
        ),
        out_specs=(P(("doc", "seq"), "head"), P(("doc", "seq"), None)),
        check_vma=False,
    )
```

```python
import math

import jax
import jax.numpy as jnp
from jax import lax
from jax.experimental import pallas as pl
from jax.experimental.pallas import tpu as pltpu
from jax.sharding import PartitionSpec as P

D = 1024
HD = 128
KCONV = 4
QBLOCK = 256
BLOCKS_PER_STEP = 4


masked_score = -1e30


def passed_along(array, axis, by):
    devices = lax.axis_size(axis)
    pairs = [(i, i + by) for i in range(devices) if 0 <= i + by < devices]
    return lax.ppermute(array, axis, pairs)


def neighbour(rim_rows, offset_by):
    return passed_along(rim_rows, "seq", offset_by)


def ring_neighbour(index, by, ring, stride):
    place = (index // stride) % ring
    return index + ((place + by) % ring - place) * stride


def ring_phase(held, sources, axis, ring, stride):
    devices = lax.axis_size(axis)

    def shifted(array, by):
        pairs = [(i, ring_neighbour(i, by, ring, stride)) for i in range(devices)]
        return lax.ppermute(array, axis, pairs)

    half = held.shape[0] // 2
    from_below = shifted(held, 1)
    from_above = shifted(held, -1)
    parts = [held, from_below, from_above, shifted(from_below[:half], 1), shifted(from_above[half:], -1)]
    origins = [
        sources,
        ring_neighbour(sources, -1, ring, stride),
        ring_neighbour(sources, 1, ring, stride),
        ring_neighbour(sources[:half], -2, ring, stride),
        ring_neighbour(sources[half:], 2, ring, stride),
    ]
    return jnp.concatenate(parts, axis=0), jnp.concatenate(origins)


def gather_blocks(block, axis):
    devices = lax.axis_size(axis)
    me = lax.axis_index(axis)
    held = block[None]
    sources = me[None]
    if devices == 32:
        other = lax.ppermute(held, axis, [(i, i ^ 1) for i in range(devices)])
        held = jnp.concatenate([held, other], axis=0)
        sources = jnp.concatenate([sources, sources ^ 1])
        held, sources = ring_phase(held, sources, axis, 4, 2)
        return ring_phase(held, sources, axis, 4, 8)
    step = 1
    while step < devices:
        other = lax.ppermute(held, axis, [(i, i ^ step) for i in range(devices)])
        held = jnp.concatenate([held, other], axis=0)
        sources = jnp.concatenate([sources, sources ^ step])
        step *= 2
    return held, sources


def summed_over(partial, axis):
    devices = lax.axis_size(axis)
    total = partial
    step = 1
    while step < devices:
        sent = total.astype(jnp.bfloat16)
        got = lax.ppermute(sent, axis, [(i, i ^ step) for i in range(devices)])
        total = sent.astype(jnp.float32) + got.astype(jnp.float32)
        step *= 2
    return total


def forward_kernel(
    shards_ref, q_ref, k_ref, v_ref, g_ref, key_code_ref, own_code_ref,
    att_ref, log_ref, delta_ref, gq_ref, gk_ref, gv_ref,
):
    rows = q_ref.shape[0]
    block_rows = rows // BLOCKS_PER_STEP
    step = pl.program_id(0)
    first = step * BLOCKS_PER_STEP
    row = lax.broadcasted_iota(jnp.int32, (rows, 1), 0)
    q_ids = row % block_rows
    for t in range(BLOCKS_PER_STEP):
        q_ids = q_ids + jnp.where(row // block_rows == t, shards_ref[first + t] * block_rows, 0)
    scale = 1.0 / math.sqrt(HD)
    by_rows = (((1,), (1,)), ((), ()))
    by_cols = (((0,), (0,)), ((), ()))
    queries = q_ref[...]
    grads = g_ref[...]
    scores = lax.dot_general(queries, k_ref[...], by_rows, preferred_element_type=jnp.float32) * scale
    scores = jnp.where(key_code_ref[...] <= q_ids, scores, masked_score)
    row_max = jnp.max(scores, axis=1, keepdims=True)
    softmax_part = jnp.exp(scores - row_max)
    row_sum = jnp.sum(softmax_part, axis=1, keepdims=True)
    product = jnp.dot(
        softmax_part.astype(jnp.bfloat16), v_ref[...], preferred_element_type=jnp.float32
    )
    attention = (product / row_sum).astype(jnp.bfloat16)
    log_total = row_max + jnp.log(row_sum)
    delta = jnp.sum(grads.astype(jnp.float32) * attention.astype(jnp.float32), axis=1, keepdims=True)
    att_ref[...] = attention
    log_ref[...] = log_total
    delta_ref[...] = delta

    own = block_rows

    @pl.when(step == 0)
    def _():
        probs = jnp.exp(scores[:own] - log_total[:own])
        grad_probs = lax.dot_general(
            grads[:own], v_ref[...], by_rows, preferred_element_type=jnp.float32
        )
        grad_scores = (probs * (grad_probs - delta[:own])).astype(jnp.bfloat16)
        gq_ref[...] = jnp.dot(grad_scores, k_ref[...], preferred_element_type=jnp.float32)
        gk_ref[...] = jnp.zeros_like(gk_ref)
        gv_ref[...] = jnp.zeros_like(gv_ref)

    own_scores = lax.dot_general(
        queries, k_ref[:own], by_rows, preferred_element_type=jnp.float32
    ) * scale
    own_scores = jnp.where(own_code_ref[...] <= q_ids, own_scores, masked_score)
    probs = jnp.exp(own_scores - log_total)
    gv_ref[...] += lax.dot_general(
        probs.astype(jnp.bfloat16), grads, by_cols, preferred_element_type=jnp.float32
    )
    grad_probs = lax.dot_general(grads, v_ref[:own], by_rows, preferred_element_type=jnp.float32)
    grad_scores = (probs * (grad_probs - delta)).astype(jnp.bfloat16)
    gk_ref[...] += lax.dot_general(grad_scores, queries, by_cols, preferred_element_type=jnp.float32)


def attention_all(queries, keys, values, grads, key_code, held_shards, own_rows):
    slots, width = queries.shape
    row_spec = pl.BlockSpec((QBLOCK, width), lambda i, shards: (i, 0))
    full_spec = pl.BlockSpec((slots, width), lambda i, shards: (0, 0))
    col_spec = pl.BlockSpec((QBLOCK, 1), lambda i, shards: (i, 0))
    own_spec = pl.BlockSpec((own_rows, width), lambda i, shards: (0, 0))
    grid_spec = pltpu.PrefetchScalarGridSpec(
        num_scalar_prefetch=1,
        grid=(slots // QBLOCK,),
        in_specs=[row_spec, full_spec, full_spec, row_spec,
                  pl.BlockSpec((1, slots), lambda i, shards: (0, 0)),
                  pl.BlockSpec((1, own_rows), lambda i, shards: (0, 0))],
        out_specs=[row_spec, col_spec, col_spec, own_spec, own_spec, own_spec],
    )
    own_grad = jax.ShapeDtypeStruct((own_rows, width), jnp.float32)
    return pl.pallas_call(
        forward_kernel,
        grid_spec=grid_spec,
        out_shape=[
            jax.ShapeDtypeStruct((slots, width), jnp.bfloat16),
            jax.ShapeDtypeStruct((slots, 1), jnp.float32),
            jax.ShapeDtypeStruct((slots, 1), jnp.float32),
            own_grad, own_grad, own_grad,
        ],
    )(held_shards, queries, keys, values, grads, key_code.reshape(1, slots),
      key_code[:own_rows].reshape(1, own_rows))


def per_device(
    byte_states,
    conv_kernel,
    mix_weight,
    norm_gain,
    query_weight,
    key_weight,
    value_weight,
    boundaries,
    span_counts,
    grad_attended,
):
    row_count = byte_states.shape[0]
    slot_count = boundaries.shape[0]
    head_width = query_weight.shape[1]
    score_scale = 1.0 / math.sqrt(HD)
    shard_index = lax.axis_index("seq")
    shards = lax.axis_size("seq")
    first_slot = shard_index * slot_count
    own_ids = first_slot + jnp.arange(slot_count, dtype=jnp.int32)
    before_rim = neighbour(byte_states[row_count - (KCONV - 1) :].astype(jnp.float32), 1)
    extended = jnp.concatenate([before_rim.astype(jnp.bfloat16), byte_states], axis=0)
    tap_rows = (boundaries[None, :] + jnp.arange(KCONV - 1, -1, -1, dtype=jnp.int32)[:, None])
    tapped = jnp.take(extended, tap_rows.reshape(-1), axis=0).astype(jnp.float32)
    tapped = tapped.reshape(KCONV, slot_count, D)
    span_depth = conv_kernel[0] * tapped[0]
    for offset in range(1, KCONV):
        span_depth = span_depth + conv_kernel[offset] * tapped[offset]
    span_depth = span_depth.astype(jnp.bfloat16)
    span_bytes = tapped[0]
    live_mask = jnp.arange(slot_count, dtype=jnp.int32) < span_counts[0]
    span_state = span_bytes + jnp.dot(span_depth, mix_weight, preferred_element_type=jnp.float32)
    inverse_rms = lax.rsqrt(jnp.mean(span_state * span_state, axis=1) + 1e-05)
    normed = (span_state * inverse_rms[:, None] * norm_gain).astype(jnp.bfloat16)
    queries = jnp.dot(normed, query_weight, preferred_element_type=jnp.float32).astype(jnp.bfloat16)
    key_rows = jnp.dot(normed, key_weight, preferred_element_type=jnp.float32).astype(jnp.bfloat16)
    value_rows = jnp.dot(normed, value_weight, preferred_element_type=jnp.float32).astype(
        jnp.bfloat16
    )
    grad_rows = jnp.where(live_mask[:, None], grad_attended, jnp.zeros_like(grad_attended))

    count_rows = jnp.broadcast_to(span_counts[0].astype(jnp.bfloat16), (16, head_width))
    packed = jnp.concatenate([queries, key_rows, value_rows, grad_rows, count_rows], axis=0)
    gathered, held_shards = gather_blocks(packed, "seq")
    total_slots = shards * slot_count

    def piece(k):
        return gathered[:, k * slot_count : (k + 1) * slot_count].reshape(total_slots, head_width)

    all_queries, all_keys, all_values, all_grads = piece(0), piece(1), piece(2), piece(3)
    all_counts = gathered[:, 4 * slot_count, 0].astype(jnp.int32)
    all_live = (
        jnp.arange(slot_count, dtype=jnp.int32)[None, :] < all_counts[:, None]
    ).reshape(total_slots)
    slot_ids = (
        held_shards[:, None] * slot_count + jnp.arange(slot_count, dtype=jnp.int32)[None, :]
    ).reshape(total_slots)

    all_attended, _, _, query_grad, key_grad, value_grad = attention_all(
        all_queries, all_keys, all_values, all_grads,
        jnp.where(all_live, slot_ids, total_slots), held_shards, slot_count,
    )
    attended = jnp.where(live_mask[:, None], all_attended[:slot_count], jnp.bfloat16(0.0))
    query_grad_rows = (query_grad * score_scale).astype(jnp.bfloat16)
    key_grad_rows = (key_grad * score_scale).astype(jnp.bfloat16)
    value_grad_rows = value_grad.astype(jnp.bfloat16)

    contract = (((1,), (1,)), ((), ()))
    partial_normed = lax.dot_general(
        jnp.concatenate([query_grad_rows, key_grad_rows, value_grad_rows], axis=1),
        jnp.concatenate([query_weight, key_weight, value_weight], axis=1),
        contract,
        preferred_element_type=jnp.float32,
    )
    grad_normed = summed_over(partial_normed, "head")
    scaled_grad = norm_gain * grad_normed
    cubed = inverse_rms * inverse_rms * inverse_rms
    grad_state = (
        inverse_rms[:, None] * scaled_grad
        - span_state * cubed[:, None] * jnp.mean(scaled_grad * span_state, axis=1)[:, None]
    )
    grad_state = jnp.where(live_mask[:, None], grad_state, jnp.float32(0.0))
    mixed_grad = lax.dot_general(
        grad_state.astype(jnp.bfloat16), mix_weight, contract, preferred_element_type=jnp.float32
    )
    mixed_grad = mixed_grad.astype(jnp.float32)
    contributions = jnp.concatenate(
        [grad_state + conv_kernel[0] * mixed_grad]
        + [conv_kernel[offset] * mixed_grad for offset in range(1, KCONV)],
        axis=0,
    )
    target_rows = (
        boundaries[None, :] - jnp.arange(KCONV, dtype=jnp.int32)[:, None]
    ).reshape(KCONV * slot_count)
    exact = lax.Precision.HIGHEST
    rim_rows = jnp.arange(-(KCONV - 1), 0, dtype=jnp.int32)
    rim_pick = (rim_rows[:, None] == target_rows[None, :]).astype(jnp.float32)
    before_rows = jnp.dot(rim_pick, contributions, precision=exact)
    after_rim = neighbour(before_rows, -1)
    row_pick = (
        jnp.arange(row_count, dtype=jnp.int32)[:, None] == target_rows[None, :]
    ).astype(jnp.float32)
    local_grad = lax.optimization_barrier(jnp.dot(row_pick, contributions, precision=exact))
    tail = jnp.concatenate(
        [jnp.zeros((row_count - (KCONV - 1), D), jnp.float32), after_rim], axis=0
    )
    grad_bytes = (local_grad + tail).astype(jnp.bfloat16)
    return (attended, grad_bytes)


def solution(mesh):
    return jax.shard_map(
        per_device,
        mesh=mesh,
        in_specs=(
            P(("doc", "seq"), None),
            P(),
            P(),
            P(),
            P(None, "head"),
            P(None, "head"),
            P(None, "head"),
            P(("doc", "seq")),
            P(("doc", "seq")),
            P(("doc", "seq"), "head"),
        ),
        out_specs=(P(("doc", "seq"), "head"), P(("doc", "seq"), None)),
        check_vma=False,
    )
```

```python
import math

import jax
import jax.numpy as jnp
from jax import lax
from jax.experimental import pallas as pl
from jax.experimental.pallas import tpu as pltpu
from jax.sharding import PartitionSpec as P

D = 1024
HD = 128
KCONV = 4
QBLOCK = 256
BLOCKS_PER_STEP = 4


masked_score = -1e30


def passed_along(array, axis, by):
    devices = lax.axis_size(axis)
    pairs = [(i, i + by) for i in range(devices) if 0 <= i + by < devices]
    return lax.ppermute(array, axis, pairs)


def neighbour(rim_rows, offset_by):
    return passed_along(rim_rows, "seq", offset_by)


def ring_neighbour(index, by, ring, stride):
    place = (index // stride) % ring
    return index + ((place + by) % ring - place) * stride


def ring_phase(held, sources, axis, ring, stride):
    devices = lax.axis_size(axis)

    def shifted(array, by):
        pairs = [(i, ring_neighbour(i, by, ring, stride)) for i in range(devices)]
        return lax.ppermute(array, axis, pairs)

    half = held.shape[0] // 2
    from_below = shifted(held, 1)
    from_above = shifted(held, -1)
    parts = [held, from_below, from_above, shifted(from_below[:half], 1), shifted(from_above[half:], -1)]
    origins = [
        sources,
        ring_neighbour(sources, -1, ring, stride),
        ring_neighbour(sources, 1, ring, stride),
        ring_neighbour(sources[:half], -2, ring, stride),
        ring_neighbour(sources[half:], 2, ring, stride),
    ]
    return jnp.concatenate(parts, axis=0), jnp.concatenate(origins)


def gather_blocks(block, axis):
    devices = lax.axis_size(axis)
    me = lax.axis_index(axis)
    held = block[None]
    sources = me[None]
    if devices == 32:
        other = lax.ppermute(held, axis, [(i, i ^ 1) for i in range(devices)])
        held = jnp.concatenate([held, other], axis=0)
        sources = jnp.concatenate([sources, sources ^ 1])
        held, sources = ring_phase(held, sources, axis, 4, 2)
        return ring_phase(held, sources, axis, 4, 8)
    step = 1
    while step < devices:
        other = lax.ppermute(held, axis, [(i, i ^ step) for i in range(devices)])
        held = jnp.concatenate([held, other], axis=0)
        sources = jnp.concatenate([sources, sources ^ step])
        step *= 2
    return held, sources


def summed_over(partial, axis):
    devices = lax.axis_size(axis)
    total = partial
    step = 1
    last = devices // 2 if devices == 8 else devices
    while step < last:
        sent = total.astype(jnp.bfloat16)
        got = lax.ppermute(sent, axis, [(i, i ^ step) for i in range(devices)])
        total = sent.astype(jnp.float32) + got.astype(jnp.float32)
        step *= 2
    if devices == 8:
        nearest = {0: 7, 1: 7, 2: 4, 3: 4, 4: 3, 5: 3, 6: 0, 7: 0}
        sent = total.astype(jnp.bfloat16)
        near = [(src, dst) for dst, src in nearest.items() if min((dst - src) % 8, (src - dst) % 8) == 1]
        far = [(src, dst) for dst, src in nearest.items() if min((dst - src) % 8, (src - dst) % 8) == 2]
        got = lax.ppermute(sent, axis, near).astype(jnp.float32) + lax.ppermute(
            sent, axis, far
        ).astype(jnp.float32)
        total = sent.astype(jnp.float32) + got
    return total


def forward_kernel(
    shards_ref, q_ref, k_ref, v_ref, g_ref, key_code_ref, own_code_ref,
    att_ref, log_ref, delta_ref, gq_ref, gk_ref, gv_ref,
):
    rows = q_ref.shape[0]
    block_rows = rows // BLOCKS_PER_STEP
    step = pl.program_id(0)
    first = step * BLOCKS_PER_STEP
    row = lax.broadcasted_iota(jnp.int32, (rows, 1), 0)
    q_ids = row % block_rows
    for t in range(BLOCKS_PER_STEP):
        q_ids = q_ids + jnp.where(row // block_rows == t, shards_ref[first + t] * block_rows, 0)
    scale = 1.0 / math.sqrt(HD)
    by_rows = (((1,), (1,)), ((), ()))
    by_cols = (((0,), (0,)), ((), ()))
    queries = q_ref[...]
    grads = g_ref[...]
    scores = lax.dot_general(queries, k_ref[...], by_rows, preferred_element_type=jnp.float32) * scale
    scores = jnp.where(key_code_ref[...] <= q_ids, scores, masked_score)
    row_max = jnp.max(scores, axis=1, keepdims=True)
    softmax_part = jnp.exp(scores - row_max)
    row_sum = jnp.sum(softmax_part, axis=1, keepdims=True)
    product = jnp.dot(
        softmax_part.astype(jnp.bfloat16), v_ref[...], preferred_element_type=jnp.float32
    )
    attention = (product / row_sum).astype(jnp.bfloat16)
    log_total = row_max + jnp.log(row_sum)
    delta = jnp.sum(grads.astype(jnp.float32) * attention.astype(jnp.float32), axis=1, keepdims=True)
    att_ref[...] = attention
    log_ref[...] = log_total
    delta_ref[...] = delta

    own = block_rows

    @pl.when(step == 0)
    def _():
        probs = jnp.exp(scores[:own] - log_total[:own])
        grad_probs = lax.dot_general(
            grads[:own], v_ref[...], by_rows, preferred_element_type=jnp.float32
        )
        grad_scores = (probs * (grad_probs - delta[:own])).astype(jnp.bfloat16)
        gq_ref[...] = jnp.dot(grad_scores, k_ref[...], preferred_element_type=jnp.float32)
        gk_ref[...] = jnp.zeros_like(gk_ref)
        gv_ref[...] = jnp.zeros_like(gv_ref)

    own_scores = lax.dot_general(
        queries, k_ref[:own], by_rows, preferred_element_type=jnp.float32
    ) * scale
    own_scores = jnp.where(own_code_ref[...] <= q_ids, own_scores, masked_score)
    probs = jnp.exp(own_scores - log_total)
    gv_ref[...] += lax.dot_general(
        probs.astype(jnp.bfloat16), grads, by_cols, preferred_element_type=jnp.float32
    )
    grad_probs = lax.dot_general(grads, v_ref[:own], by_rows, preferred_element_type=jnp.float32)
    grad_scores = (probs * (grad_probs - delta)).astype(jnp.bfloat16)
    gk_ref[...] += lax.dot_general(grad_scores, queries, by_cols, preferred_element_type=jnp.float32)


def attention_all(queries, keys, values, grads, key_code, held_shards, own_rows):
    slots, width = queries.shape
    row_spec = pl.BlockSpec((QBLOCK, width), lambda i, shards: (i, 0))
    full_spec = pl.BlockSpec((slots, width), lambda i, shards: (0, 0))
    col_spec = pl.BlockSpec((QBLOCK, 1), lambda i, shards: (i, 0))
    own_spec = pl.BlockSpec((own_rows, width), lambda i, shards: (0, 0))
    grid_spec = pltpu.PrefetchScalarGridSpec(
        num_scalar_prefetch=1,
        grid=(slots // QBLOCK,),
        in_specs=[row_spec, full_spec, full_spec, row_spec,
                  pl.BlockSpec((1, slots), lambda i, shards: (0, 0)),
                  pl.BlockSpec((1, own_rows), lambda i, shards: (0, 0))],
        out_specs=[row_spec, col_spec, col_spec, own_spec, own_spec, own_spec],
    )
    own_grad = jax.ShapeDtypeStruct((own_rows, width), jnp.float32)
    return pl.pallas_call(
        forward_kernel,
        grid_spec=grid_spec,
        out_shape=[
            jax.ShapeDtypeStruct((slots, width), jnp.bfloat16),
            jax.ShapeDtypeStruct((slots, 1), jnp.float32),
            jax.ShapeDtypeStruct((slots, 1), jnp.float32),
            own_grad, own_grad, own_grad,
        ],
    )(held_shards, queries, keys, values, grads, key_code.reshape(1, slots),
      key_code[:own_rows].reshape(1, own_rows))


def per_device(
    byte_states,
    conv_kernel,
    mix_weight,
    norm_gain,
    query_weight,
    key_weight,
    value_weight,
    boundaries,
    span_counts,
    grad_attended,
):
    row_count = byte_states.shape[0]
    slot_count = boundaries.shape[0]
    head_width = query_weight.shape[1]
    score_scale = 1.0 / math.sqrt(HD)
    shard_index = lax.axis_index("seq")
    shards = lax.axis_size("seq")
    first_slot = shard_index * slot_count
    own_ids = first_slot + jnp.arange(slot_count, dtype=jnp.int32)
    before_rim = neighbour(byte_states[row_count - (KCONV - 1) :].astype(jnp.float32), 1)
    extended = jnp.concatenate([before_rim.astype(jnp.bfloat16), byte_states], axis=0)
    tap_rows = (boundaries[None, :] + jnp.arange(KCONV - 1, -1, -1, dtype=jnp.int32)[:, None])
    tapped = jnp.take(extended, tap_rows.reshape(-1), axis=0).astype(jnp.float32)
    tapped = tapped.reshape(KCONV, slot_count, D)
    span_depth = conv_kernel[0] * tapped[0]
    for offset in range(1, KCONV):
        span_depth = span_depth + conv_kernel[offset] * tapped[offset]
    span_depth = span_depth.astype(jnp.bfloat16)
    span_bytes = tapped[0]
    live_mask = jnp.arange(slot_count, dtype=jnp.int32) < span_counts[0]
    span_state = span_bytes + jnp.dot(span_depth, mix_weight, preferred_element_type=jnp.float32)
    inverse_rms = lax.rsqrt(jnp.mean(span_state * span_state, axis=1) + 1e-05)
    normed = (span_state * inverse_rms[:, None] * norm_gain).astype(jnp.bfloat16)
    queries = jnp.dot(normed, query_weight, preferred_element_type=jnp.float32).astype(jnp.bfloat16)
    key_rows = jnp.dot(normed, key_weight, preferred_element_type=jnp.float32).astype(jnp.bfloat16)
    value_rows = jnp.dot(normed, value_weight, preferred_element_type=jnp.float32).astype(
        jnp.bfloat16
    )
    grad_rows = jnp.where(live_mask[:, None], grad_attended, jnp.zeros_like(grad_attended))

    count_rows = jnp.broadcast_to(span_counts[0].astype(jnp.bfloat16), (16, head_width))
    packed = jnp.concatenate([queries, key_rows, value_rows, grad_rows, count_rows], axis=0)
    gathered, held_shards = gather_blocks(packed, "seq")
    total_slots = shards * slot_count

    def piece(k):
        return gathered[:, k * slot_count : (k + 1) * slot_count].reshape(total_slots, head_width)

    all_queries, all_keys, all_values, all_grads = piece(0), piece(1), piece(2), piece(3)
    all_counts = gathered[:, 4 * slot_count, 0].astype(jnp.int32)
    all_live = (
        jnp.arange(slot_count, dtype=jnp.int32)[None, :] < all_counts[:, None]
    ).reshape(total_slots)
    slot_ids = (
        held_shards[:, None] * slot_count + jnp.arange(slot_count, dtype=jnp.int32)[None, :]
    ).reshape(total_slots)

    all_attended, _, _, query_grad, key_grad, value_grad = attention_all(
        all_queries, all_keys, all_values, all_grads,
        jnp.where(all_live, slot_ids, total_slots), held_shards, slot_count,
    )
    attended = jnp.where(live_mask[:, None], all_attended[:slot_count], jnp.bfloat16(0.0))
    query_grad_rows = (query_grad * score_scale).astype(jnp.bfloat16)
    key_grad_rows = (key_grad * score_scale).astype(jnp.bfloat16)
    value_grad_rows = value_grad.astype(jnp.bfloat16)

    contract = (((1,), (1,)), ((), ()))
    partial_normed = lax.dot_general(
        jnp.concatenate([query_grad_rows, key_grad_rows, value_grad_rows], axis=1),
        jnp.concatenate([query_weight, key_weight, value_weight], axis=1),
        contract,
        preferred_element_type=jnp.float32,
    )
    grad_normed = summed_over(partial_normed, "head")
    scaled_grad = norm_gain * grad_normed
    cubed = inverse_rms * inverse_rms * inverse_rms
    grad_state = (
        inverse_rms[:, None] * scaled_grad
        - span_state * cubed[:, None] * jnp.mean(scaled_grad * span_state, axis=1)[:, None]
    )
    grad_state = jnp.where(live_mask[:, None], grad_state, jnp.float32(0.0))
    mixed_grad = lax.dot_general(
        grad_state.astype(jnp.bfloat16), mix_weight, contract, preferred_element_type=jnp.float32
    )
    mixed_grad = mixed_grad.astype(jnp.float32)
    contributions = jnp.concatenate(
        [grad_state + conv_kernel[0] * mixed_grad]
        + [conv_kernel[offset] * mixed_grad for offset in range(1, KCONV)],
        axis=0,
    )
    target_rows = (
        boundaries[None, :] - jnp.arange(KCONV, dtype=jnp.int32)[:, None]
    ).reshape(KCONV * slot_count)
    exact = lax.Precision.HIGHEST
    rim_rows = jnp.arange(-(KCONV - 1), 0, dtype=jnp.int32)
    rim_pick = (rim_rows[:, None] == target_rows[None, :]).astype(jnp.float32)
    before_rows = jnp.dot(rim_pick, contributions, precision=exact)
    after_rim = neighbour(before_rows, -1)
    row_pick = (
        jnp.arange(row_count, dtype=jnp.int32)[:, None] == target_rows[None, :]
    ).astype(jnp.float32)
    local_grad = lax.optimization_barrier(jnp.dot(row_pick, contributions, precision=exact))
    tail = jnp.concatenate(
        [jnp.zeros((row_count - (KCONV - 1), D), jnp.float32), after_rim], axis=0
    )
    grad_bytes = (local_grad + tail).astype(jnp.bfloat16)
    return (attended, grad_bytes)


def solution(mesh):
    return jax.shard_map(
        per_device,
        mesh=mesh,
        in_specs=(
            P(("doc", "seq"), None),
            P(),
            P(),
            P(),
            P(None, "head"),
            P(None, "head"),
            P(None, "head"),
            P(("doc", "seq")),
            P(("doc", "seq")),
            P(("doc", "seq"), "head"),
        ),
        out_specs=(P(("doc", "seq"), "head"), P(("doc", "seq"), None)),
        check_vma=False,
    )
```

```python
import math

import jax
import jax.numpy as jnp
from jax import lax
from jax.experimental import pallas as pl
from jax.experimental.pallas import tpu as pltpu
from jax.sharding import PartitionSpec as P

D = 1024
HD = 128
KCONV = 4
QBLOCK = 256
BLOCKS_PER_STEP = 4


masked_score = -1e30


def passed_along(array, axis, by):
    devices = lax.axis_size(axis)
    pairs = [(i, i + by) for i in range(devices) if 0 <= i + by < devices]
    return lax.ppermute(array, axis, pairs)


def neighbour(rim_rows, offset_by):
    return passed_along(rim_rows, "seq", offset_by)


def ring_neighbour(index, by, ring, stride):
    place = (index // stride) % ring
    return index + ((place + by) % ring - place) * stride


def ring_phase(held, sources, axis, ring, stride):
    devices = lax.axis_size(axis)

    def shifted(array, by):
        pairs = [(i, ring_neighbour(i, by, ring, stride)) for i in range(devices)]
        return lax.ppermute(array, axis, pairs)

    half = held.shape[0] // 2
    from_below = shifted(held, 1)
    from_above = shifted(held, -1)
    parts = [held, from_below, from_above, shifted(from_below[:half], 1), shifted(from_above[half:], -1)]
    origins = [
        sources,
        ring_neighbour(sources, -1, ring, stride),
        ring_neighbour(sources, 1, ring, stride),
        ring_neighbour(sources[:half], -2, ring, stride),
        ring_neighbour(sources[half:], 2, ring, stride),
    ]
    return jnp.concatenate(parts, axis=0), jnp.concatenate(origins)


def gather_blocks(block, axis):
    devices = lax.axis_size(axis)
    me = lax.axis_index(axis)
    held = block[None]
    sources = me[None]
    if devices == 32:
        other = lax.ppermute(held, axis, [(i, i ^ 1) for i in range(devices)])
        held = jnp.concatenate([held, other], axis=0)
        sources = jnp.concatenate([sources, sources ^ 1])
        held, sources = ring_phase(held, sources, axis, 4, 2)
        return ring_phase(held, sources, axis, 4, 8)
    step = 1
    while step < devices:
        other = lax.ppermute(held, axis, [(i, i ^ step) for i in range(devices)])
        held = jnp.concatenate([held, other], axis=0)
        sources = jnp.concatenate([sources, sources ^ step])
        step *= 2
    return held, sources


def summed_over(partial, axis):
    devices = lax.axis_size(axis)
    total = partial
    step = 1
    last = devices // 2 if devices == 8 else devices
    while step < last:
        sent = total.astype(jnp.bfloat16)
        got = lax.ppermute(sent, axis, [(i, i ^ step) for i in range(devices)])
        total = sent.astype(jnp.float32) + got.astype(jnp.float32)
        step *= 2
    if devices == 8:
        nearest = {0: 7, 1: 7, 2: 4, 3: 4, 4: 3, 5: 3, 6: 0, 7: 0}
        sent = total.astype(jnp.bfloat16)
        near = [(src, dst) for dst, src in nearest.items() if min((dst - src) % 8, (src - dst) % 8) == 1]
        far = [(src, dst) for dst, src in nearest.items() if min((dst - src) % 8, (src - dst) % 8) == 2]
        got = lax.ppermute(sent, axis, near).astype(jnp.float32) + lax.ppermute(
            sent, axis, far
        ).astype(jnp.float32)
        total = sent.astype(jnp.float32) + got
    return total


def forward_kernel(
    shards_ref, q_ref, k_ref, v_ref, g_ref, key_code_ref, own_code_ref,
    att_ref, gq_ref, gk_ref, gv_ref,
):
    block_rows = q_ref.shape[1]
    rows = q_ref.shape[0] * block_rows
    width = q_ref.shape[2]
    step = pl.program_id(0)
    first = step * BLOCKS_PER_STEP
    row = lax.broadcasted_iota(jnp.int32, (rows, 1), 0)
    q_ids = row % block_rows
    for t in range(BLOCKS_PER_STEP):
        q_ids = q_ids + jnp.where(row // block_rows == t, shards_ref[first + t] * block_rows, 0)
    scale = 1.0 / math.sqrt(HD)
    by_rows = (((1,), (1,)), ((), ()))
    by_cols = (((0,), (0,)), ((), ()))
    queries = q_ref[...].reshape(rows, width)
    grads = g_ref[...].reshape(rows, width)
    keys = k_ref[...].reshape(-1, width)
    values = v_ref[...].reshape(-1, width)
    scores = lax.dot_general(queries, keys, by_rows, preferred_element_type=jnp.float32) * scale
    scores = jnp.where(key_code_ref[...] <= q_ids, scores, masked_score)
    row_max = jnp.max(scores, axis=1, keepdims=True)
    softmax_part = jnp.exp(scores - row_max)
    row_sum = jnp.sum(softmax_part, axis=1, keepdims=True)
    product = jnp.dot(
        softmax_part.astype(jnp.bfloat16), values, preferred_element_type=jnp.float32
    )
    attention = (product / row_sum).astype(jnp.bfloat16)
    log_total = row_max + jnp.log(row_sum)
    delta = jnp.sum(grads.astype(jnp.float32) * attention.astype(jnp.float32), axis=1, keepdims=True)

    own = block_rows

    @pl.when(step == 0)
    def _():
        probs = jnp.exp(scores[:own] - log_total[:own])
        grad_probs = lax.dot_general(
            grads[:own], values, by_rows, preferred_element_type=jnp.float32
        )
        grad_scores = (probs * (grad_probs - delta[:own])).astype(jnp.bfloat16)
        gq_ref[...] = jnp.dot(grad_scores, keys, preferred_element_type=jnp.float32)
        att_ref[...] = attention[:own]
        gk_ref[...] = jnp.zeros_like(gk_ref)
        gv_ref[...] = jnp.zeros_like(gv_ref)

    own_scores = lax.dot_general(
        queries, k_ref[0], by_rows, preferred_element_type=jnp.float32
    ) * scale
    own_scores = jnp.where(own_code_ref[...] <= q_ids, own_scores, masked_score)
    probs = jnp.exp(own_scores - log_total)
    gv_ref[...] += lax.dot_general(
        probs.astype(jnp.bfloat16), grads, by_cols, preferred_element_type=jnp.float32
    )
    grad_probs = lax.dot_general(grads, v_ref[0], by_rows, preferred_element_type=jnp.float32)
    grad_scores = (probs * (grad_probs - delta)).astype(jnp.bfloat16)
    gk_ref[...] += lax.dot_general(grad_scores, queries, by_cols, preferred_element_type=jnp.float32)


def attention_all(gathered, key_code, held_shards):
    blocks, _, width = gathered.shape
    block_rows = key_code.shape[0] // blocks
    slots = blocks * block_rows
    step_spec = lambda part: pl.BlockSpec(
        (BLOCKS_PER_STEP, block_rows, width), lambda i, shards: (i, part, 0)
    )
    all_spec = lambda part: pl.BlockSpec(
        (blocks, block_rows, width), lambda i, shards: (0, part, 0)
    )
    own_spec = pl.BlockSpec((block_rows, width), lambda i, shards: (0, 0))
    grid_spec = pltpu.PrefetchScalarGridSpec(
        num_scalar_prefetch=1,
        grid=(blocks // BLOCKS_PER_STEP,),
        in_specs=[step_spec(0), all_spec(1), all_spec(2), step_spec(3),
                  pl.BlockSpec((1, slots), lambda i, shards: (0, 0)),
                  pl.BlockSpec((1, block_rows), lambda i, shards: (0, 0))],
        out_specs=[own_spec, own_spec, own_spec, own_spec],
    )
    own_grad = jax.ShapeDtypeStruct((block_rows, width), jnp.float32)
    return pl.pallas_call(
        forward_kernel,
        grid_spec=grid_spec,
        out_shape=[jax.ShapeDtypeStruct((block_rows, width), jnp.bfloat16), own_grad, own_grad, own_grad],
    )(held_shards, gathered, gathered, gathered, gathered, key_code.reshape(1, slots),
      key_code[:block_rows].reshape(1, block_rows))


def per_device(
    byte_states,
    conv_kernel,
    mix_weight,
    norm_gain,
    query_weight,
    key_weight,
    value_weight,
    boundaries,
    span_counts,
    grad_attended,
):
    row_count = byte_states.shape[0]
    slot_count = boundaries.shape[0]
    head_width = query_weight.shape[1]
    score_scale = 1.0 / math.sqrt(HD)
    shard_index = lax.axis_index("seq")
    shards = lax.axis_size("seq")
    first_slot = shard_index * slot_count
    own_ids = first_slot + jnp.arange(slot_count, dtype=jnp.int32)
    before_rim = neighbour(byte_states[row_count - (KCONV - 1) :].astype(jnp.float32), 1)
    extended = jnp.concatenate([before_rim.astype(jnp.bfloat16), byte_states], axis=0)
    tap_rows = (boundaries[None, :] + jnp.arange(KCONV - 1, -1, -1, dtype=jnp.int32)[:, None])
    tapped = jnp.take(extended, tap_rows.reshape(-1), axis=0).astype(jnp.float32)
    tapped = tapped.reshape(KCONV, slot_count, D)
    span_depth = conv_kernel[0] * tapped[0]
    for offset in range(1, KCONV):
        span_depth = span_depth + conv_kernel[offset] * tapped[offset]
    span_depth = span_depth.astype(jnp.bfloat16)
    span_bytes = tapped[0]
    live_mask = jnp.arange(slot_count, dtype=jnp.int32) < span_counts[0]
    span_state = span_bytes + jnp.dot(span_depth, mix_weight, preferred_element_type=jnp.float32)
    inverse_rms = lax.rsqrt(jnp.mean(span_state * span_state, axis=1) + 1e-05)
    normed = (span_state * inverse_rms[:, None] * norm_gain).astype(jnp.bfloat16)
    queries = jnp.dot(normed, query_weight, preferred_element_type=jnp.float32).astype(jnp.bfloat16)
    key_rows = jnp.dot(normed, key_weight, preferred_element_type=jnp.float32).astype(jnp.bfloat16)
    value_rows = jnp.dot(normed, value_weight, preferred_element_type=jnp.float32).astype(
        jnp.bfloat16
    )
    grad_rows = jnp.where(live_mask[:, None], grad_attended, jnp.zeros_like(grad_attended))

    count_rows = jnp.broadcast_to(span_counts[0].astype(jnp.bfloat16), (16, head_width))
    packed = jnp.concatenate([queries, key_rows, value_rows, grad_rows, count_rows], axis=0)
    gathered, held_shards = gather_blocks(packed, "seq")
    total_slots = shards * slot_count

    all_counts = gathered[:, 4 * slot_count, 0].astype(jnp.int32)
    all_live = (
        jnp.arange(slot_count, dtype=jnp.int32)[None, :] < all_counts[:, None]
    ).reshape(total_slots)
    slot_ids = (
        held_shards[:, None] * slot_count + jnp.arange(slot_count, dtype=jnp.int32)[None, :]
    ).reshape(total_slots)

    own_attended, query_grad, key_grad, value_grad = attention_all(
        gathered, jnp.where(all_live, slot_ids, total_slots), held_shards
    )
    attended = jnp.where(live_mask[:, None], own_attended, jnp.bfloat16(0.0))
    query_grad_rows = (query_grad * score_scale).astype(jnp.bfloat16)
    key_grad_rows = (key_grad * score_scale).astype(jnp.bfloat16)
    value_grad_rows = value_grad.astype(jnp.bfloat16)

    contract = (((1,), (1,)), ((), ()))
    partial_normed = lax.dot_general(
        jnp.concatenate([query_grad_rows, key_grad_rows, value_grad_rows], axis=1),
        jnp.concatenate([query_weight, key_weight, value_weight], axis=1),
        contract,
        preferred_element_type=jnp.float32,
    )
    grad_normed = summed_over(partial_normed, "head")
    scaled_grad = norm_gain * grad_normed
    cubed = inverse_rms * inverse_rms * inverse_rms
    grad_state = (
        inverse_rms[:, None] * scaled_grad
        - span_state * cubed[:, None] * jnp.mean(scaled_grad * span_state, axis=1)[:, None]
    )
    grad_state = jnp.where(live_mask[:, None], grad_state, jnp.float32(0.0))
    mixed_grad = lax.dot_general(
        grad_state.astype(jnp.bfloat16), mix_weight, contract, preferred_element_type=jnp.float32
    )
    mixed_grad = mixed_grad.astype(jnp.float32)
    contributions = jnp.concatenate(
        [grad_state + conv_kernel[0] * mixed_grad]
        + [conv_kernel[offset] * mixed_grad for offset in range(1, KCONV)],
        axis=0,
    )
    target_rows = (
        boundaries[None, :] - jnp.arange(KCONV, dtype=jnp.int32)[:, None]
    ).reshape(KCONV * slot_count)
    exact = lax.Precision.HIGHEST
    rim_rows = jnp.arange(-(KCONV - 1), 0, dtype=jnp.int32)
    rim_pick = (rim_rows[:, None] == target_rows[None, :]).astype(jnp.float32)
    before_rows = jnp.dot(rim_pick, contributions, precision=exact)
    after_rim = neighbour(before_rows, -1)
    row_pick = (
        jnp.arange(row_count, dtype=jnp.int32)[:, None] == target_rows[None, :]
    ).astype(jnp.float32)
    local_grad = lax.optimization_barrier(jnp.dot(row_pick, contributions, precision=exact))
    tail = jnp.concatenate(
        [jnp.zeros((row_count - (KCONV - 1), D), jnp.float32), after_rim], axis=0
    )
    grad_bytes = (local_grad + tail).astype(jnp.bfloat16)
    return (attended, grad_bytes)


def solution(mesh):
    return jax.shard_map(
        per_device,
        mesh=mesh,
        in_specs=(
            P(("doc", "seq"), None),
            P(),
            P(),
            P(),
            P(None, "head"),
            P(None, "head"),
            P(None, "head"),
            P(("doc", "seq")),
            P(("doc", "seq")),
            P(("doc", "seq"), "head"),
        ),
        out_specs=(P(("doc", "seq"), "head"), P(("doc", "seq"), None)),
        check_vma=False,
    )
```

```python
import math

import jax
import jax.numpy as jnp
from jax import lax
from jax.experimental import pallas as pl
from jax.experimental.pallas import tpu as pltpu
from jax.sharding import PartitionSpec as P

D = 1024
HD = 128
KCONV = 4
QBLOCK = 256
BLOCKS_PER_STEP = 4


masked_score = -1e30


def passed_along(array, axis, by):
    devices = lax.axis_size(axis)
    pairs = [(i, i + by) for i in range(devices) if 0 <= i + by < devices]
    return lax.ppermute(array, axis, pairs)


def neighbour(rim_rows, offset_by):
    return passed_along(rim_rows, "seq", offset_by)


def ring_neighbour(index, by, ring, stride):
    place = (index // stride) % ring
    return index + ((place + by) % ring - place) * stride


def ring_phase(held, sources, axis, ring, stride):
    devices = lax.axis_size(axis)

    def shifted(array, by):
        pairs = [(i, ring_neighbour(i, by, ring, stride)) for i in range(devices)]
        return lax.ppermute(array, axis, pairs)

    half = held.shape[0] // 2
    from_below = shifted(held, 1)
    from_above = shifted(held, -1)
    parts = [held, from_below, from_above, shifted(from_below[:half], 1), shifted(from_above[half:], -1)]
    origins = [
        sources,
        ring_neighbour(sources, -1, ring, stride),
        ring_neighbour(sources, 1, ring, stride),
        ring_neighbour(sources[:half], -2, ring, stride),
        ring_neighbour(sources[half:], 2, ring, stride),
    ]
    return jnp.concatenate(parts, axis=0), jnp.concatenate(origins)


def gather_blocks(block, axis):
    devices = lax.axis_size(axis)
    me = lax.axis_index(axis)
    held = block[None]
    sources = me[None]
    if devices == 32:
        other = lax.ppermute(held, axis, [(i, i ^ 1) for i in range(devices)])
        held = jnp.concatenate([held, other], axis=0)
        sources = jnp.concatenate([sources, sources ^ 1])
        held, sources = ring_phase(held, sources, axis, 4, 2)
        return ring_phase(held, sources, axis, 4, 8)
    step = 1
    while step < devices:
        other = lax.ppermute(held, axis, [(i, i ^ step) for i in range(devices)])
        held = jnp.concatenate([held, other], axis=0)
        sources = jnp.concatenate([sources, sources ^ step])
        step *= 2
    return held, sources


def nearest_exchange(value, axis, nearest):
    devices = lax.axis_size(axis)

    def distance(src, dst):
        return min((dst - src) % devices, (src - dst) % devices)

    got = None
    for hops in sorted({distance(src, dst) for dst, src in nearest.items()}):
        pairs = [(src, dst) for dst, src in nearest.items() if distance(src, dst) == hops]
        part = lax.ppermute(value, axis, pairs).astype(jnp.float32)
        got = part if got is None else got + part
    return got


def summed_over(partial, axis):
    devices = lax.axis_size(axis)
    if devices == 8:
        sent = partial.astype(jnp.bfloat16)
        total = sent.astype(jnp.float32) + lax.ppermute(
            sent, axis, [(i, i ^ 1) for i in range(devices)]
        ).astype(jnp.float32)
        for nearest in (
            {0: 2, 1: 2, 2: 1, 3: 1, 4: 6, 5: 6, 6: 5, 7: 5},
            {0: 7, 1: 7, 2: 4, 3: 4, 4: 3, 5: 3, 6: 0, 7: 0},
        ):
            sent = total.astype(jnp.bfloat16)
            total = sent.astype(jnp.float32) + nearest_exchange(sent, axis, nearest)
        return total
    total = partial
    step = 1
    while step < devices:
        sent = total.astype(jnp.bfloat16)
        got = lax.ppermute(sent, axis, [(i, i ^ step) for i in range(devices)])
        total = sent.astype(jnp.float32) + got.astype(jnp.float32)
        step *= 2
    return total


def forward_kernel(
    shards_ref, q_ref, k_ref, v_ref, g_ref, key_code_ref, own_code_ref,
    att_ref, gq_ref, gk_ref, gv_ref,
):
    block_rows = q_ref.shape[1]
    rows = q_ref.shape[0] * block_rows
    width = q_ref.shape[2]
    step = pl.program_id(0)
    first = step * BLOCKS_PER_STEP
    row = lax.broadcasted_iota(jnp.int32, (rows, 1), 0)
    q_ids = row % block_rows
    for t in range(BLOCKS_PER_STEP):
        q_ids = q_ids + jnp.where(row // block_rows == t, shards_ref[first + t] * block_rows, 0)
    scale = 1.0 / math.sqrt(HD)
    by_rows = (((1,), (1,)), ((), ()))
    by_cols = (((0,), (0,)), ((), ()))
    queries = q_ref[...].reshape(rows, width)
    grads = g_ref[...].reshape(rows, width)
    keys = k_ref[...].reshape(-1, width)
    values = v_ref[...].reshape(-1, width)
    scores = lax.dot_general(queries, keys, by_rows, preferred_element_type=jnp.float32) * scale
    scores = jnp.where(key_code_ref[...] <= q_ids, scores, masked_score)
    row_max = jnp.max(scores, axis=1, keepdims=True)
    softmax_part = jnp.exp(scores - row_max)
    row_sum = jnp.sum(softmax_part, axis=1, keepdims=True)
    product = jnp.dot(
        softmax_part.astype(jnp.bfloat16), values, preferred_element_type=jnp.float32
    )
    attention = (product / row_sum).astype(jnp.bfloat16)
    log_total = row_max + jnp.log(row_sum)
    delta = jnp.sum(grads.astype(jnp.float32) * attention.astype(jnp.float32), axis=1, keepdims=True)

    own = block_rows

    @pl.when(step == 0)
    def _():
        probs = jnp.exp(scores[:own] - log_total[:own])
        grad_probs = lax.dot_general(
            grads[:own], values, by_rows, preferred_element_type=jnp.float32
        )
        grad_scores = (probs * (grad_probs - delta[:own])).astype(jnp.bfloat16)
        gq_ref[...] = jnp.dot(grad_scores, keys, preferred_element_type=jnp.float32)
        att_ref[...] = attention[:own]
        gk_ref[...] = jnp.zeros_like(gk_ref)
        gv_ref[...] = jnp.zeros_like(gv_ref)

    own_scores = lax.dot_general(
        queries, k_ref[0], by_rows, preferred_element_type=jnp.float32
    ) * scale
    own_scores = jnp.where(own_code_ref[...] <= q_ids, own_scores, masked_score)
    probs = jnp.exp(own_scores - log_total)
    gv_ref[...] += lax.dot_general(
        probs.astype(jnp.bfloat16), grads, by_cols, preferred_element_type=jnp.float32
    )
    grad_probs = lax.dot_general(grads, v_ref[0], by_rows, preferred_element_type=jnp.float32)
    grad_scores = (probs * (grad_probs - delta)).astype(jnp.bfloat16)
    gk_ref[...] += lax.dot_general(grad_scores, queries, by_cols, preferred_element_type=jnp.float32)


def attention_all(gathered, key_code, held_shards):
    blocks, _, width = gathered.shape
    block_rows = key_code.shape[0] // blocks
    slots = blocks * block_rows
    step_spec = lambda part: pl.BlockSpec(
        (BLOCKS_PER_STEP, block_rows, width), lambda i, shards: (i, part, 0)
    )
    all_spec = lambda part: pl.BlockSpec(
        (blocks, block_rows, width), lambda i, shards: (0, part, 0)
    )
    own_spec = pl.BlockSpec((block_rows, width), lambda i, shards: (0, 0))
    grid_spec = pltpu.PrefetchScalarGridSpec(
        num_scalar_prefetch=1,
        grid=(blocks // BLOCKS_PER_STEP,),
        in_specs=[step_spec(0), all_spec(1), all_spec(2), step_spec(3),
                  pl.BlockSpec((1, slots), lambda i, shards: (0, 0)),
                  pl.BlockSpec((1, block_rows), lambda i, shards: (0, 0))],
        out_specs=[own_spec, own_spec, own_spec, own_spec],
    )
    own_grad = jax.ShapeDtypeStruct((block_rows, width), jnp.float32)
    return pl.pallas_call(
        forward_kernel,
        grid_spec=grid_spec,
        out_shape=[jax.ShapeDtypeStruct((block_rows, width), jnp.bfloat16), own_grad, own_grad, own_grad],
    )(held_shards, gathered, gathered, gathered, gathered, key_code.reshape(1, slots),
      key_code[:block_rows].reshape(1, block_rows))


def per_device(
    byte_states,
    conv_kernel,
    mix_weight,
    norm_gain,
    query_weight,
    key_weight,
    value_weight,
    boundaries,
    span_counts,
    grad_attended,
):
    row_count = byte_states.shape[0]
    slot_count = boundaries.shape[0]
    head_width = query_weight.shape[1]
    score_scale = 1.0 / math.sqrt(HD)
    shard_index = lax.axis_index("seq")
    shards = lax.axis_size("seq")
    first_slot = shard_index * slot_count
    own_ids = first_slot + jnp.arange(slot_count, dtype=jnp.int32)
    before_rim = neighbour(byte_states[row_count - (KCONV - 1) :].astype(jnp.float32), 1)
    extended = jnp.concatenate([before_rim.astype(jnp.bfloat16), byte_states], axis=0)
    tap_rows = (boundaries[None, :] + jnp.arange(KCONV - 1, -1, -1, dtype=jnp.int32)[:, None])
    tapped = jnp.take(extended, tap_rows.reshape(-1), axis=0).astype(jnp.float32)
    tapped = tapped.reshape(KCONV, slot_count, D)
    span_depth = conv_kernel[0] * tapped[0]
    for offset in range(1, KCONV):
        span_depth = span_depth + conv_kernel[offset] * tapped[offset]
    span_depth = span_depth.astype(jnp.bfloat16)
    span_bytes = tapped[0]
    live_mask = jnp.arange(slot_count, dtype=jnp.int32) < span_counts[0]
    span_state = span_bytes + jnp.dot(span_depth, mix_weight, preferred_element_type=jnp.float32)
    inverse_rms = lax.rsqrt(jnp.mean(span_state * span_state, axis=1) + 1e-05)
    normed = (span_state * inverse_rms[:, None] * norm_gain).astype(jnp.bfloat16)
    queries = jnp.dot(normed, query_weight, preferred_element_type=jnp.float32).astype(jnp.bfloat16)
    key_rows = jnp.dot(normed, key_weight, preferred_element_type=jnp.float32).astype(jnp.bfloat16)
    value_rows = jnp.dot(normed, value_weight, preferred_element_type=jnp.float32).astype(
        jnp.bfloat16
    )
    grad_rows = jnp.where(live_mask[:, None], grad_attended, jnp.zeros_like(grad_attended))

    count_rows = jnp.broadcast_to(span_counts[0].astype(jnp.bfloat16), (16, head_width))
    packed = jnp.concatenate([queries, key_rows, value_rows, grad_rows, count_rows], axis=0)
    gathered, held_shards = gather_blocks(packed, "seq")
    total_slots = shards * slot_count

    all_counts = gathered[:, 4 * slot_count, 0].astype(jnp.int32)
    all_live = (
        jnp.arange(slot_count, dtype=jnp.int32)[None, :] < all_counts[:, None]
    ).reshape(total_slots)
    slot_ids = (
        held_shards[:, None] * slot_count + jnp.arange(slot_count, dtype=jnp.int32)[None, :]
    ).reshape(total_slots)

    own_attended, query_grad, key_grad, value_grad = attention_all(
        gathered, jnp.where(all_live, slot_ids, total_slots), held_shards
    )
    attended = jnp.where(live_mask[:, None], own_attended, jnp.bfloat16(0.0))
    query_grad_rows = (query_grad * score_scale).astype(jnp.bfloat16)
    key_grad_rows = (key_grad * score_scale).astype(jnp.bfloat16)
    value_grad_rows = value_grad.astype(jnp.bfloat16)

    contract = (((1,), (1,)), ((), ()))
    partial_normed = lax.dot_general(
        jnp.concatenate([query_grad_rows, key_grad_rows, value_grad_rows], axis=1),
        jnp.concatenate([query_weight, key_weight, value_weight], axis=1),
        contract,
        preferred_element_type=jnp.float32,
    )
    grad_normed = summed_over(partial_normed, "head")
    scaled_grad = norm_gain * grad_normed
    cubed = inverse_rms * inverse_rms * inverse_rms
    grad_state = (
        inverse_rms[:, None] * scaled_grad
        - span_state * cubed[:, None] * jnp.mean(scaled_grad * span_state, axis=1)[:, None]
    )
    grad_state = jnp.where(live_mask[:, None], grad_state, jnp.float32(0.0))
    mixed_grad = lax.dot_general(
        grad_state.astype(jnp.bfloat16), mix_weight, contract, preferred_element_type=jnp.float32
    )
    mixed_grad = mixed_grad.astype(jnp.float32)
    contributions = jnp.concatenate(
        [grad_state + conv_kernel[0] * mixed_grad]
        + [conv_kernel[offset] * mixed_grad for offset in range(1, KCONV)],
        axis=0,
    )
    target_rows = (
        boundaries[None, :] - jnp.arange(KCONV, dtype=jnp.int32)[:, None]
    ).reshape(KCONV * slot_count)
    exact = lax.Precision.HIGHEST
    rim_rows = jnp.arange(-(KCONV - 1), 0, dtype=jnp.int32)
    rim_pick = (rim_rows[:, None] == target_rows[None, :]).astype(jnp.float32)
    before_rows = jnp.dot(rim_pick, contributions, precision=exact)
    after_rim = neighbour(before_rows, -1)
    row_pick = (
        jnp.arange(row_count, dtype=jnp.int32)[:, None] == target_rows[None, :]
    ).astype(jnp.float32)
    local_grad = lax.optimization_barrier(jnp.dot(row_pick, contributions, precision=exact))
    tail = jnp.concatenate(
        [jnp.zeros((row_count - (KCONV - 1), D), jnp.float32), after_rim], axis=0
    )
    grad_bytes = (local_grad + tail).astype(jnp.bfloat16)
    return (attended, grad_bytes)


def solution(mesh):
    return jax.shard_map(
        per_device,
        mesh=mesh,
        in_specs=(
            P(("doc", "seq"), None),
            P(),
            P(),
            P(),
            P(None, "head"),
            P(None, "head"),
            P(None, "head"),
            P(("doc", "seq")),
            P(("doc", "seq")),
            P(("doc", "seq"), "head"),
        ),
        out_specs=(P(("doc", "seq"), "head"), P(("doc", "seq"), None)),
        check_vma=False,
    )
```

```python
import math

import jax
import jax.numpy as jnp
from jax import lax
from jax.experimental import pallas as pl
from jax.experimental.pallas import tpu as pltpu
from jax.sharding import PartitionSpec as P

D = 1024
HD = 128
KCONV = 4
QBLOCK = 256
BLOCKS_PER_STEP = 4


masked_score = -1e30


def passed_along(array, axis, by):
    devices = lax.axis_size(axis)
    pairs = [(i, i + by) for i in range(devices) if 0 <= i + by < devices]
    return lax.ppermute(array, axis, pairs)


def neighbour(rim_rows, offset_by):
    return passed_along(rim_rows, "seq", offset_by)


def ring_neighbour(index, by, ring, stride):
    place = (index // stride) % ring
    return index + ((place + by) % ring - place) * stride


def ring_phase(held, sources, axis, ring, stride):
    devices = lax.axis_size(axis)

    def shifted(array, by):
        pairs = [(i, ring_neighbour(i, by, ring, stride)) for i in range(devices)]
        return lax.ppermute(array, axis, pairs)

    half = held.shape[0] // 2
    from_below = shifted(held, 1)
    from_above = shifted(held, -1)
    parts = [held, from_below, from_above, shifted(from_below[:half], 1), shifted(from_above[half:], -1)]
    origins = [
        sources,
        ring_neighbour(sources, -1, ring, stride),
        ring_neighbour(sources, 1, ring, stride),
        ring_neighbour(sources[:half], -2, ring, stride),
        ring_neighbour(sources[half:], 2, ring, stride),
    ]
    return jnp.concatenate(parts, axis=0), jnp.concatenate(origins)


def gather_blocks(block, axis):
    devices = lax.axis_size(axis)
    me = lax.axis_index(axis)
    held = block[None]
    sources = me[None]
    if devices == 32:
        other = lax.ppermute(held, axis, [(i, i ^ 1) for i in range(devices)])
        held = jnp.concatenate([held, other], axis=0)
        sources = jnp.concatenate([sources, sources ^ 1])
        held, sources = ring_phase(held, sources, axis, 4, 2)
        return ring_phase(held, sources, axis, 4, 8)
    step = 1
    while step < devices:
        other = lax.ppermute(held, axis, [(i, i ^ step) for i in range(devices)])
        held = jnp.concatenate([held, other], axis=0)
        sources = jnp.concatenate([sources, sources ^ step])
        step *= 2
    return held, sources


def summed_over(partial, axis):
    devices = lax.axis_size(axis)
    total = partial
    step = 1
    last = devices // 2 if devices == 8 else devices
    while step < last:
        sent = total.astype(jnp.bfloat16)
        got = lax.ppermute(sent, axis, [(i, i ^ step) for i in range(devices)])
        total = sent.astype(jnp.float32) + got.astype(jnp.float32)
        step *= 2
    if devices == 8:
        nearest = {0: 7, 1: 7, 2: 4, 3: 4, 4: 3, 5: 3, 6: 0, 7: 0}
        sent = total.astype(jnp.bfloat16)
        near = [(src, dst) for dst, src in nearest.items() if min((dst - src) % 8, (src - dst) % 8) == 1]
        far = [(src, dst) for dst, src in nearest.items() if min((dst - src) % 8, (src - dst) % 8) == 2]
        got = lax.ppermute(sent, axis, near).astype(jnp.float32) + lax.ppermute(
            sent, axis, far
        ).astype(jnp.float32)
        total = sent.astype(jnp.float32) + got
    return total


def forward_kernel(
    shards_ref, q_ref, k_ref, v_ref, g_ref, key_code_ref, own_code_ref,
    att_ref, gq_ref, gk_ref, gv_ref,
):
    block_rows = q_ref.shape[1]
    rows = q_ref.shape[0] * block_rows
    width = q_ref.shape[2]
    step = pl.program_id(0)
    first = step * BLOCKS_PER_STEP
    row = lax.broadcasted_iota(jnp.int32, (rows, 1), 0)
    q_ids = row % block_rows
    for t in range(BLOCKS_PER_STEP):
        q_ids = q_ids + jnp.where(row // block_rows == t, shards_ref[first + t] * block_rows, 0)
    scale = 1.0 / math.sqrt(HD)
    by_rows = (((1,), (1,)), ((), ()))
    by_cols = (((0,), (0,)), ((), ()))
    queries = q_ref[...].reshape(rows, width)
    grads = g_ref[...].reshape(rows, width)
    keys = k_ref[...].reshape(-1, width)
    values = v_ref[...].reshape(-1, width)
    scores = lax.dot_general(queries, keys, by_rows, preferred_element_type=jnp.float32) * scale
    scores = jnp.where(key_code_ref[...] <= q_ids, scores, masked_score)
    row_max = jnp.max(scores, axis=1, keepdims=True)
    softmax_part = jnp.exp(scores - row_max)
    row_sum = jnp.sum(softmax_part, axis=1, keepdims=True)
    product = jnp.dot(
        softmax_part.astype(jnp.bfloat16), values, preferred_element_type=jnp.float32
    )
    attention = (product / row_sum).astype(jnp.bfloat16)
    log_total = row_max + jnp.log(row_sum)
    delta = jnp.sum(grads.astype(jnp.float32) * attention.astype(jnp.float32), axis=1, keepdims=True)

    own = block_rows

    @pl.when(step == 0)
    def _():
        probs = jnp.exp(scores[:own] - log_total[:own])
        grad_probs = lax.dot_general(
            grads[:own], values, by_rows, preferred_element_type=jnp.float32
        )
        grad_scores = (probs * (grad_probs - delta[:own])).astype(jnp.bfloat16)
        gq_ref[...] = jnp.dot(grad_scores, keys, preferred_element_type=jnp.float32)
        att_ref[...] = attention[:own]
        gk_ref[...] = jnp.zeros_like(gk_ref)
        gv_ref[...] = jnp.zeros_like(gv_ref)

    own_scores = lax.dot_general(
        queries, k_ref[0], by_rows, preferred_element_type=jnp.float32
    ) * scale
    own_scores = jnp.where(own_code_ref[...] <= q_ids, own_scores, masked_score)
    probs = jnp.exp(own_scores - log_total)
    gv_ref[...] += lax.dot_general(
        probs.astype(jnp.bfloat16), grads, by_cols, preferred_element_type=jnp.float32
    )
    grad_probs = lax.dot_general(grads, v_ref[0], by_rows, preferred_element_type=jnp.float32)
    grad_scores = (probs * (grad_probs - delta)).astype(jnp.bfloat16)
    gk_ref[...] += lax.dot_general(grad_scores, queries, by_cols, preferred_element_type=jnp.float32)


def attention_all(gathered, key_code, held_shards):
    blocks, _, width = gathered.shape
    block_rows = key_code.shape[0] // blocks
    slots = blocks * block_rows
    step_spec = lambda part: pl.BlockSpec(
        (BLOCKS_PER_STEP, block_rows, width), lambda i, shards: (i, part, 0)
    )
    all_spec = lambda part: pl.BlockSpec(
        (blocks, block_rows, width), lambda i, shards: (0, part, 0)
    )
    own_spec = pl.BlockSpec((block_rows, width), lambda i, shards: (0, 0))
    grid_spec = pltpu.PrefetchScalarGridSpec(
        num_scalar_prefetch=1,
        grid=(blocks // BLOCKS_PER_STEP,),
        in_specs=[step_spec(0), all_spec(1), all_spec(2), step_spec(3),
                  pl.BlockSpec((1, slots), lambda i, shards: (0, 0)),
                  pl.BlockSpec((1, block_rows), lambda i, shards: (0, 0))],
        out_specs=[own_spec, own_spec, own_spec, own_spec],
    )
    own_grad = jax.ShapeDtypeStruct((block_rows, width), jnp.float32)
    return pl.pallas_call(
        forward_kernel,
        grid_spec=grid_spec,
        out_shape=[jax.ShapeDtypeStruct((block_rows, width), jnp.bfloat16), own_grad, own_grad, own_grad],
    )(held_shards, gathered, gathered, gathered, gathered, key_code.reshape(1, slots),
      key_code[:block_rows].reshape(1, block_rows))


def per_device(
    byte_states,
    conv_kernel,
    mix_weight,
    norm_gain,
    query_weight,
    key_weight,
    value_weight,
    boundaries,
    span_counts,
    grad_attended,
):
    row_count = byte_states.shape[0]
    slot_count = boundaries.shape[0]
    head_width = query_weight.shape[1]
    score_scale = 1.0 / math.sqrt(HD)
    shard_index = lax.axis_index("seq")
    shards = lax.axis_size("seq")
    first_slot = shard_index * slot_count
    own_ids = first_slot + jnp.arange(slot_count, dtype=jnp.int32)
    before_rim = neighbour(byte_states[row_count - (KCONV - 1) :].astype(jnp.float32), 1)
    tap_rows = (boundaries[None, :] - jnp.arange(KCONV, dtype=jnp.int32)[:, None]).reshape(-1)
    tapped = jnp.take(byte_states, jnp.maximum(tap_rows, 0), axis=0).astype(jnp.float32)
    rim_tapped = jnp.take(before_rim, jnp.clip(tap_rows + (KCONV - 1), 0, KCONV - 2), axis=0)
    tapped = jnp.where((tap_rows < 0)[:, None], rim_tapped, tapped)
    tapped = tapped.reshape(KCONV, slot_count, D)
    span_depth = conv_kernel[0] * tapped[0]
    for offset in range(1, KCONV):
        span_depth = span_depth + conv_kernel[offset] * tapped[offset]
    span_depth = span_depth.astype(jnp.bfloat16)
    span_bytes = tapped[0]
    live_mask = jnp.arange(slot_count, dtype=jnp.int32) < span_counts[0]
    span_state = span_bytes + jnp.dot(span_depth, mix_weight, preferred_element_type=jnp.float32)
    inverse_rms = lax.rsqrt(jnp.mean(span_state * span_state, axis=1) + 1e-05)
    normed = (span_state * inverse_rms[:, None] * norm_gain).astype(jnp.bfloat16)
    queries = jnp.dot(normed, query_weight, preferred_element_type=jnp.float32).astype(jnp.bfloat16)
    key_rows = jnp.dot(normed, key_weight, preferred_element_type=jnp.float32).astype(jnp.bfloat16)
    value_rows = jnp.dot(normed, value_weight, preferred_element_type=jnp.float32).astype(
        jnp.bfloat16
    )
    grad_rows = jnp.where(live_mask[:, None], grad_attended, jnp.zeros_like(grad_attended))

    count_rows = jnp.broadcast_to(span_counts[0].astype(jnp.bfloat16), (16, head_width))
    packed = jnp.concatenate([queries, key_rows, value_rows, grad_rows, count_rows], axis=0)
    gathered, held_shards = gather_blocks(packed, "seq")
    total_slots = shards * slot_count

    all_counts = gathered[:, 4 * slot_count, 0].astype(jnp.int32)
    all_live = (
        jnp.arange(slot_count, dtype=jnp.int32)[None, :] < all_counts[:, None]
    ).reshape(total_slots)
    slot_ids = (
        held_shards[:, None] * slot_count + jnp.arange(slot_count, dtype=jnp.int32)[None, :]
    ).reshape(total_slots)

    own_attended, query_grad, key_grad, value_grad = attention_all(
        gathered, jnp.where(all_live, slot_ids, total_slots), held_shards
    )
    attended = jnp.where(live_mask[:, None], own_attended, jnp.bfloat16(0.0))
    query_grad_rows = (query_grad * score_scale).astype(jnp.bfloat16)
    key_grad_rows = (key_grad * score_scale).astype(jnp.bfloat16)
    value_grad_rows = value_grad.astype(jnp.bfloat16)

    contract = (((1,), (1,)), ((), ()))
    partial_normed = lax.dot_general(
        jnp.concatenate([query_grad_rows, key_grad_rows, value_grad_rows], axis=1),
        jnp.concatenate([query_weight, key_weight, value_weight], axis=1),
        contract,
        preferred_element_type=jnp.float32,
    )
    grad_normed = summed_over(partial_normed, "head")
    scaled_grad = norm_gain * grad_normed
    cubed = inverse_rms * inverse_rms * inverse_rms
    grad_state = (
        inverse_rms[:, None] * scaled_grad
        - span_state * cubed[:, None] * jnp.mean(scaled_grad * span_state, axis=1)[:, None]
    )
    grad_state = jnp.where(live_mask[:, None], grad_state, jnp.float32(0.0))
    mixed_grad = lax.dot_general(
        grad_state.astype(jnp.bfloat16), mix_weight, contract, preferred_element_type=jnp.float32
    )
    mixed_grad = mixed_grad.astype(jnp.float32)
    contributions = jnp.concatenate(
        [grad_state + conv_kernel[0] * mixed_grad]
        + [conv_kernel[offset] * mixed_grad for offset in range(1, KCONV)],
        axis=0,
    )
    target_rows = (
        boundaries[None, :] - jnp.arange(KCONV, dtype=jnp.int32)[:, None]
    ).reshape(KCONV * slot_count)
    exact = lax.Precision.HIGHEST
    rim_rows = jnp.arange(-(KCONV - 1), 0, dtype=jnp.int32)
    rim_pick = (rim_rows[:, None] == target_rows[None, :]).astype(jnp.float32)
    before_rows = jnp.dot(rim_pick, contributions, precision=exact)
    after_rim = neighbour(before_rows, -1)
    row_pick = (
        jnp.arange(row_count, dtype=jnp.int32)[:, None] == target_rows[None, :]
    ).astype(jnp.float32)
    local_grad = lax.optimization_barrier(jnp.dot(row_pick, contributions, precision=exact))
    tail = jnp.concatenate(
        [jnp.zeros((row_count - (KCONV - 1), D), jnp.float32), after_rim], axis=0
    )
    grad_bytes = (local_grad + tail).astype(jnp.bfloat16)
    return (attended, grad_bytes)


def solution(mesh):
    return jax.shard_map(
        per_device,
        mesh=mesh,
        in_specs=(
            P(("doc", "seq"), None),
            P(),
            P(),
            P(),
            P(None, "head"),
            P(None, "head"),
            P(None, "head"),
            P(("doc", "seq")),
            P(("doc", "seq")),
            P(("doc", "seq"), "head"),
        ),
        out_specs=(P(("doc", "seq"), "head"), P(("doc", "seq"), None)),
        check_vma=False,
    )
```

```python
import math

import jax
import jax.numpy as jnp
from jax import lax
from jax.experimental import pallas as pl
from jax.experimental.pallas import tpu as pltpu
from jax.sharding import PartitionSpec as P

D = 1024
HD = 128
KCONV = 4
QBLOCK = 256
BLOCKS_PER_STEP = 4


masked_score = -1e30


def passed_along(array, axis, by):
    devices = lax.axis_size(axis)
    pairs = [(i, i + by) for i in range(devices) if 0 <= i + by < devices]
    return lax.ppermute(array, axis, pairs)


def neighbour(rim_rows, offset_by):
    return passed_along(rim_rows, "seq", offset_by)


def ring_neighbour(index, by, ring, stride):
    place = (index // stride) % ring
    return index + ((place + by) % ring - place) * stride


def ring_phase(held, sources, axis, ring, stride):
    devices = lax.axis_size(axis)

    def shifted(array, by):
        pairs = [(i, ring_neighbour(i, by, ring, stride)) for i in range(devices)]
        return lax.ppermute(array, axis, pairs)

    half = held.shape[0] // 2
    from_below = shifted(held, 1)
    from_above = shifted(held, -1)
    parts = [held, from_below, from_above, shifted(from_below[:half], 1), shifted(from_above[half:], -1)]
    origins = [
        sources,
        ring_neighbour(sources, -1, ring, stride),
        ring_neighbour(sources, 1, ring, stride),
        ring_neighbour(sources[:half], -2, ring, stride),
        ring_neighbour(sources[half:], 2, ring, stride),
    ]
    return jnp.concatenate(parts, axis=0), jnp.concatenate(origins)


def gather_blocks(block, axis):
    devices = lax.axis_size(axis)
    me = lax.axis_index(axis)
    held = block[None]
    sources = me[None]
    if devices == 32:
        other = lax.ppermute(held, axis, [(i, i ^ 1) for i in range(devices)])
        held = jnp.concatenate([held, other], axis=0)
        sources = jnp.concatenate([sources, sources ^ 1])
        held, sources = ring_phase(held, sources, axis, 4, 2)
        return ring_phase(held, sources, axis, 4, 8)
    step = 1
    while step < devices:
        other = lax.ppermute(held, axis, [(i, i ^ step) for i in range(devices)])
        held = jnp.concatenate([held, other], axis=0)
        sources = jnp.concatenate([sources, sources ^ step])
        step *= 2
    return held, sources


def summed_over(partial, axis):
    devices = lax.axis_size(axis)
    total = partial
    step = 1
    last = devices // 2 if devices == 8 else devices
    while step < last:
        sent = total.astype(jnp.bfloat16)
        got = lax.ppermute(sent, axis, [(i, i ^ step) for i in range(devices)])
        total = sent.astype(jnp.float32) + got.astype(jnp.float32)
        step *= 2
    if devices == 8:
        nearest = {0: 7, 1: 7, 2: 4, 3: 4, 4: 3, 5: 3, 6: 0, 7: 0}
        sent = total.astype(jnp.bfloat16)
        near = [(src, dst) for dst, src in nearest.items() if min((dst - src) % 8, (src - dst) % 8) == 1]
        far = [(src, dst) for dst, src in nearest.items() if min((dst - src) % 8, (src - dst) % 8) == 2]
        got = lax.ppermute(sent, axis, near).astype(jnp.float32) + lax.ppermute(
            sent, axis, far
        ).astype(jnp.float32)
        total = sent.astype(jnp.float32) + got
    return total


def forward_kernel(
    shards_ref, q_ref, k_ref, v_ref, g_ref, info_ref,
    att_ref, gq_ref, gk_ref, gv_ref,
):
    block_rows = q_ref.shape[1]
    rows = q_ref.shape[0] * block_rows
    width = q_ref.shape[2]
    step = pl.program_id(0)
    first = step * BLOCKS_PER_STEP
    row = lax.broadcasted_iota(jnp.int32, (rows, 1), 0)
    q_ids = row % block_rows
    for t in range(BLOCKS_PER_STEP):
        q_ids = q_ids + jnp.where(row // block_rows == t, shards_ref[first + t] * block_rows, 0)
    scale = 1.0 / math.sqrt(HD)
    by_rows = (((1,), (1,)), ((), ()))
    by_cols = (((0,), (0,)), ((), ()))
    blocks = k_ref.shape[0]
    slots = blocks * block_rows
    info = jnp.max(info_ref[...].astype(jnp.float32), axis=1)
    column = lax.broadcasted_iota(jnp.int32, (blocks, slots), 1)
    pick = (column // block_rows == lax.broadcasted_iota(jnp.int32, (blocks, slots), 0))
    spread = lax.dot_general(info, pick.astype(jnp.float32), by_cols, preferred_element_type=jnp.float32)
    lane = lax.broadcasted_iota(jnp.int32, (1, slots), 1) % block_rows
    counts_row = spread[0:1].astype(jnp.int32)
    sources_row = spread[info.shape[1] // 2 : info.shape[1] // 2 + 1].astype(jnp.int32)
    key_code = jnp.where(lane < counts_row, sources_row * block_rows + lane, slots)
    queries = q_ref[...].reshape(rows, width)
    grads = g_ref[...].reshape(rows, width)
    keys = k_ref[...].reshape(-1, width)
    values = v_ref[...].reshape(-1, width)
    scores = lax.dot_general(queries, keys, by_rows, preferred_element_type=jnp.float32) * scale
    scores = jnp.where(key_code <= q_ids, scores, masked_score)
    row_max = jnp.max(scores, axis=1, keepdims=True)
    softmax_part = jnp.exp(scores - row_max)
    row_sum = jnp.sum(softmax_part, axis=1, keepdims=True)
    product = jnp.dot(
        softmax_part.astype(jnp.bfloat16), values, preferred_element_type=jnp.float32
    )
    attention = (product / row_sum).astype(jnp.bfloat16)
    log_total = row_max + jnp.log(row_sum)
    delta = jnp.sum(grads.astype(jnp.float32) * attention.astype(jnp.float32), axis=1, keepdims=True)

    own = block_rows

    @pl.when(step == 0)
    def _():
        probs = jnp.exp(scores[:own] - log_total[:own])
        grad_probs = lax.dot_general(
            grads[:own], values, by_rows, preferred_element_type=jnp.float32
        )
        grad_scores = (probs * (grad_probs - delta[:own])).astype(jnp.bfloat16)
        gq_ref[...] = jnp.dot(grad_scores, keys, preferred_element_type=jnp.float32)
        att_ref[...] = attention[:own]
        gk_ref[...] = jnp.zeros_like(gk_ref)
        gv_ref[...] = jnp.zeros_like(gv_ref)

    own_scores = lax.dot_general(
        queries, k_ref[0], by_rows, preferred_element_type=jnp.float32
    ) * scale
    own_scores = jnp.where(key_code[:, :own] <= q_ids, own_scores, masked_score)
    probs = jnp.exp(own_scores - log_total)
    gv_ref[...] += lax.dot_general(
        probs.astype(jnp.bfloat16), grads, by_cols, preferred_element_type=jnp.float32
    )
    grad_probs = lax.dot_general(grads, v_ref[0], by_rows, preferred_element_type=jnp.float32)
    grad_scores = (probs * (grad_probs - delta)).astype(jnp.bfloat16)
    gk_ref[...] += lax.dot_general(grad_scores, queries, by_cols, preferred_element_type=jnp.float32)


def attention_all(gathered, held_shards, block_rows, info_rows):
    blocks, _, width = gathered.shape
    step_spec = lambda part: pl.BlockSpec(
        (BLOCKS_PER_STEP, block_rows, width), lambda i, shards: (i, part, 0)
    )
    all_spec = lambda part: pl.BlockSpec(
        (blocks, block_rows, width), lambda i, shards: (0, part, 0)
    )
    own_spec = pl.BlockSpec((block_rows, width), lambda i, shards: (0, 0))
    grid_spec = pltpu.PrefetchScalarGridSpec(
        num_scalar_prefetch=1,
        grid=(blocks // BLOCKS_PER_STEP,),
        in_specs=[step_spec(0), all_spec(1), all_spec(2), step_spec(3),
                  pl.BlockSpec((blocks, info_rows, width),
                               lambda i, shards: (0, 4 * block_rows // info_rows, 0))],
        out_specs=[own_spec, own_spec, own_spec, own_spec],
    )
    own_grad = jax.ShapeDtypeStruct((block_rows, width), jnp.float32)
    return pl.pallas_call(
        forward_kernel,
        grid_spec=grid_spec,
        out_shape=[jax.ShapeDtypeStruct((block_rows, width), jnp.bfloat16), own_grad, own_grad, own_grad],
    )(held_shards, gathered, gathered, gathered, gathered, gathered)


def per_device(
    byte_states,
    conv_kernel,
    mix_weight,
    norm_gain,
    query_weight,
    key_weight,
    value_weight,
    boundaries,
    span_counts,
    grad_attended,
):
    row_count = byte_states.shape[0]
    slot_count = boundaries.shape[0]
    head_width = query_weight.shape[1]
    score_scale = 1.0 / math.sqrt(HD)
    shard_index = lax.axis_index("seq")
    shards = lax.axis_size("seq")
    first_slot = shard_index * slot_count
    own_ids = first_slot + jnp.arange(slot_count, dtype=jnp.int32)
    before_rim = neighbour(byte_states[row_count - (KCONV - 1) :].astype(jnp.float32), 1)
    extended = jnp.concatenate([before_rim.astype(jnp.bfloat16), byte_states], axis=0)
    tap_rows = (boundaries[None, :] + jnp.arange(KCONV - 1, -1, -1, dtype=jnp.int32)[:, None])
    tapped = jnp.take(extended, tap_rows.reshape(-1), axis=0).astype(jnp.float32)
    tapped = tapped.reshape(KCONV, slot_count, D)
    span_depth = conv_kernel[0] * tapped[0]
    for offset in range(1, KCONV):
        span_depth = span_depth + conv_kernel[offset] * tapped[offset]
    span_depth = span_depth.astype(jnp.bfloat16)
    span_bytes = tapped[0]
    live_mask = jnp.arange(slot_count, dtype=jnp.int32) < span_counts[0]
    span_state = span_bytes + jnp.dot(span_depth, mix_weight, preferred_element_type=jnp.float32)
    inverse_rms = lax.rsqrt(jnp.mean(span_state * span_state, axis=1) + 1e-05)
    normed = (span_state * inverse_rms[:, None] * norm_gain).astype(jnp.bfloat16)
    queries = jnp.dot(normed, query_weight, preferred_element_type=jnp.float32).astype(jnp.bfloat16)
    key_rows = jnp.dot(normed, key_weight, preferred_element_type=jnp.float32).astype(jnp.bfloat16)
    value_rows = jnp.dot(normed, value_weight, preferred_element_type=jnp.float32).astype(
        jnp.bfloat16
    )
    grad_rows = jnp.where(live_mask[:, None], grad_attended, jnp.zeros_like(grad_attended))

    info_rows = jnp.concatenate(
        [
            jnp.broadcast_to(span_counts[0].astype(jnp.bfloat16), (16, head_width // 2)),
            jnp.broadcast_to(shard_index.astype(jnp.bfloat16), (16, head_width // 2)),
        ],
        axis=1,
    )
    packed = jnp.concatenate([queries, key_rows, value_rows, grad_rows, info_rows], axis=0)
    gathered, held_shards = gather_blocks(packed, "seq")
    total_slots = shards * slot_count

    own_attended, query_grad, key_grad, value_grad = attention_all(gathered, held_shards, slot_count, 16)
    attended = jnp.where(live_mask[:, None], own_attended, jnp.bfloat16(0.0))
    query_grad_rows = (query_grad * score_scale).astype(jnp.bfloat16)
    key_grad_rows = (key_grad * score_scale).astype(jnp.bfloat16)
    value_grad_rows = value_grad.astype(jnp.bfloat16)

    contract = (((1,), (1,)), ((), ()))
    partial_normed = lax.dot_general(
        jnp.concatenate([query_grad_rows, key_grad_rows, value_grad_rows], axis=1),
        jnp.concatenate([query_weight, key_weight, value_weight], axis=1),
        contract,
        preferred_element_type=jnp.float32,
    )
    grad_normed = summed_over(partial_normed, "head")
    scaled_grad = norm_gain * grad_normed
    cubed = inverse_rms * inverse_rms * inverse_rms
    grad_state = (
        inverse_rms[:, None] * scaled_grad
        - span_state * cubed[:, None] * jnp.mean(scaled_grad * span_state, axis=1)[:, None]
    )
    grad_state = jnp.where(live_mask[:, None], grad_state, jnp.float32(0.0))
    mixed_grad = lax.dot_general(
        grad_state.astype(jnp.bfloat16), mix_weight, contract, preferred_element_type=jnp.float32
    )
    mixed_grad = mixed_grad.astype(jnp.float32)
    contributions = jnp.concatenate(
        [grad_state + conv_kernel[0] * mixed_grad]
        + [conv_kernel[offset] * mixed_grad for offset in range(1, KCONV)],
        axis=0,
    )
    target_rows = (
        boundaries[None, :] - jnp.arange(KCONV, dtype=jnp.int32)[:, None]
    ).reshape(KCONV * slot_count)
    exact = lax.Precision.HIGHEST
    rim_rows = jnp.arange(-(KCONV - 1), 0, dtype=jnp.int32)
    rim_pick = (rim_rows[:, None] == target_rows[None, :]).astype(jnp.float32)
    before_rows = jnp.dot(rim_pick, contributions, precision=exact)
    after_rim = neighbour(before_rows, -1)
    row_pick = (
        jnp.arange(row_count, dtype=jnp.int32)[:, None] == target_rows[None, :]
    ).astype(jnp.float32)
    local_grad = lax.optimization_barrier(jnp.dot(row_pick, contributions, precision=exact))
    tail = jnp.concatenate(
        [jnp.zeros((row_count - (KCONV - 1), D), jnp.float32), after_rim], axis=0
    )
    grad_bytes = (local_grad + tail).astype(jnp.bfloat16)
    return (attended, grad_bytes)


def solution(mesh):
    return jax.shard_map(
        per_device,
        mesh=mesh,
        in_specs=(
            P(("doc", "seq"), None),
            P(),
            P(),
            P(),
            P(None, "head"),
            P(None, "head"),
            P(None, "head"),
            P(("doc", "seq")),
            P(("doc", "seq")),
            P(("doc", "seq"), "head"),
        ),
        out_specs=(P(("doc", "seq"), "head"), P(("doc", "seq"), None)),
        check_vma=False,
    )
```

```python
import math

import jax
import jax.numpy as jnp
from jax import lax
from jax.experimental import pallas as pl
from jax.experimental.pallas import tpu as pltpu
from jax.sharding import PartitionSpec as P

D = 1024
HD = 128
KCONV = 4
QBLOCK = 256
BLOCKS_PER_STEP = 4


masked_score = -1e30


def passed_along(array, axis, by):
    devices = lax.axis_size(axis)
    pairs = [(i, i + by) for i in range(devices) if 0 <= i + by < devices]
    return lax.ppermute(array, axis, pairs)


def neighbour(rim_rows, offset_by):
    return passed_along(rim_rows, "seq", offset_by)


def ring_neighbour(index, by, ring, stride):
    place = (index // stride) % ring
    return index + ((place + by) % ring - place) * stride


def ring_phase(held, sources, axis, ring, stride):
    devices = lax.axis_size(axis)

    def shifted(array, by):
        pairs = [(i, ring_neighbour(i, by, ring, stride)) for i in range(devices)]
        return lax.ppermute(array, axis, pairs)

    half = held.shape[0] // 2
    from_below = shifted(held, 1)
    from_above = shifted(held, -1)
    parts = [held, from_below, from_above, shifted(from_below[:half], 1), shifted(from_above[half:], -1)]
    origins = [
        sources,
        ring_neighbour(sources, -1, ring, stride),
        ring_neighbour(sources, 1, ring, stride),
        ring_neighbour(sources[:half], -2, ring, stride),
        ring_neighbour(sources[half:], 2, ring, stride),
    ]
    return jnp.concatenate(parts, axis=0), jnp.concatenate(origins)


def gather_blocks(block, axis):
    devices = lax.axis_size(axis)
    me = lax.axis_index(axis)
    held = block[None]
    sources = me[None]
    if devices == 32:
        other = lax.ppermute(held, axis, [(i, i ^ 1) for i in range(devices)])
        held = jnp.concatenate([held, other], axis=0)
        sources = jnp.concatenate([sources, sources ^ 1])
        held, sources = ring_phase(held, sources, axis, 4, 2)
        return ring_phase(held, sources, axis, 4, 8)
    step = 1
    while step < devices:
        other = lax.ppermute(held, axis, [(i, i ^ step) for i in range(devices)])
        held = jnp.concatenate([held, other], axis=0)
        sources = jnp.concatenate([sources, sources ^ step])
        step *= 2
    return held, sources


def summed_over(partial, axis):
    devices = lax.axis_size(axis)
    total = partial
    step = 1
    last = devices // 2 if devices == 8 else devices
    while step < last:
        sent = total.astype(jnp.bfloat16)
        got = lax.ppermute(sent, axis, [(i, i ^ step) for i in range(devices)])
        total = sent.astype(jnp.float32) + got.astype(jnp.float32)
        step *= 2
    if devices == 8:
        nearest = {0: 7, 1: 7, 2: 4, 3: 4, 4: 3, 5: 3, 6: 0, 7: 0}
        sent = total.astype(jnp.bfloat16)
        near = [(src, dst) for dst, src in nearest.items() if min((dst - src) % 8, (src - dst) % 8) == 1]
        far = [(src, dst) for dst, src in nearest.items() if min((dst - src) % 8, (src - dst) % 8) == 2]
        got = lax.ppermute(sent, axis, near).astype(jnp.float32) + lax.ppermute(
            sent, axis, far
        ).astype(jnp.float32)
        total = sent.astype(jnp.float32) + got
    return total


def forward_kernel(
    shards_ref, q_ref, k_ref, v_ref, g_ref, key_code_ref, own_code_ref,
    att_ref, grad_ref, gk_ref, gv_ref,
):
    block_rows = q_ref.shape[1]
    rows = q_ref.shape[0] * block_rows
    width = q_ref.shape[2]
    step = pl.program_id(0)
    first = step * BLOCKS_PER_STEP
    row = lax.broadcasted_iota(jnp.int32, (rows, 1), 0)
    q_ids = row % block_rows
    for t in range(BLOCKS_PER_STEP):
        q_ids = q_ids + jnp.where(row // block_rows == t, shards_ref[first + t] * block_rows, 0)
    scale = 1.0 / math.sqrt(HD)
    by_rows = (((1,), (1,)), ((), ()))
    by_cols = (((0,), (0,)), ((), ()))
    queries = q_ref[...].reshape(rows, width)
    grads = g_ref[...].reshape(rows, width)
    keys = k_ref[...].reshape(-1, width)
    values = v_ref[...].reshape(-1, width)
    scores = lax.dot_general(queries, keys, by_rows, preferred_element_type=jnp.float32) * scale
    scores = jnp.where(key_code_ref[...] <= q_ids, scores, masked_score)
    row_max = jnp.max(scores, axis=1, keepdims=True)
    softmax_part = jnp.exp(scores - row_max)
    row_sum = jnp.sum(softmax_part, axis=1, keepdims=True)
    product = jnp.dot(
        softmax_part.astype(jnp.bfloat16), values, preferred_element_type=jnp.float32
    )
    attention = (product / row_sum).astype(jnp.bfloat16)
    log_total = row_max + jnp.log(row_sum)
    delta = jnp.sum(grads.astype(jnp.float32) * attention.astype(jnp.float32), axis=1, keepdims=True)

    own = block_rows

    @pl.when(step == 0)
    def _():
        probs = jnp.exp(scores[:own] - log_total[:own])
        grad_probs = lax.dot_general(
            grads[:own], values, by_rows, preferred_element_type=jnp.float32
        )
        grad_scores = (probs * (grad_probs - delta[:own])).astype(jnp.bfloat16)
        query_grad = jnp.dot(grad_scores, keys, preferred_element_type=jnp.float32) * scale
        grad_ref[:, :width] = query_grad.astype(jnp.bfloat16)
        att_ref[...] = attention[:own]
        gk_ref[...] = jnp.zeros_like(gk_ref)
        gv_ref[...] = jnp.zeros_like(gv_ref)

    own_scores = lax.dot_general(
        queries, k_ref[0], by_rows, preferred_element_type=jnp.float32
    ) * scale
    own_scores = jnp.where(own_code_ref[...] <= q_ids, own_scores, masked_score)
    probs = jnp.exp(own_scores - log_total)
    gv_ref[...] += lax.dot_general(
        probs.astype(jnp.bfloat16), grads, by_cols, preferred_element_type=jnp.float32
    )
    grad_probs = lax.dot_general(grads, v_ref[0], by_rows, preferred_element_type=jnp.float32)
    grad_scores = (probs * (grad_probs - delta)).astype(jnp.bfloat16)
    gk_ref[...] += lax.dot_general(grad_scores, queries, by_cols, preferred_element_type=jnp.float32)

    @pl.when(step == pl.num_programs(0) - 1)
    def _():
        grad_ref[:, width : 2 * width] = (gk_ref[...] * scale).astype(jnp.bfloat16)
        grad_ref[:, 2 * width :] = gv_ref[...].astype(jnp.bfloat16)


def attention_all(gathered, key_code, held_shards):
    blocks, _, width = gathered.shape
    block_rows = key_code.shape[0] // blocks
    slots = blocks * block_rows
    step_spec = lambda part: pl.BlockSpec(
        (BLOCKS_PER_STEP, block_rows, width), lambda i, shards: (i, part, 0)
    )
    all_spec = lambda part: pl.BlockSpec(
        (blocks, block_rows, width), lambda i, shards: (0, part, 0)
    )
    own_spec = pl.BlockSpec((block_rows, width), lambda i, shards: (0, 0))
    grid_spec = pltpu.PrefetchScalarGridSpec(
        num_scalar_prefetch=1,
        grid=(blocks // BLOCKS_PER_STEP,),
        in_specs=[step_spec(0), all_spec(1), all_spec(2), step_spec(3),
                  pl.BlockSpec((1, slots), lambda i, shards: (0, 0)),
                  pl.BlockSpec((1, block_rows), lambda i, shards: (0, 0))],
        out_specs=[own_spec, pl.BlockSpec((block_rows, 3 * width), lambda i, shards: (0, 0))],
        scratch_shapes=[pltpu.VMEM((block_rows, width), jnp.float32)] * 2,
    )
    return pl.pallas_call(
        forward_kernel,
        grid_spec=grid_spec,
        out_shape=[
            jax.ShapeDtypeStruct((block_rows, width), jnp.bfloat16),
            jax.ShapeDtypeStruct((block_rows, 3 * width), jnp.bfloat16),
        ],
    )(held_shards, gathered, gathered, gathered, gathered, key_code.reshape(1, slots),
      key_code[:block_rows].reshape(1, block_rows))


def per_device(
    byte_states,
    conv_kernel,
    mix_weight,
    norm_gain,
    query_weight,
    key_weight,
    value_weight,
    boundaries,
    span_counts,
    grad_attended,
):
    row_count = byte_states.shape[0]
    slot_count = boundaries.shape[0]
    head_width = query_weight.shape[1]
    score_scale = 1.0 / math.sqrt(HD)
    shard_index = lax.axis_index("seq")
    shards = lax.axis_size("seq")
    first_slot = shard_index * slot_count
    own_ids = first_slot + jnp.arange(slot_count, dtype=jnp.int32)
    before_rim = neighbour(byte_states[row_count - (KCONV - 1) :].astype(jnp.float32), 1)
    extended = jnp.concatenate([before_rim.astype(jnp.bfloat16), byte_states], axis=0)
    tap_rows = (boundaries[None, :] + jnp.arange(KCONV - 1, -1, -1, dtype=jnp.int32)[:, None])
    tapped = jnp.take(extended, tap_rows.reshape(-1), axis=0).astype(jnp.float32)
    tapped = tapped.reshape(KCONV, slot_count, D)
    span_depth = conv_kernel[0] * tapped[0]
    for offset in range(1, KCONV):
        span_depth = span_depth + conv_kernel[offset] * tapped[offset]
    span_depth = span_depth.astype(jnp.bfloat16)
    span_bytes = tapped[0]
    live_mask = jnp.arange(slot_count, dtype=jnp.int32) < span_counts[0]
    span_state = span_bytes + jnp.dot(span_depth, mix_weight, preferred_element_type=jnp.float32)
    inverse_rms = lax.rsqrt(jnp.mean(span_state * span_state, axis=1) + 1e-05)
    normed = (span_state * inverse_rms[:, None] * norm_gain).astype(jnp.bfloat16)
    queries = jnp.dot(normed, query_weight, preferred_element_type=jnp.float32).astype(jnp.bfloat16)
    key_rows = jnp.dot(normed, key_weight, preferred_element_type=jnp.float32).astype(jnp.bfloat16)
    value_rows = jnp.dot(normed, value_weight, preferred_element_type=jnp.float32).astype(
        jnp.bfloat16
    )
    grad_rows = jnp.where(live_mask[:, None], grad_attended, jnp.zeros_like(grad_attended))

    count_rows = jnp.broadcast_to(span_counts[0].astype(jnp.bfloat16), (16, head_width))
    packed = jnp.concatenate([queries, key_rows, value_rows, grad_rows, count_rows], axis=0)
    gathered, held_shards = gather_blocks(packed, "seq")
    total_slots = shards * slot_count

    all_counts = gathered[:, 4 * slot_count, 0].astype(jnp.int32)
    all_live = (
        jnp.arange(slot_count, dtype=jnp.int32)[None, :] < all_counts[:, None]
    ).reshape(total_slots)
    slot_ids = (
        held_shards[:, None] * slot_count + jnp.arange(slot_count, dtype=jnp.int32)[None, :]
    ).reshape(total_slots)

    own_attended, own_grads = attention_all(
        gathered, jnp.where(all_live, slot_ids, total_slots), held_shards
    )
    attended = jnp.where(live_mask[:, None], own_attended, jnp.bfloat16(0.0))

    contract = (((1,), (1,)), ((), ()))
    partial_normed = lax.dot_general(
        own_grads,
        jnp.concatenate([query_weight, key_weight, value_weight], axis=1),
        contract,
        preferred_element_type=jnp.float32,
    )
    grad_normed = summed_over(partial_normed, "head")
    scaled_grad = norm_gain * grad_normed
    cubed = inverse_rms * inverse_rms * inverse_rms
    grad_state = (
        inverse_rms[:, None] * scaled_grad
        - span_state * cubed[:, None] * jnp.mean(scaled_grad * span_state, axis=1)[:, None]
    )
    grad_state = jnp.where(live_mask[:, None], grad_state, jnp.float32(0.0))
    mixed_grad = lax.dot_general(
        grad_state.astype(jnp.bfloat16), mix_weight, contract, preferred_element_type=jnp.float32
    )
    mixed_grad = mixed_grad.astype(jnp.float32)
    contributions = jnp.concatenate(
        [grad_state + conv_kernel[0] * mixed_grad]
        + [conv_kernel[offset] * mixed_grad for offset in range(1, KCONV)],
        axis=0,
    )
    target_rows = (
        boundaries[None, :] - jnp.arange(KCONV, dtype=jnp.int32)[:, None]
    ).reshape(KCONV * slot_count)
    exact = lax.Precision.HIGHEST
    rim_rows = jnp.arange(-(KCONV - 1), 0, dtype=jnp.int32)
    rim_pick = (rim_rows[:, None] == target_rows[None, :]).astype(jnp.float32)
    before_rows = jnp.dot(rim_pick, contributions, precision=exact)
    after_rim = neighbour(before_rows, -1)
    row_pick = (
        jnp.arange(row_count, dtype=jnp.int32)[:, None] == target_rows[None, :]
    ).astype(jnp.float32)
    local_grad = lax.optimization_barrier(jnp.dot(row_pick, contributions, precision=exact))
    tail = jnp.concatenate(
        [jnp.zeros((row_count - (KCONV - 1), D), jnp.float32), after_rim], axis=0
    )
    grad_bytes = (local_grad + tail).astype(jnp.bfloat16)
    return (attended, grad_bytes)


def solution(mesh):
    return jax.shard_map(
        per_device,
        mesh=mesh,
        in_specs=(
            P(("doc", "seq"), None),
            P(),
            P(),
            P(),
            P(None, "head"),
            P(None, "head"),
            P(None, "head"),
            P(("doc", "seq")),
            P(("doc", "seq")),
            P(("doc", "seq"), "head"),
        ),
        out_specs=(P(("doc", "seq"), "head"), P(("doc", "seq"), None)),
        check_vma=False,
    )
```

```python
import math

import jax
import jax.numpy as jnp
from jax import lax
from jax.experimental import pallas as pl
from jax.experimental.pallas import tpu as pltpu
from jax.sharding import PartitionSpec as P

D = 1024
HD = 128
KCONV = 4
QBLOCK = 256
BLOCKS_PER_STEP = 4


masked_score = -1e30


def passed_along(array, axis, by):
    devices = lax.axis_size(axis)
    pairs = [(i, i + by) for i in range(devices) if 0 <= i + by < devices]
    return lax.ppermute(array, axis, pairs)


def neighbour(rim_rows, offset_by):
    return passed_along(rim_rows, "seq", offset_by)


def ring_neighbour(index, by, ring, stride):
    place = (index // stride) % ring
    return index + ((place + by) % ring - place) * stride


def ring_phase(held, sources, axis, ring, stride):
    devices = lax.axis_size(axis)

    def shifted(array, by):
        pairs = [(i, ring_neighbour(i, by, ring, stride)) for i in range(devices)]
        return lax.ppermute(array, axis, pairs)

    half = held.shape[0] // 2
    from_below = shifted(held, 1)
    from_above = shifted(held, -1)
    parts = [held, from_below, from_above, shifted(from_below[:half], 1), shifted(from_above[half:], -1)]
    origins = [
        sources,
        ring_neighbour(sources, -1, ring, stride),
        ring_neighbour(sources, 1, ring, stride),
        ring_neighbour(sources[:half], -2, ring, stride),
        ring_neighbour(sources[half:], 2, ring, stride),
    ]
    return jnp.concatenate(parts, axis=0), jnp.concatenate(origins)


def gather_blocks(block, axis):
    devices = lax.axis_size(axis)
    me = lax.axis_index(axis)
    held = block[None]
    sources = me[None]
    if devices == 32:
        other = lax.ppermute(held, axis, [(i, i ^ 1) for i in range(devices)])
        held = jnp.concatenate([held, other], axis=0)
        sources = jnp.concatenate([sources, sources ^ 1])
        held, sources = ring_phase(held, sources, axis, 4, 2)
        return ring_phase(held, sources, axis, 4, 8)
    step = 1
    while step < devices:
        other = lax.ppermute(held, axis, [(i, i ^ step) for i in range(devices)])
        held = jnp.concatenate([held, other], axis=0)
        sources = jnp.concatenate([sources, sources ^ step])
        step *= 2
    return held, sources


def summed_over(partial, axis):
    devices = lax.axis_size(axis)
    total = partial
    step = 1
    last = devices // 2 if devices == 8 else devices
    while step < last:
        sent = total.astype(jnp.bfloat16)
        got = lax.ppermute(sent, axis, [(i, i ^ step) for i in range(devices)])
        total = sent.astype(jnp.float32) + got.astype(jnp.float32)
        step *= 2
    if devices == 8:
        nearest = {0: 7, 1: 7, 2: 4, 3: 4, 4: 3, 5: 3, 6: 0, 7: 0}
        sent = total.astype(jnp.bfloat16)
        near = [(src, dst) for dst, src in nearest.items() if min((dst - src) % 8, (src - dst) % 8) == 1]
        far = [(src, dst) for dst, src in nearest.items() if min((dst - src) % 8, (src - dst) % 8) == 2]
        got = lax.ppermute(sent, axis, near).astype(jnp.float32) + lax.ppermute(
            sent, axis, far
        ).astype(jnp.float32)
        total = sent.astype(jnp.float32) + got
    return total


def forward_kernel(
    shards_ref, q_ref, k_ref, v_ref, g_ref, key_code_ref, own_code_ref, w_ref,
    att_ref, partial_ref, grad_ref, gk_ref, gv_ref,
):
    block_rows = q_ref.shape[1]
    rows = q_ref.shape[0] * block_rows
    width = q_ref.shape[2]
    step = pl.program_id(0)
    first = step * BLOCKS_PER_STEP
    row = lax.broadcasted_iota(jnp.int32, (rows, 1), 0)
    q_ids = row % block_rows
    for t in range(BLOCKS_PER_STEP):
        q_ids = q_ids + jnp.where(row // block_rows == t, shards_ref[first + t] * block_rows, 0)
    scale = 1.0 / math.sqrt(HD)
    by_rows = (((1,), (1,)), ((), ()))
    by_cols = (((0,), (0,)), ((), ()))
    queries = q_ref[...].reshape(rows, width)
    grads = g_ref[...].reshape(rows, width)
    keys = k_ref[...].reshape(-1, width)
    values = v_ref[...].reshape(-1, width)
    scores = lax.dot_general(queries, keys, by_rows, preferred_element_type=jnp.float32) * scale
    scores = jnp.where(key_code_ref[...] <= q_ids, scores, masked_score)
    row_max = jnp.max(scores, axis=1, keepdims=True)
    softmax_part = jnp.exp(scores - row_max)
    row_sum = jnp.sum(softmax_part, axis=1, keepdims=True)
    product = jnp.dot(
        softmax_part.astype(jnp.bfloat16), values, preferred_element_type=jnp.float32
    )
    attention = (product / row_sum).astype(jnp.bfloat16)
    log_total = row_max + jnp.log(row_sum)
    delta = jnp.sum(grads.astype(jnp.float32) * attention.astype(jnp.float32), axis=1, keepdims=True)

    own = block_rows

    @pl.when(step == 0)
    def _():
        probs = jnp.exp(scores[:own] - log_total[:own])
        grad_probs = lax.dot_general(
            grads[:own], values, by_rows, preferred_element_type=jnp.float32
        )
        grad_scores = (probs * (grad_probs - delta[:own])).astype(jnp.bfloat16)
        query_grad = jnp.dot(grad_scores, keys, preferred_element_type=jnp.float32) * scale
        grad_ref[:, :width] = query_grad.astype(jnp.bfloat16)
        att_ref[...] = attention[:own]
        gk_ref[...] = jnp.zeros_like(gk_ref)
        gv_ref[...] = jnp.zeros_like(gv_ref)

    own_scores = lax.dot_general(
        queries, k_ref[0], by_rows, preferred_element_type=jnp.float32
    ) * scale
    own_scores = jnp.where(own_code_ref[...] <= q_ids, own_scores, masked_score)
    probs = jnp.exp(own_scores - log_total)
    gv_ref[...] += lax.dot_general(
        probs.astype(jnp.bfloat16), grads, by_cols, preferred_element_type=jnp.float32
    )
    grad_probs = lax.dot_general(grads, v_ref[0], by_rows, preferred_element_type=jnp.float32)
    grad_scores = (probs * (grad_probs - delta)).astype(jnp.bfloat16)
    gk_ref[...] += lax.dot_general(grad_scores, queries, by_cols, preferred_element_type=jnp.float32)

    @pl.when(step == pl.num_programs(0) - 1)
    def _():
        grad_ref[:, width : 2 * width] = (gk_ref[...] * scale).astype(jnp.bfloat16)
        grad_ref[:, 2 * width :] = gv_ref[...].astype(jnp.bfloat16)
        partial_ref[...] = lax.dot_general(
            grad_ref[...], w_ref[...], by_rows, preferred_element_type=jnp.float32
        ).astype(jnp.bfloat16)


def attention_all(gathered, key_code, held_shards, weights):
    blocks, _, width = gathered.shape
    block_rows = key_code.shape[0] // blocks
    slots = blocks * block_rows
    step_spec = lambda part: pl.BlockSpec(
        (BLOCKS_PER_STEP, block_rows, width), lambda i, shards: (i, part, 0)
    )
    all_spec = lambda part: pl.BlockSpec(
        (blocks, block_rows, width), lambda i, shards: (0, part, 0)
    )
    own_spec = pl.BlockSpec((block_rows, width), lambda i, shards: (0, 0))
    grid_spec = pltpu.PrefetchScalarGridSpec(
        num_scalar_prefetch=1,
        grid=(blocks // BLOCKS_PER_STEP,),
        in_specs=[step_spec(0), all_spec(1), all_spec(2), step_spec(3),
                  pl.BlockSpec((1, slots), lambda i, shards: (0, 0)),
                  pl.BlockSpec((1, block_rows), lambda i, shards: (0, 0)),
                  pl.BlockSpec(weights.shape, lambda i, shards: (0, 0))],
        out_specs=[own_spec, pl.BlockSpec((block_rows, weights.shape[0]), lambda i, shards: (0, 0))],
        scratch_shapes=[pltpu.VMEM((block_rows, 3 * width), jnp.bfloat16)]
        + [pltpu.VMEM((block_rows, width), jnp.float32)] * 2,
    )
    return pl.pallas_call(
        forward_kernel,
        grid_spec=grid_spec,
        out_shape=[
            jax.ShapeDtypeStruct((block_rows, width), jnp.bfloat16),
            jax.ShapeDtypeStruct((block_rows, weights.shape[0]), jnp.bfloat16),
        ],
    )(held_shards, gathered, gathered, gathered, gathered, key_code.reshape(1, slots),
      key_code[:block_rows].reshape(1, block_rows), weights)


def per_device(
    byte_states,
    conv_kernel,
    mix_weight,
    norm_gain,
    query_weight,
    key_weight,
    value_weight,
    boundaries,
    span_counts,
    grad_attended,
):
    row_count = byte_states.shape[0]
    slot_count = boundaries.shape[0]
    head_width = query_weight.shape[1]
    score_scale = 1.0 / math.sqrt(HD)
    shard_index = lax.axis_index("seq")
    shards = lax.axis_size("seq")
    first_slot = shard_index * slot_count
    own_ids = first_slot + jnp.arange(slot_count, dtype=jnp.int32)
    before_rim = neighbour(byte_states[row_count - (KCONV - 1) :].astype(jnp.float32), 1)
    extended = jnp.concatenate([before_rim.astype(jnp.bfloat16), byte_states], axis=0)
    tap_rows = (boundaries[None, :] + jnp.arange(KCONV - 1, -1, -1, dtype=jnp.int32)[:, None])
    tapped = jnp.take(extended, tap_rows.reshape(-1), axis=0).astype(jnp.float32)
    tapped = tapped.reshape(KCONV, slot_count, D)
    span_depth = conv_kernel[0] * tapped[0]
    for offset in range(1, KCONV):
        span_depth = span_depth + conv_kernel[offset] * tapped[offset]
    span_depth = span_depth.astype(jnp.bfloat16)
    span_bytes = tapped[0]
    live_mask = jnp.arange(slot_count, dtype=jnp.int32) < span_counts[0]
    span_state = span_bytes + jnp.dot(span_depth, mix_weight, preferred_element_type=jnp.float32)
    inverse_rms = lax.rsqrt(jnp.mean(span_state * span_state, axis=1) + 1e-05)
    normed = (span_state * inverse_rms[:, None] * norm_gain).astype(jnp.bfloat16)
    queries = jnp.dot(normed, query_weight, preferred_element_type=jnp.float32).astype(jnp.bfloat16)
    key_rows = jnp.dot(normed, key_weight, preferred_element_type=jnp.float32).astype(jnp.bfloat16)
    value_rows = jnp.dot(normed, value_weight, preferred_element_type=jnp.float32).astype(
        jnp.bfloat16
    )
    grad_rows = jnp.where(live_mask[:, None], grad_attended, jnp.zeros_like(grad_attended))

    count_rows = jnp.broadcast_to(span_counts[0].astype(jnp.bfloat16), (16, head_width))
    packed = jnp.concatenate([queries, key_rows, value_rows, grad_rows, count_rows], axis=0)
    gathered, held_shards = gather_blocks(packed, "seq")
    total_slots = shards * slot_count

    all_counts = gathered[:, 4 * slot_count, 0].astype(jnp.int32)
    all_live = (
        jnp.arange(slot_count, dtype=jnp.int32)[None, :] < all_counts[:, None]
    ).reshape(total_slots)
    slot_ids = (
        held_shards[:, None] * slot_count + jnp.arange(slot_count, dtype=jnp.int32)[None, :]
    ).reshape(total_slots)

    own_attended, partial_normed = attention_all(
        gathered, jnp.where(all_live, slot_ids, total_slots), held_shards,
        jnp.concatenate([query_weight, key_weight, value_weight], axis=1),
    )
    attended = jnp.where(live_mask[:, None], own_attended, jnp.bfloat16(0.0))

    contract = (((1,), (1,)), ((), ()))
    grad_normed = summed_over(partial_normed, "head")
    scaled_grad = norm_gain * grad_normed
    cubed = inverse_rms * inverse_rms * inverse_rms
    grad_state = (
        inverse_rms[:, None] * scaled_grad
        - span_state * cubed[:, None] * jnp.mean(scaled_grad * span_state, axis=1)[:, None]
    )
    grad_state = jnp.where(live_mask[:, None], grad_state, jnp.float32(0.0))
    mixed_grad = lax.dot_general(
        grad_state.astype(jnp.bfloat16), mix_weight, contract, preferred_element_type=jnp.float32
    )
    mixed_grad = mixed_grad.astype(jnp.float32)
    contributions = jnp.concatenate(
        [grad_state + conv_kernel[0] * mixed_grad]
        + [conv_kernel[offset] * mixed_grad for offset in range(1, KCONV)],
        axis=0,
    )
    target_rows = (
        boundaries[None, :] - jnp.arange(KCONV, dtype=jnp.int32)[:, None]
    ).reshape(KCONV * slot_count)
    exact = lax.Precision.HIGHEST
    rim_rows = jnp.arange(-(KCONV - 1), 0, dtype=jnp.int32)
    rim_pick = (rim_rows[:, None] == target_rows[None, :]).astype(jnp.float32)
    before_rows = jnp.dot(rim_pick, contributions, precision=exact)
    after_rim = neighbour(before_rows, -1)
    row_pick = (
        jnp.arange(row_count, dtype=jnp.int32)[:, None] == target_rows[None, :]
    ).astype(jnp.float32)
    local_grad = lax.optimization_barrier(jnp.dot(row_pick, contributions, precision=exact))
    tail = jnp.concatenate(
        [jnp.zeros((row_count - (KCONV - 1), D), jnp.float32), after_rim], axis=0
    )
    grad_bytes = (local_grad + tail).astype(jnp.bfloat16)
    return (attended, grad_bytes)


def solution(mesh):
    return jax.shard_map(
        per_device,
        mesh=mesh,
        in_specs=(
            P(("doc", "seq"), None),
            P(),
            P(),
            P(),
            P(None, "head"),
            P(None, "head"),
            P(None, "head"),
            P(("doc", "seq")),
            P(("doc", "seq")),
            P(("doc", "seq"), "head"),
        ),
        out_specs=(P(("doc", "seq"), "head"), P(("doc", "seq"), None)),
        check_vma=False,
    )
```

```python
import math

import jax
import jax.numpy as jnp
from jax import lax
from jax.experimental import pallas as pl
from jax.experimental.pallas import tpu as pltpu
from jax.sharding import PartitionSpec as P

D = 1024
HD = 128
KCONV = 4
QBLOCK = 128
BLOCKS_PER_STEP = 2


masked_score = -1e30


def passed_along(array, axis, by):
    devices = lax.axis_size(axis)
    pairs = [(i, i + by) for i in range(devices) if 0 <= i + by < devices]
    return lax.ppermute(array, axis, pairs)


def neighbour(rim_rows, offset_by):
    return passed_along(rim_rows, "seq", offset_by)


def ring_neighbour(index, by, ring, stride):
    place = (index // stride) % ring
    return index + ((place + by) % ring - place) * stride


def ring_phase(held, sources, axis, ring, stride):
    devices = lax.axis_size(axis)

    def shifted(array, by):
        pairs = [(i, ring_neighbour(i, by, ring, stride)) for i in range(devices)]
        return lax.ppermute(array, axis, pairs)

    half = held.shape[0] // 2
    from_below = shifted(held, 1)
    from_above = shifted(held, -1)
    parts = [held, from_below, from_above, shifted(from_below[:half], 1), shifted(from_above[half:], -1)]
    origins = [
        sources,
        ring_neighbour(sources, -1, ring, stride),
        ring_neighbour(sources, 1, ring, stride),
        ring_neighbour(sources[:half], -2, ring, stride),
        ring_neighbour(sources[half:], 2, ring, stride),
    ]
    return jnp.concatenate(parts, axis=0), jnp.concatenate(origins)


def gather_blocks(block, axis):
    devices = lax.axis_size(axis)
    me = lax.axis_index(axis)
    held = block[None]
    sources = me[None]
    if devices == 32:
        other = lax.ppermute(held, axis, [(i, i ^ 1) for i in range(devices)])
        held = jnp.concatenate([held, other], axis=0)
        sources = jnp.concatenate([sources, sources ^ 1])
        held, sources = ring_phase(held, sources, axis, 4, 2)
        return ring_phase(held, sources, axis, 4, 8)
    step = 1
    while step < devices:
        other = lax.ppermute(held, axis, [(i, i ^ step) for i in range(devices)])
        held = jnp.concatenate([held, other], axis=0)
        sources = jnp.concatenate([sources, sources ^ step])
        step *= 2
    return held, sources


def summed_over(partial, axis):
    devices = lax.axis_size(axis)
    total = partial
    step = 1
    last = devices // 2 if devices == 8 else devices
    while step < last:
        sent = total.astype(jnp.bfloat16)
        got = lax.ppermute(sent, axis, [(i, i ^ step) for i in range(devices)])
        total = sent.astype(jnp.float32) + got.astype(jnp.float32)
        step *= 2
    if devices == 8:
        nearest = {0: 7, 1: 7, 2: 4, 3: 4, 4: 3, 5: 3, 6: 0, 7: 0}
        sent = total.astype(jnp.bfloat16)
        near = [(src, dst) for dst, src in nearest.items() if min((dst - src) % 8, (src - dst) % 8) == 1]
        far = [(src, dst) for dst, src in nearest.items() if min((dst - src) % 8, (src - dst) % 8) == 2]
        got = lax.ppermute(sent, axis, near).astype(jnp.float32) + lax.ppermute(
            sent, axis, far
        ).astype(jnp.float32)
        total = sent.astype(jnp.float32) + got
    return total


def forward_kernel(
    shards_ref, q_ref, k_ref, v_ref, g_ref, key_code_ref, own_code_ref,
    att_ref, grad_ref, gk_ref, gv_ref,
):
    block_rows = q_ref.shape[1]
    rows = q_ref.shape[0] * block_rows
    width = q_ref.shape[2]
    step = pl.program_id(0)
    first = step * BLOCKS_PER_STEP
    row = lax.broadcasted_iota(jnp.int32, (rows, 1), 0)
    q_ids = row % block_rows
    for t in range(BLOCKS_PER_STEP):
        q_ids = q_ids + jnp.where(row // block_rows == t, shards_ref[first + t] * block_rows, 0)
    scale = 1.0 / math.sqrt(HD)
    by_rows = (((1,), (1,)), ((), ()))
    by_cols = (((0,), (0,)), ((), ()))
    queries = q_ref[...].reshape(rows, width)
    grads = g_ref[...].reshape(rows, width)
    keys = k_ref[...].reshape(-1, width)
    values = v_ref[...].reshape(-1, width)
    scores = lax.dot_general(queries, keys, by_rows, preferred_element_type=jnp.float32) * scale
    scores = jnp.where(key_code_ref[...] <= q_ids, scores, masked_score)
    row_max = jnp.max(scores, axis=1, keepdims=True)
    softmax_part = jnp.exp(scores - row_max)
    row_sum = jnp.sum(softmax_part, axis=1, keepdims=True)
    product = jnp.dot(
        softmax_part.astype(jnp.bfloat16), values, preferred_element_type=jnp.float32
    )
    attention = (product / row_sum).astype(jnp.bfloat16)
    log_total = row_max + jnp.log(row_sum)
    delta = jnp.sum(grads.astype(jnp.float32) * attention.astype(jnp.float32), axis=1, keepdims=True)

    own = block_rows

    @pl.when(step == 0)
    def _():
        probs = jnp.exp(scores[:own] - log_total[:own])
        grad_probs = lax.dot_general(
            grads[:own], values, by_rows, preferred_element_type=jnp.float32
        )
        grad_scores = (probs * (grad_probs - delta[:own])).astype(jnp.bfloat16)
        query_grad = jnp.dot(grad_scores, keys, preferred_element_type=jnp.float32) * scale
        grad_ref[:, :width] = query_grad.astype(jnp.bfloat16)
        att_ref[...] = attention[:own]
        gk_ref[...] = jnp.zeros_like(gk_ref)
        gv_ref[...] = jnp.zeros_like(gv_ref)

    own_scores = lax.dot_general(
        queries, k_ref[0], by_rows, preferred_element_type=jnp.float32
    ) * scale
    own_scores = jnp.where(own_code_ref[...] <= q_ids, own_scores, masked_score)
    probs = jnp.exp(own_scores - log_total)
    gv_ref[...] += lax.dot_general(
        probs.astype(jnp.bfloat16), grads, by_cols, preferred_element_type=jnp.float32
    )
    grad_probs = lax.dot_general(grads, v_ref[0], by_rows, preferred_element_type=jnp.float32)
    grad_scores = (probs * (grad_probs - delta)).astype(jnp.bfloat16)
    gk_ref[...] += lax.dot_general(grad_scores, queries, by_cols, preferred_element_type=jnp.float32)

    @pl.when(step == pl.num_programs(0) - 1)
    def _():
        grad_ref[:, width : 2 * width] = (gk_ref[...] * scale).astype(jnp.bfloat16)
        grad_ref[:, 2 * width :] = gv_ref[...].astype(jnp.bfloat16)


def attention_all(gathered, key_code, held_shards):
    blocks, _, width = gathered.shape
    block_rows = key_code.shape[0] // blocks
    slots = blocks * block_rows
    step_spec = lambda part: pl.BlockSpec(
        (BLOCKS_PER_STEP, block_rows, width), lambda i, shards: (i, part, 0)
    )
    all_spec = lambda part: pl.BlockSpec(
        (blocks, block_rows, width), lambda i, shards: (0, part, 0)
    )
    own_spec = pl.BlockSpec((block_rows, width), lambda i, shards: (0, 0))
    grid_spec = pltpu.PrefetchScalarGridSpec(
        num_scalar_prefetch=1,
        grid=(blocks // BLOCKS_PER_STEP,),
        in_specs=[step_spec(0), all_spec(1), all_spec(2), step_spec(3),
                  pl.BlockSpec((1, slots), lambda i, shards: (0, 0)),
                  pl.BlockSpec((1, block_rows), lambda i, shards: (0, 0))],
        out_specs=[own_spec, pl.BlockSpec((block_rows, 3 * width), lambda i, shards: (0, 0))],
        scratch_shapes=[pltpu.VMEM((block_rows, width), jnp.float32)] * 2,
    )
    return pl.pallas_call(
        forward_kernel,
        grid_spec=grid_spec,
        out_shape=[
            jax.ShapeDtypeStruct((block_rows, width), jnp.bfloat16),
            jax.ShapeDtypeStruct((block_rows, 3 * width), jnp.bfloat16),
        ],
    )(held_shards, gathered, gathered, gathered, gathered, key_code.reshape(1, slots),
      key_code[:block_rows].reshape(1, block_rows))


def per_device(
    byte_states,
    conv_kernel,
    mix_weight,
    norm_gain,
    query_weight,
    key_weight,
    value_weight,
    boundaries,
    span_counts,
    grad_attended,
):
    row_count = byte_states.shape[0]
    slot_count = boundaries.shape[0]
    head_width = query_weight.shape[1]
    score_scale = 1.0 / math.sqrt(HD)
    shard_index = lax.axis_index("seq")
    shards = lax.axis_size("seq")
    first_slot = shard_index * slot_count
    own_ids = first_slot + jnp.arange(slot_count, dtype=jnp.int32)
    before_rim = neighbour(byte_states[row_count - (KCONV - 1) :].astype(jnp.float32), 1)
    extended = jnp.concatenate([before_rim.astype(jnp.bfloat16), byte_states], axis=0)
    tap_rows = (boundaries[None, :] + jnp.arange(KCONV - 1, -1, -1, dtype=jnp.int32)[:, None])
    tapped = jnp.take(extended, tap_rows.reshape(-1), axis=0).astype(jnp.float32)
    tapped = tapped.reshape(KCONV, slot_count, D)
    span_depth = conv_kernel[0] * tapped[0]
    for offset in range(1, KCONV):
        span_depth = span_depth + conv_kernel[offset] * tapped[offset]
    span_depth = span_depth.astype(jnp.bfloat16)
    span_bytes = tapped[0]
    live_mask = jnp.arange(slot_count, dtype=jnp.int32) < span_counts[0]
    span_state = span_bytes + jnp.dot(span_depth, mix_weight, preferred_element_type=jnp.float32)
    inverse_rms = lax.rsqrt(jnp.mean(span_state * span_state, axis=1) + 1e-05)
    normed = (span_state * inverse_rms[:, None] * norm_gain).astype(jnp.bfloat16)
    queries = jnp.dot(normed, query_weight, preferred_element_type=jnp.float32).astype(jnp.bfloat16)
    key_rows = jnp.dot(normed, key_weight, preferred_element_type=jnp.float32).astype(jnp.bfloat16)
    value_rows = jnp.dot(normed, value_weight, preferred_element_type=jnp.float32).astype(
        jnp.bfloat16
    )
    grad_rows = jnp.where(live_mask[:, None], grad_attended, jnp.zeros_like(grad_attended))

    count_rows = jnp.broadcast_to(span_counts[0].astype(jnp.bfloat16), (16, head_width))
    packed = jnp.concatenate([queries, key_rows, value_rows, grad_rows, count_rows], axis=0)
    gathered, held_shards = gather_blocks(packed, "seq")
    total_slots = shards * slot_count

    all_counts = gathered[:, 4 * slot_count, 0].astype(jnp.int32)
    all_live = (
        jnp.arange(slot_count, dtype=jnp.int32)[None, :] < all_counts[:, None]
    ).reshape(total_slots)
    slot_ids = (
        held_shards[:, None] * slot_count + jnp.arange(slot_count, dtype=jnp.int32)[None, :]
    ).reshape(total_slots)

    own_attended, own_grads = attention_all(
        gathered, jnp.where(all_live, slot_ids, total_slots), held_shards
    )
    attended = jnp.where(live_mask[:, None], own_attended, jnp.bfloat16(0.0))

    contract = (((1,), (1,)), ((), ()))
    partial_normed = lax.dot_general(
        own_grads,
        jnp.concatenate([query_weight, key_weight, value_weight], axis=1),
        contract,
        preferred_element_type=jnp.float32,
    )
    grad_normed = summed_over(partial_normed, "head")
    scaled_grad = norm_gain * grad_normed
    cubed = inverse_rms * inverse_rms * inverse_rms
    grad_state = (
        inverse_rms[:, None] * scaled_grad
        - span_state * cubed[:, None] * jnp.mean(scaled_grad * span_state, axis=1)[:, None]
    )
    grad_state = jnp.where(live_mask[:, None], grad_state, jnp.float32(0.0))
    mixed_grad = lax.dot_general(
        grad_state.astype(jnp.bfloat16), mix_weight, contract, preferred_element_type=jnp.float32
    )
    mixed_grad = mixed_grad.astype(jnp.float32)
    contributions = jnp.concatenate(
        [grad_state + conv_kernel[0] * mixed_grad]
        + [conv_kernel[offset] * mixed_grad for offset in range(1, KCONV)],
        axis=0,
    )
    target_rows = (
        boundaries[None, :] - jnp.arange(KCONV, dtype=jnp.int32)[:, None]
    ).reshape(KCONV * slot_count)
    exact = lax.Precision.HIGHEST
    rim_rows = jnp.arange(-(KCONV - 1), 0, dtype=jnp.int32)
    rim_pick = (rim_rows[:, None] == target_rows[None, :]).astype(jnp.float32)
    before_rows = jnp.dot(rim_pick, contributions, precision=exact)
    after_rim = neighbour(before_rows, -1)
    row_pick = (
        jnp.arange(row_count, dtype=jnp.int32)[:, None] == target_rows[None, :]
    ).astype(jnp.float32)
    local_grad = lax.optimization_barrier(jnp.dot(row_pick, contributions, precision=exact))
    tail = jnp.concatenate(
        [jnp.zeros((row_count - (KCONV - 1), D), jnp.float32), after_rim], axis=0
    )
    grad_bytes = (local_grad + tail).astype(jnp.bfloat16)
    return (attended, grad_bytes)


def solution(mesh):
    return jax.shard_map(
        per_device,
        mesh=mesh,
        in_specs=(
            P(("doc", "seq"), None),
            P(),
            P(),
            P(),
            P(None, "head"),
            P(None, "head"),
            P(None, "head"),
            P(("doc", "seq")),
            P(("doc", "seq")),
            P(("doc", "seq"), "head"),
        ),
        out_specs=(P(("doc", "seq"), "head"), P(("doc", "seq"), None)),
        check_vma=False,
    )
```
